32 devices in a mesh: len: 16 (over z, y, x), band: 2 (over core).
Axes of the slice: x: 2, y: 2, z: 4, core: 2. Of those that a mesh axis runs over, the one named last changes fastest.
Arguments:
- populations: float32 [19, 128, 32, 128], P(None, 'len', 'band'), as said below
- solid_mask: int32 [128, 32, 128], P('len', 'band'), may hold values from 0 to 1, as said below
- smoke_field: float32 [128, 32, 128], P('len', 'band'), may hold values from 0 to 1
- fan_hubs: int32 [8, 3], replicated, may hold values from 0 to 127, as said below
- fan_gain: float32 [8], replicated, may hold values from 0.15 to 0.5
- jet_speed: float32 [8], replicated, may hold values from 0.05 to 0.12
- sources: int32 [16, 3], replicated, may hold values from 0 to 127, as said below
- source_rate: float32 [16], replicated, may hold values from 0.2 to 1
Outputs:
- populations_out: float32 [19, 128, 32, 128], P(None, 'len', 'band')
- smoke_out: float32 [128, 32, 128], P('len', 'band')
The draws below stay inside these ranges and needn't reach their ends.
Inputs may be any that keep to these rules, and one draw needn't show every extreme that they name: `solid_mask`: 1 on every node with y = 0, y = 31, y = 16, z = 0 or z = 128 - 1 (walls of the two bores). `fan_hubs`: hub_y lies in 4 .. 27 and hub_z in 4 .. 123. `sources`: source nodes have 1 <= y <= 30 and 1 <= z <= 126. `populations`: every population is positive.
All inputs are finite; a program needn't handle non-finite values.
Results may differ from the reference program's by a relative error of at most 0.0001.
Values sent between devices are 32-bit elements; how exact they have to be, the bound alone decides.
No kernel may reach another device: no remote copies, remote signals or barrier semaphores. Data moves between devices by JAX's collectives and lax.ppermute only.
A program may use at most 64 MiB of HBM per device.

```python
import math
import jax
import jax.numpy as jnp

NZ = 128
FANS = 8
RAD = 3
FAN_LEN = 16
NSRC = 16
ITERS = 3
NX = 128
NY = 32


LATTICE = ((0, 0, 0), (1, 0, 0), (-1, 0, 0), (0, 1, 0), (0, -1, 0), (0, 0, 1), (0, 0, -1), (1, 1, 0), (-1, -1, 0), (1, -1, 0), (-1, 1, 0), (1, 0, 1), (-1, 0, -1), (1, 0, -1), (-1, 0, 1), (0, 1, 1), (0, -1, -1), (0, 1, -1), (0, -1, 1))


LATTICE_WEIGHTS = (1.0 / 3.0,) + (1.0 / 18.0,) * 6 + (1.0 / 36.0,) * 12


def draw_populations(key, part):
    first_key, second_key = jax.random.split(jax.random.fold_in(key, 11))
    density = 1.0 + jnp.clip(0.03 * jax.random.normal(first_key, (NX, NY, NZ), jnp.float32), -0.08, 0.08)
    velocity = jnp.clip(0.03 * jax.random.normal(second_key, (3, NX, NY, NZ), jnp.float32), -0.06, 0.06)
    speed_sq = velocity[0] * velocity[0] + velocity[1] * velocity[1] + velocity[2] * velocity[2]
    result = []
    for which in range(19):
        shift_x, shift_y, shift_z = LATTICE[which]
        along = shift_x * velocity[0] + shift_y * velocity[1] + shift_z * velocity[2]
        result.append(LATTICE_WEIGHTS[which] * density * (1.0 + 3.0 * along + 4.5 * along * along - 1.5 * speed_sq))
    return jnp.stack(result).astype(jnp.float32)


def draw_solid_mask(key, part):
    random_part = jax.random.randint(jax.random.fold_in(key, 23), (NX, NY, NZ), 0, 32) == 0
    coord_y = jnp.arange(NY, dtype=jnp.int32)[None, :, None]
    coord_z = jnp.arange(NZ, dtype=jnp.int32)[None, None, :]
    walls = (coord_y == 0) | (coord_y == NY - 1) | (coord_y == NY // 2) | (coord_z == 0) | (coord_z == NZ - 1)
    return (random_part | walls).astype(jnp.int32)


def draw_fan_hubs(key, part):
    keys = jax.random.split(jax.random.fold_in(key, 37), 3)
    along = jax.random.randint(keys[0], (FANS,), 0, NX)
    across = jax.random.randint(keys[1], (FANS,), RAD + 1, NY - RAD - 1)
    upward = jax.random.randint(keys[2], (FANS,), RAD + 1, NZ - RAD - 1)
    return jnp.stack([along, across, upward], axis=1).astype(jnp.int32)


def draw_sources(key, part):
    keys = jax.random.split(jax.random.fold_in(key, 41), 3)
    along = jax.random.randint(keys[0], (NSRC,), 0, NX)
    across = jax.random.randint(keys[1], (NSRC,), 1, NY - 1)
    upward = jax.random.randint(keys[2], (NSRC,), 1, NZ - 1)
    return jnp.stack([along, across, upward], axis=1).astype(jnp.int32)


def block_scale(stream_key, dims, shards, least, high):
    factor_of = 1.0
    for dim, shards_of in shards:
        heights = jax.random.uniform(jax.random.fold_in(jax.random.fold_in(stream_key, 6), dim), (shards_of,), jnp.float32, least / len(shards), high / len(shards))
        factor_of = factor_of * jnp.repeat(jnp.exp(heights), dims[dim] // shards_of).reshape((-1,) + (1,) * (len(dims) - 1 - dim))
    return factor_of


def setup_inputs(seed: int = 0) -> dict:
    key_list = jax.random.split(jax.random.key(seed), 9)
    return {
        "populations": draw_populations(jax.random.fold_in(key_list[8], 71), 0),
        "solid_mask": draw_solid_mask(jax.random.fold_in(key_list[8], 71), 0),
        "smoke_field": jnp.clip(1.0 * jax.random.uniform(key_list[2], (NX, NY, NZ), jnp.float32) ** block_scale(key_list[2], (NX, NY, NZ), ((0, 16), (1, 2)), -0.2, 0.2), 0.0, 1.0),
        "fan_hubs": draw_fan_hubs(jax.random.fold_in(key_list[8], 71), 0),
        "fan_gain": jnp.clip(jnp.exp(jax.random.uniform(key_list[4], (FANS,), jnp.float32, math.log(0.15), math.log(0.5))), 0.15, 0.5),
        "jet_speed": jnp.clip(jax.random.uniform(key_list[5], (FANS,), jnp.float32, 0.05, 0.12), 0.05, 0.12),
        "sources": draw_sources(jax.random.fold_in(key_list[8], 71), 0),
        "source_rate": jnp.clip(jnp.exp(jax.random.uniform(key_list[7], (NSRC,), jnp.float32, math.log(0.2), math.log(1.0))), 0.2, 1.0),
    }


VELOCITIES = ((0, 0, 0), (1, 0, 0), (-1, 0, 0), (0, 1, 0), (0, -1, 0), (0, 0, 1), (0, 0, -1), (1, 1, 0), (-1, -1, 0), (1, -1, 0), (-1, 1, 0), (1, 0, 1), (-1, 0, -1), (1, 0, -1), (-1, 0, 1), (0, 1, 1), (0, -1, -1), (0, 1, -1), (0, -1, 1))
WEIGHTS = (1.0 / 3.0,) + (1.0 / 18.0,) * 6 + (1.0 / 36.0,) * 12
OPPOSITE = (0, 2, 1, 4, 3, 6, 5, 8, 7, 10, 9, 12, 11, 14, 13, 16, 15, 18, 17)
RELAX_RATE = 1.0 / 0.6
DIFFUSIVITY = 0.12


def moments(populations):
    density = jnp.sum(populations, axis=0)
    velocity = []
    for dimension in range(3):
        forward = [populations[which] for which in range(19) if VELOCITIES[which][dimension] == 1]
        backward = [populations[which] for which in range(19) if VELOCITIES[which][dimension] == -1]
        velocity.append((sum(forward) - sum(backward)) / density)
    return density, velocity


def collide(populations, density, velocity, force_field, solid_flag):
    speed_sq = velocity[0] * velocity[0] + velocity[1] * velocity[1] + velocity[2] * velocity[2]
    posts = []
    for which in range(19):
        shift_x, shift_y, shift_z = VELOCITIES[which]
        along = shift_x * velocity[0] + shift_y * velocity[1] + shift_z * velocity[2]
        balance = WEIGHTS[which] * density * (1.0 + 3.0 * along + 4.5 * along * along - 1.5 * speed_sq)
        relaxed = populations[which] - RELAX_RATE * (populations[which] - balance) + 3.0 * WEIGHTS[which] * shift_x * force_field
        posts.append(jnp.where(solid_flag, populations[OPPOSITE[which]], relaxed))
    return jnp.stack(posts)


def disc_count():
    inside = 0
    for offset_a in range(-RAD, RAD + 1):
        for offset_b in range(-RAD, RAD + 1):
            if offset_a * offset_a + offset_b * offset_b <= RAD * RAD:
                inside = inside + 1
    return FAN_LEN * inside


def fan_discs(fan_hubs, coord_x, coord_y, coord_z, length_total):
    discs = []
    for fan_number in range(fan_hubs.shape[0]):
        offset_x = jnp.mod(coord_x - fan_hubs[fan_number, 0], length_total)
        offset_y = coord_y - fan_hubs[fan_number, 1]
        offset_z = coord_z - fan_hubs[fan_number, 2]
        discs.append((offset_x < FAN_LEN) & (offset_y * offset_y + offset_z * offset_z <= RAD * RAD))
    return discs


def partial_flow(discs, velocity, solid_flag):
    return jnp.stack([jnp.sum(jnp.where(disc_nodes & jnp.logical_not(solid_flag), velocity[0], 0.0)) for disc_nodes in discs])


def force_from(discs, totals, fan_gain, jet_speed):
    strength = fan_gain * (jet_speed - totals / float(disc_count()))
    force_field = jnp.zeros(discs[0].shape, jnp.float32)
    for fan_number in range(len(discs)):
        force_field = force_field + jnp.where(discs[fan_number], strength[fan_number], 0.0)
    return force_field


def advance(center, ahead_x, behind_x, ahead_y, behind_y, ahead_z, behind_z, velocity, solid_flag):
    laplace = ahead_x + behind_x + ahead_y + behind_y + ahead_z + behind_z - 6.0 * center
    advect = 0.5 * (velocity[0] * (ahead_x - behind_x) + velocity[1] * (ahead_y - behind_y) + velocity[2] * (ahead_z - behind_z))
    return jnp.where(solid_flag, 0.0, center + DIFFUSIVITY * laplace - advect)


def stream(posts):
    moved = []
    for which in range(19):
        shift_x, shift_y, shift_z = VELOCITIES[which]
        rolled = jnp.roll(posts[which], (shift_x, shift_y), axis=(0, 1))
        padded = jnp.pad(rolled, ((0, 0), (0, 0), (1, 1)))
        moved.append(padded[:, :, 1 - shift_z:1 - shift_z + NZ])
    return jnp.stack(moved)


def reference(populations, solid_mask, smoke_field, fan_hubs, fan_gain, jet_speed, sources, source_rate):
    solid_flag = solid_mask == 1
    coord_x = jnp.arange(NX, dtype=jnp.int32)[:, None, None]
    coord_y = jnp.arange(NY, dtype=jnp.int32)[None, :, None]
    coord_z = jnp.arange(NZ, dtype=jnp.int32)[None, None, :]
    discs = fan_discs(fan_hubs, coord_x, coord_y, coord_z, NX)
    for repeat in range(ITERS):
        density, velocity = moments(populations)
        totals = partial_flow(discs, velocity, solid_flag)
        force_field = force_from(discs, totals, fan_gain, jet_speed)
        posts = collide(populations, density, velocity, force_field, solid_flag)
        padded_z = jnp.pad(smoke_field, ((0, 0), (0, 0), (1, 1)))
        smoke_field = advance(smoke_field, jnp.roll(smoke_field, -1, 0), jnp.roll(smoke_field, 1, 0),
                              jnp.roll(smoke_field, -1, 1), jnp.roll(smoke_field, 1, 1),
                              padded_z[:, :, 2:], padded_z[:, :, :-2], velocity, solid_flag)
        smoke_field = smoke_field.at[sources[:, 0], sources[:, 1], sources[:, 2]].add(source_rate)
        populations = stream(posts)
    return populations, smoke_field
```

```python
import jax
import jax.numpy as jnp
from jax import lax
from jax.experimental import pallas as pl
from jax.experimental.pallas import tpu as pltpu
from jax.sharding import PartitionSpec as P

RAD = 3
FAN_LEN = 16
ITERS = 3


VELOCITIES = (
    (0, 0, 0),
    (1, 0, 0),
    (-1, 0, 0),
    (0, 1, 0),
    (0, -1, 0),
    (0, 0, 1),
    (0, 0, -1),
    (1, 1, 0),
    (-1, -1, 0),
    (1, -1, 0),
    (-1, 1, 0),
    (1, 0, 1),
    (-1, 0, -1),
    (1, 0, -1),
    (-1, 0, 1),
    (0, 1, 1),
    (0, -1, -1),
    (0, 1, -1),
    (0, -1, 1),
)
WEIGHTS = (1.0 / 3.0,) + (1.0 / 18.0,) * 6 + (1.0 / 36.0,) * 12
OPPOSITE = (0, 2, 1, 4, 3, 6, 5, 8, 7, 10, 9, 12, 11, 14, 13, 16, 15, 18, 17)
RELAX_RATE = 1.0 / 0.6
DIFFUSIVITY = 0.12


def extended_2(cells, sides, width):
    for axis, dim in sides:
        count = lax.axis_size(axis)
        head = lax.slice_in_dim(cells, 0, width, axis=dim)
        tail = lax.slice_in_dim(cells, cells.shape[dim] - width, cells.shape[dim], axis=dim)
        cells = jnp.concatenate(
            [
                lax.ppermute(tail, axis, [(i, (i + 1) % count) for i in range(count)]),
                cells,
                lax.ppermute(head, axis, [((i + 1) % count, i) for i in range(count)]),
            ],
            axis=dim,
        )
    return cells


def moments(populations):
    density = jnp.sum(populations, axis=0)
    velocity = []
    for dimension in range(3):
        forward = [populations[which] for which in range(19) if VELOCITIES[which][dimension] == 1]
        backward = [populations[which] for which in range(19) if VELOCITIES[which][dimension] == -1]
        velocity.append((sum(forward) - sum(backward)) / density)
    return (density, velocity)


def collide(populations, density, velocity, force_field, solid_flag):
    speed_sq = velocity[0] * velocity[0] + velocity[1] * velocity[1] + velocity[2] * velocity[2]
    posts = []
    for which in range(19):
        shift_x, shift_y, shift_z = VELOCITIES[which]
        along = shift_x * velocity[0] + shift_y * velocity[1] + shift_z * velocity[2]
        balance = (
            WEIGHTS[which] * density * (1.0 + 3.0 * along + 4.5 * along * along - 1.5 * speed_sq)
        )
        relaxed = (
            populations[which]
            - RELAX_RATE * (populations[which] - balance)
            + 3.0 * WEIGHTS[which] * shift_x * force_field
        )
        posts.append(jnp.where(solid_flag, populations[OPPOSITE[which]], relaxed))
    return jnp.stack(posts)


def disc_count():
    inside = 0
    for offset_a in range(-RAD, RAD + 1):
        for offset_b in range(-RAD, RAD + 1):
            if offset_a * offset_a + offset_b * offset_b <= RAD * RAD:
                inside = inside + 1
    return FAN_LEN * inside


def fan_discs(fan_hubs, coord_x, coord_y, coord_z, length_total):
    discs = []
    for fan_number in range(fan_hubs.shape[0]):
        offset_x = jnp.mod(coord_x - fan_hubs[fan_number, 0], length_total)
        offset_y = coord_y - fan_hubs[fan_number, 1]
        offset_z = coord_z - fan_hubs[fan_number, 2]
        discs.append(
            (offset_x < FAN_LEN) & (offset_y * offset_y + offset_z * offset_z <= RAD * RAD)
        )
    return discs


def partial_flow(discs, velocity, solid_flag):
    return jnp.stack(
        [
            jnp.sum(jnp.where(disc_nodes & jnp.logical_not(solid_flag), velocity[0], 0.0))
            for disc_nodes in discs
        ]
    )


def force_from(discs, totals, fan_gain, jet_speed):
    strength = fan_gain * (jet_speed - totals / float(disc_count()))
    force_field = jnp.zeros(discs[0].shape, jnp.float32)
    for fan_number in range(len(discs)):
        force_field = force_field + jnp.where(discs[fan_number], strength[fan_number], 0.0)
    return force_field


def advance(center, ahead_x, behind_x, ahead_y, behind_y, ahead_z, behind_z, velocity, solid_flag):
    laplace = ahead_x + behind_x + ahead_y + behind_y + ahead_z + behind_z - 6.0 * center
    advect = 0.5 * (
        velocity[0] * (ahead_x - behind_x)
        + velocity[1] * (ahead_y - behind_y)
        + velocity[2] * (ahead_z - behind_z)
    )
    return jnp.where(solid_flag, 0.0, center + DIFFUSIVITY * laplace - advect)


def shift_height(field, shift_z):
    if shift_z == 0:
        return field
    zero_layer = jnp.zeros(field.shape[:-1] + (1,), field.dtype)
    if shift_z == 1:
        return jnp.concatenate([zero_layer, field[..., :-1]], axis=-1)
    return jnp.concatenate([field[..., 1:], zero_layer], axis=-1)


def stream_kernel(extended_ref, out_ref):
    slab_len, band_width, height = out_ref.shape[1:]
    lane = lax.broadcasted_iota(jnp.int32, (slab_len, band_width, height), 2)
    for which in range(19):
        shift_x, shift_y, shift_z = VELOCITIES[which]
        piece = extended_ref[
            which, 1 - shift_x : 1 - shift_x + slab_len, 1 - shift_y : 1 - shift_y + band_width, :
        ]
        if shift_z == 1:
            piece = jnp.where(lane == 0, 0.0, pltpu.roll(piece, 1, 2))
        elif shift_z == -1:
            piece = jnp.where(lane == height - 1, 0.0, pltpu.roll(piece, height - 1, 2))
        out_ref[which] = piece


def stream_rimmed(extended, slab_len, band_width):
    shape = (19, slab_len, band_width, extended.shape[3])
    return pl.pallas_call(
        stream_kernel,
        out_shape=jax.ShapeDtypeStruct(shape, jnp.float32),
        in_specs=[pl.BlockSpec(memory_space=pltpu.VMEM)],
        out_specs=pl.BlockSpec(memory_space=pltpu.VMEM),
        cost_estimate=pl.CostEstimate(
            flops=0, transcendentals=0, bytes_accessed=8 * extended.size
        ),
    )(extended)


def window_sum(values, axis, width):
    count = lax.axis_size(axis)
    total = values
    for offset in sorted(set(step % count for step in range(-width, width + 1)) - {0}):
        total = total + lax.ppermute(
            values, axis, [(i, (i + offset) % count) for i in range(count)]
        )
    return total


def source_release(sources, source_rate, offset_len, offset_band, slab_len, band_width, height):
    local_x = sources[:, 0] - offset_len
    local_y = sources[:, 1] - offset_band
    pick_x = (local_x[:, None] == jnp.arange(slab_len, dtype=jnp.int32)[None, :]).astype(
        jnp.float32
    )
    pick_y = (local_y[:, None] == jnp.arange(band_width, dtype=jnp.int32)[None, :]).astype(
        jnp.float32
    )
    pick_z = (sources[:, 2][:, None] == jnp.arange(height, dtype=jnp.int32)[None, :]).astype(
        jnp.float32
    )
    weighted = source_rate[:, None] * pick_x
    cross_table = (pick_y[:, :, None] * pick_z[:, None, :]).reshape(
        sources.shape[0], band_width * height
    )
    released = jnp.dot(
        weighted.T, cross_table, precision=lax.Precision.HIGHEST, preferred_element_type=jnp.float32
    )
    return released.reshape(slab_len, band_width, height)


def body(populations, solid_mask, smoke_field, fan_hubs, fan_gain, jet_speed, sources, source_rate):
    slab_len = populations.shape[1]
    band_width = populations.shape[2]
    height = populations.shape[3]
    offset_len = lax.axis_index("len") * slab_len
    offset_band = lax.axis_index("band") * band_width
    length_total = slab_len * lax.axis_size("len")
    solid_flag = solid_mask == 1
    coord_x = offset_len + jnp.arange(slab_len, dtype=jnp.int32)[:, None, None]
    coord_y = offset_band + jnp.arange(band_width, dtype=jnp.int32)[None, :, None]
    coord_z = jnp.arange(height, dtype=jnp.int32)[None, None, :]
    discs = fan_discs(fan_hubs, coord_x, coord_y, coord_z, length_total)
    released = source_release(
        sources, source_rate, offset_len, offset_band, slab_len, band_width, height
    )
    len_reach = -(-(FAN_LEN - 1) // slab_len)
    band_reach = -(-(2 * RAD) // band_width)
    for repeat in range(ITERS):
        density, velocity = moments(populations)
        partials = partial_flow(discs, velocity, solid_flag)
        totals = window_sum(window_sum(partials, "band", band_reach), "len", len_reach)
        force_field = force_from(discs, totals, fan_gain, jet_speed)
        posts = collide(populations, density, velocity, force_field, solid_flag)
        rimmed = extended_2(smoke_field, (("len", 0), ("band", 1)), 1)
        extended = extended_2(posts, (("len", 1), ("band", 2)), 1)
        read = stream_rimmed(extended, slab_len, band_width)
        ahead_x = rimmed[2:, 1:-1]
        behind_x = rimmed[:-2, 1:-1]
        ahead_y = rimmed[1:-1, 2:]
        behind_y = rimmed[1:-1, :-2]
        smoke_field = advance(
            smoke_field,
            ahead_x,
            behind_x,
            ahead_y,
            behind_y,
            shift_height(smoke_field, -1),
            shift_height(smoke_field, 1),
            velocity,
            solid_flag,
        )
        smoke_field = smoke_field + released
        populations = read
    return (populations, smoke_field)


def solution(mesh):
    placed = (
        P(None, "len", "band", None),
        P("len", "band", None),
        P("len", "band", None),
        P(),
        P(),
        P(),
        P(),
        P(),
    )
    return jax.shard_map(
        body,
        mesh=mesh,
        in_specs=placed,
        out_specs=(P(None, "len", "band", None), P("len", "band", None)),
        check_vma=False,
    )
```

```python
import jax
import jax.numpy as jnp
from jax import lax
from jax.experimental import pallas as pl
from jax.experimental.pallas import tpu as pltpu
from jax.sharding import PartitionSpec as P

RAD = 3
FAN_LEN = 16
ITERS = 3


VELOCITIES = (
    (0, 0, 0),
    (1, 0, 0),
    (-1, 0, 0),
    (0, 1, 0),
    (0, -1, 0),
    (0, 0, 1),
    (0, 0, -1),
    (1, 1, 0),
    (-1, -1, 0),
    (1, -1, 0),
    (-1, 1, 0),
    (1, 0, 1),
    (-1, 0, -1),
    (1, 0, -1),
    (-1, 0, 1),
    (0, 1, 1),
    (0, -1, -1),
    (0, 1, -1),
    (0, -1, 1),
)
WEIGHTS = (1.0 / 3.0,) + (1.0 / 18.0,) * 6 + (1.0 / 36.0,) * 12
OPPOSITE = (0, 2, 1, 4, 3, 6, 5, 8, 7, 10, 9, 12, 11, 14, 13, 16, 15, 18, 17)
RELAX_RATE = 1.0 / 0.6
DIFFUSIVITY = 0.12


def extended_2(cells, sides, width):
    for axis, dim in sides:
        count = lax.axis_size(axis)
        head = lax.slice_in_dim(cells, 0, width, axis=dim)
        tail = lax.slice_in_dim(cells, cells.shape[dim] - width, cells.shape[dim], axis=dim)
        cells = jnp.concatenate(
            [
                lax.ppermute(tail, axis, [(i, (i + 1) % count) for i in range(count)]),
                cells,
                lax.ppermute(head, axis, [((i + 1) % count, i) for i in range(count)]),
            ],
            axis=dim,
        )
    return cells


def moments(populations):
    density = jnp.sum(populations, axis=0)
    velocity = []
    for dimension in range(3):
        forward = [populations[which] for which in range(19) if VELOCITIES[which][dimension] == 1]
        backward = [populations[which] for which in range(19) if VELOCITIES[which][dimension] == -1]
        velocity.append((sum(forward) - sum(backward)) / density)
    return (density, velocity)


def collide_kernel(populations_ref, force_ref, solid_ref, posts_ref):
    def plane(index, carry):
        populations = [populations_ref[which, index] for which in range(19)]
        density = sum(populations[1:], populations[0])
        velocity = []
        for dimension in range(3):
            forward = [populations[which] for which in range(19) if VELOCITIES[which][dimension] == 1]
            backward = [
                populations[which] for which in range(19) if VELOCITIES[which][dimension] == -1
            ]
            velocity.append((sum(forward) - sum(backward)) / density)
        force_field = force_ref[index]
        solid_flag = solid_ref[index] != 0
        speed_sq = velocity[0] * velocity[0] + velocity[1] * velocity[1] + velocity[2] * velocity[2]
        for which in range(19):
            shift_x, shift_y, shift_z = VELOCITIES[which]
            along = shift_x * velocity[0] + shift_y * velocity[1] + shift_z * velocity[2]
            balance = (
                WEIGHTS[which] * density * (1.0 + 3.0 * along + 4.5 * along * along - 1.5 * speed_sq)
            )
            relaxed = populations[which] - RELAX_RATE * (populations[which] - balance)
            if shift_x != 0:
                relaxed = relaxed + 3.0 * WEIGHTS[which] * shift_x * force_field
            posts_ref[which, index] = jnp.where(solid_flag, populations[OPPOSITE[which]], relaxed)
        return carry

    lax.fori_loop(0, populations_ref.shape[1], plane, 0)


def collide(populations, force_field, solid_mask):
    return pl.pallas_call(
        collide_kernel,
        out_shape=jax.ShapeDtypeStruct(populations.shape, jnp.float32),
        in_specs=[pl.BlockSpec(memory_space=pltpu.VMEM)] * 3,
        out_specs=pl.BlockSpec(memory_space=pltpu.VMEM),
        cost_estimate=pl.CostEstimate(
            flops=200 * force_field.size, transcendentals=0, bytes_accessed=8 * populations.size
        ),
    )(populations, force_field, solid_mask)


def disc_count():
    inside = 0
    for offset_a in range(-RAD, RAD + 1):
        for offset_b in range(-RAD, RAD + 1):
            if offset_a * offset_a + offset_b * offset_b <= RAD * RAD:
                inside = inside + 1
    return FAN_LEN * inside


def fan_discs(fan_hubs, coord_x, coord_y, coord_z, length_total):
    discs = []
    for fan_number in range(fan_hubs.shape[0]):
        offset_x = jnp.mod(coord_x - fan_hubs[fan_number, 0], length_total)
        offset_y = coord_y - fan_hubs[fan_number, 1]
        offset_z = coord_z - fan_hubs[fan_number, 2]
        discs.append(
            (offset_x < FAN_LEN) & (offset_y * offset_y + offset_z * offset_z <= RAD * RAD)
        )
    return discs


def partial_flow(discs, velocity, solid_flag):
    return jnp.stack(
        [
            jnp.sum(jnp.where(disc_nodes & jnp.logical_not(solid_flag), velocity[0], 0.0))
            for disc_nodes in discs
        ]
    )


def force_from(discs, totals, fan_gain, jet_speed):
    strength = fan_gain * (jet_speed - totals / float(disc_count()))
    force_field = jnp.zeros(discs[0].shape, jnp.float32)
    for fan_number in range(len(discs)):
        force_field = force_field + jnp.where(discs[fan_number], strength[fan_number], 0.0)
    return force_field


def advance(center, ahead_x, behind_x, ahead_y, behind_y, ahead_z, behind_z, velocity, solid_flag):
    laplace = ahead_x + behind_x + ahead_y + behind_y + ahead_z + behind_z - 6.0 * center
    advect = 0.5 * (
        velocity[0] * (ahead_x - behind_x)
        + velocity[1] * (ahead_y - behind_y)
        + velocity[2] * (ahead_z - behind_z)
    )
    return jnp.where(solid_flag, 0.0, center + DIFFUSIVITY * laplace - advect)


def shift_height(field, shift_z):
    if shift_z == 0:
        return field
    zero_layer = jnp.zeros(field.shape[:-1] + (1,), field.dtype)
    if shift_z == 1:
        return jnp.concatenate([zero_layer, field[..., :-1]], axis=-1)
    return jnp.concatenate([field[..., 1:], zero_layer], axis=-1)


def stream_kernel(extended_ref, out_ref):
    slab_len, band_width, height = out_ref.shape[1:]
    lane = lax.broadcasted_iota(jnp.int32, (slab_len, band_width, height), 2)
    for which in range(19):
        shift_x, shift_y, shift_z = VELOCITIES[which]
        piece = extended_ref[
            which, 1 - shift_x : 1 - shift_x + slab_len, 1 - shift_y : 1 - shift_y + band_width, :
        ]
        if shift_z == 1:
            piece = jnp.where(lane == 0, 0.0, pltpu.roll(piece, 1, 2))
        elif shift_z == -1:
            piece = jnp.where(lane == height - 1, 0.0, pltpu.roll(piece, height - 1, 2))
        out_ref[which] = piece


def stream_rimmed(extended, slab_len, band_width):
    shape = (19, slab_len, band_width, extended.shape[3])
    return pl.pallas_call(
        stream_kernel,
        out_shape=jax.ShapeDtypeStruct(shape, jnp.float32),
        in_specs=[pl.BlockSpec(memory_space=pltpu.VMEM)],
        out_specs=pl.BlockSpec(memory_space=pltpu.VMEM),
        cost_estimate=pl.CostEstimate(
            flops=0, transcendentals=0, bytes_accessed=8 * extended.size
        ),
    )(extended)


def window_sum(values, axis, width):
    count = lax.axis_size(axis)
    total = values
    for offset in sorted(set(step % count for step in range(-width, width + 1)) - {0}):
        total = total + lax.ppermute(
            values, axis, [(i, (i + offset) % count) for i in range(count)]
        )
    return total


def source_release(sources, source_rate, offset_len, offset_band, slab_len, band_width, height):
    local_x = sources[:, 0] - offset_len
    local_y = sources[:, 1] - offset_band
    pick_x = (local_x[:, None] == jnp.arange(slab_len, dtype=jnp.int32)[None, :]).astype(
        jnp.float32
    )
    pick_y = (local_y[:, None] == jnp.arange(band_width, dtype=jnp.int32)[None, :]).astype(
        jnp.float32
    )
    pick_z = (sources[:, 2][:, None] == jnp.arange(height, dtype=jnp.int32)[None, :]).astype(
        jnp.float32
    )
    weighted = source_rate[:, None] * pick_x
    cross_table = (pick_y[:, :, None] * pick_z[:, None, :]).reshape(
        sources.shape[0], band_width * height
    )
    released = jnp.dot(
        weighted.T, cross_table, precision=lax.Precision.HIGHEST, preferred_element_type=jnp.float32
    )
    return released.reshape(slab_len, band_width, height)


def body(populations, solid_mask, smoke_field, fan_hubs, fan_gain, jet_speed, sources, source_rate):
    slab_len = populations.shape[1]
    band_width = populations.shape[2]
    height = populations.shape[3]
    offset_len = lax.axis_index("len") * slab_len
    offset_band = lax.axis_index("band") * band_width
    length_total = slab_len * lax.axis_size("len")
    solid_flag = solid_mask == 1
    coord_x = offset_len + jnp.arange(slab_len, dtype=jnp.int32)[:, None, None]
    coord_y = offset_band + jnp.arange(band_width, dtype=jnp.int32)[None, :, None]
    coord_z = jnp.arange(height, dtype=jnp.int32)[None, None, :]
    discs = fan_discs(fan_hubs, coord_x, coord_y, coord_z, length_total)
    released = source_release(
        sources, source_rate, offset_len, offset_band, slab_len, band_width, height
    )
    len_reach = -(-(FAN_LEN - 1) // slab_len)
    band_reach = -(-(2 * RAD) // band_width)
    for repeat in range(ITERS):
        density, velocity = moments(populations)
        partials = partial_flow(discs, velocity, solid_flag)
        totals = window_sum(window_sum(partials, "band", band_reach), "len", len_reach)
        force_field = force_from(discs, totals, fan_gain, jet_speed)
        posts = collide(populations, force_field, solid_mask)
        rimmed = extended_2(smoke_field, (("len", 0), ("band", 1)), 1)
        extended = extended_2(posts, (("len", 1), ("band", 2)), 1)
        read = stream_rimmed(extended, slab_len, band_width)
        ahead_x = rimmed[2:, 1:-1]
        behind_x = rimmed[:-2, 1:-1]
        ahead_y = rimmed[1:-1, 2:]
        behind_y = rimmed[1:-1, :-2]
        smoke_field = advance(
            smoke_field,
            ahead_x,
            behind_x,
            ahead_y,
            behind_y,
            shift_height(smoke_field, -1),
            shift_height(smoke_field, 1),
            velocity,
            solid_flag,
        )
        smoke_field = smoke_field + released
        populations = read
    return (populations, smoke_field)


def solution(mesh):
    placed = (
        P(None, "len", "band", None),
        P("len", "band", None),
        P("len", "band", None),
        P(),
        P(),
        P(),
        P(),
        P(),
    )
    return jax.shard_map(
        body,
        mesh=mesh,
        in_specs=placed,
        out_specs=(P(None, "len", "band", None), P("len", "band", None)),
        check_vma=False,
    )
```

```python
import functools

import jax
import jax.numpy as jnp
from jax import lax
from jax.experimental import pallas as pl
from jax.experimental.pallas import tpu as pltpu
from jax.sharding import PartitionSpec as P

RAD = 3
FAN_LEN = 16
ITERS = 3


VELOCITIES = (
    (0, 0, 0),
    (1, 0, 0),
    (-1, 0, 0),
    (0, 1, 0),
    (0, -1, 0),
    (0, 0, 1),
    (0, 0, -1),
    (1, 1, 0),
    (-1, -1, 0),
    (1, -1, 0),
    (-1, 1, 0),
    (1, 0, 1),
    (-1, 0, -1),
    (1, 0, -1),
    (-1, 0, 1),
    (0, 1, 1),
    (0, -1, -1),
    (0, 1, -1),
    (0, -1, 1),
)
WEIGHTS = (1.0 / 3.0,) + (1.0 / 18.0,) * 6 + (1.0 / 36.0,) * 12
OPPOSITE = (0, 2, 1, 4, 3, 6, 5, 8, 7, 10, 9, 12, 11, 14, 13, 16, 15, 18, 17)
RELAX_RATE = 1.0 / 0.6
DIFFUSIVITY = 0.12


def extended_2(cells, sides, width):
    for axis, dim in sides:
        count = lax.axis_size(axis)
        head = lax.slice_in_dim(cells, 0, width, axis=dim)
        tail = lax.slice_in_dim(cells, cells.shape[dim] - width, cells.shape[dim], axis=dim)
        cells = jnp.concatenate(
            [
                lax.ppermute(tail, axis, [(i, (i + 1) % count) for i in range(count)]),
                cells,
                lax.ppermute(head, axis, [((i + 1) % count, i) for i in range(count)]),
            ],
            axis=dim,
        )
    return cells


def moments(populations):
    density = jnp.sum(populations, axis=0)
    velocity = []
    for dimension in range(3):
        forward = [populations[which] for which in range(19) if VELOCITIES[which][dimension] == 1]
        backward = [populations[which] for which in range(19) if VELOCITIES[which][dimension] == -1]
        velocity.append((sum(forward) - sum(backward)) / density)
    return (density, velocity)


def plane_moments(populations):
    density = sum(populations[1:], populations[0])
    velocity = []
    for dimension in range(3):
        forward = [populations[which] for which in range(19) if VELOCITIES[which][dimension] == 1]
        backward = [populations[which] for which in range(19) if VELOCITIES[which][dimension] == -1]
        velocity.append((sum(forward) - sum(backward)) / density)
    return (density, velocity)


def step_kernel(with_moments, strength_ref, populations_ref, discs_ref, solid_ref, *rest):
    if with_moments:
        out_ref, velocity_ref, flow_ref, posts_ref = rest
    else:
        out_ref, posts_ref = rest
    fans = discs_ref.shape[0]
    slab_len, band_width, height = out_ref.shape[1:]

    def collide_plane(index, carry):
        populations = [populations_ref[which, index] for which in range(19)]
        density, velocity = plane_moments(populations)
        force_field = strength_ref[0] * discs_ref[0, index]
        for fan_number in range(1, fans):
            force_field = force_field + strength_ref[fan_number] * discs_ref[fan_number, index]
        solid_flag = solid_ref[index] != 0.0
        speed_sq = velocity[0] * velocity[0] + velocity[1] * velocity[1] + velocity[2] * velocity[2]
        for which in range(19):
            shift_x, shift_y, shift_z = VELOCITIES[which]
            along = shift_x * velocity[0] + shift_y * velocity[1] + shift_z * velocity[2]
            balance = (
                WEIGHTS[which] * density * (1.0 + 3.0 * along + 4.5 * along * along - 1.5 * speed_sq)
            )
            relaxed = populations[which] - RELAX_RATE * (populations[which] - balance)
            if shift_x != 0:
                relaxed = relaxed + 3.0 * WEIGHTS[which] * shift_x * force_field
            posts_ref[which, index] = jnp.where(solid_flag, populations[OPPOSITE[which]], relaxed)
        return carry

    lax.fori_loop(0, populations_ref.shape[1], collide_plane, 0)
    lane = lax.broadcasted_iota(jnp.int32, (slab_len, band_width, height), 2)
    for which in range(19):
        shift_x, shift_y, shift_z = VELOCITIES[which]
        piece = posts_ref[
            which, 1 - shift_x : 1 - shift_x + slab_len, 1 - shift_y : 1 - shift_y + band_width, :
        ]
        if shift_z == 1:
            piece = jnp.where(lane == 0, 0.0, pltpu.roll(piece, 1, 2))
        elif shift_z == -1:
            piece = jnp.where(lane == height - 1, 0.0, pltpu.roll(piece, height - 1, 2))
        out_ref[which] = piece
    if not with_moments:
        return
    flow_ref[...] = jnp.zeros(flow_ref.shape, jnp.float32)

    def moment_plane(index, carry):
        density, velocity = plane_moments([out_ref[which, index] for which in range(19)])
        for dimension in range(3):
            velocity_ref[dimension, index] = velocity[dimension]
        for fan_number in range(fans):
            flow_ref[fan_number] += (
                discs_ref[fan_number, index + 1, 1 : 1 + band_width, :] * velocity[0]
            )
        return carry

    lax.fori_loop(0, slab_len, moment_plane, 0)


def lattice_step(strength, extended, discs, solid_rim, with_moments):
    slab_len = extended.shape[1] - 2
    band_width = extended.shape[2] - 2
    height = extended.shape[3]
    fans = discs.shape[0]
    out_shape = [jax.ShapeDtypeStruct((19, slab_len, band_width, height), jnp.float32)]
    if with_moments:
        out_shape.append(jax.ShapeDtypeStruct((3, slab_len, band_width, height), jnp.float32))
        out_shape.append(jax.ShapeDtypeStruct((fans, band_width, height), jnp.float32))
    vmem = pl.BlockSpec(memory_space=pltpu.VMEM)
    return pl.pallas_call(
        functools.partial(step_kernel, with_moments),
        out_shape=tuple(out_shape),
        in_specs=[pl.BlockSpec(memory_space=pltpu.SMEM), vmem, vmem, vmem],
        out_specs=tuple([vmem] * len(out_shape)),
        scratch_shapes=[pltpu.VMEM(extended.shape, jnp.float32)],
        cost_estimate=pl.CostEstimate(
            flops=300 * solid_rim.size, transcendentals=0, bytes_accessed=12 * extended.size
        ),
    )(strength, extended, discs, solid_rim)


def disc_count():
    inside = 0
    for offset_a in range(-RAD, RAD + 1):
        for offset_b in range(-RAD, RAD + 1):
            if offset_a * offset_a + offset_b * offset_b <= RAD * RAD:
                inside = inside + 1
    return FAN_LEN * inside


def fan_discs(fan_hubs, coord_x, coord_y, coord_z, length_total):
    discs = []
    for fan_number in range(fan_hubs.shape[0]):
        offset_x = jnp.mod(coord_x - fan_hubs[fan_number, 0], length_total)
        offset_y = coord_y - fan_hubs[fan_number, 1]
        offset_z = coord_z - fan_hubs[fan_number, 2]
        discs.append(
            (offset_x < FAN_LEN) & (offset_y * offset_y + offset_z * offset_z <= RAD * RAD)
        )
    return discs


def partial_flow(discs, velocity, solid_flag):
    return jnp.stack(
        [
            jnp.sum(jnp.where(disc_nodes & jnp.logical_not(solid_flag), velocity[0], 0.0))
            for disc_nodes in discs
        ]
    )


def force_from(discs, totals, fan_gain, jet_speed):
    strength = fan_gain * (jet_speed - totals / float(disc_count()))
    force_field = jnp.zeros(discs[0].shape, jnp.float32)
    for fan_number in range(len(discs)):
        force_field = force_field + jnp.where(discs[fan_number], strength[fan_number], 0.0)
    return force_field


def advance(center, ahead_x, behind_x, ahead_y, behind_y, ahead_z, behind_z, velocity, solid_flag):
    laplace = ahead_x + behind_x + ahead_y + behind_y + ahead_z + behind_z - 6.0 * center
    advect = 0.5 * (
        velocity[0] * (ahead_x - behind_x)
        + velocity[1] * (ahead_y - behind_y)
        + velocity[2] * (ahead_z - behind_z)
    )
    return jnp.where(solid_flag, 0.0, center + DIFFUSIVITY * laplace - advect)


def shift_height(field, shift_z):
    if shift_z == 0:
        return field
    zero_layer = jnp.zeros(field.shape[:-1] + (1,), field.dtype)
    if shift_z == 1:
        return jnp.concatenate([zero_layer, field[..., :-1]], axis=-1)
    return jnp.concatenate([field[..., 1:], zero_layer], axis=-1)


def window_sum(values, axis, width):
    count = lax.axis_size(axis)
    total = values
    for offset in sorted(set(step % count for step in range(-width, width + 1)) - {0}):
        total = total + lax.ppermute(
            values, axis, [(i, (i + offset) % count) for i in range(count)]
        )
    return total


def source_release(sources, source_rate, offset_len, offset_band, slab_len, band_width, height):
    local_x = sources[:, 0] - offset_len
    local_y = sources[:, 1] - offset_band
    pick_x = (local_x[:, None] == jnp.arange(slab_len, dtype=jnp.int32)[None, :]).astype(
        jnp.float32
    )
    pick_y = (local_y[:, None] == jnp.arange(band_width, dtype=jnp.int32)[None, :]).astype(
        jnp.float32
    )
    pick_z = (sources[:, 2][:, None] == jnp.arange(height, dtype=jnp.int32)[None, :]).astype(
        jnp.float32
    )
    weighted = source_rate[:, None] * pick_x
    cross_table = (pick_y[:, :, None] * pick_z[:, None, :]).reshape(
        sources.shape[0], band_width * height
    )
    released = jnp.dot(
        weighted.T, cross_table, precision=lax.Precision.HIGHEST, preferred_element_type=jnp.float32
    )
    return released.reshape(slab_len, band_width, height)


def body(populations, solid_mask, smoke_field, fan_hubs, fan_gain, jet_speed, sources, source_rate):
    slab_len = populations.shape[1]
    band_width = populations.shape[2]
    height = populations.shape[3]
    offset_len = lax.axis_index("len") * slab_len
    offset_band = lax.axis_index("band") * band_width
    length_total = slab_len * lax.axis_size("len")
    breadth_total = band_width * lax.axis_size("band")
    solid_flag = solid_mask == 1
    solid_rim = extended_2(solid_flag.astype(jnp.float32), (("len", 0), ("band", 1)), 1)
    coord_x = offset_len - 1 + jnp.arange(slab_len + 2, dtype=jnp.int32)[:, None, None]
    coord_y = jnp.mod(
        offset_band - 1 + jnp.arange(band_width + 2, dtype=jnp.int32)[None, :, None], breadth_total
    )
    coord_z = jnp.arange(height, dtype=jnp.int32)[None, None, :]
    air_rim = solid_rim == 0.0
    discs = jnp.stack(
        [
            (disc_nodes & air_rim).astype(jnp.float32)
            for disc_nodes in fan_discs(fan_hubs, coord_x, coord_y, coord_z, length_total)
        ]
    )
    released = source_release(
        sources, source_rate, offset_len, offset_band, slab_len, band_width, height
    )
    len_reach = max(-(-FAN_LEN // slab_len), (slab_len + FAN_LEN - 1) // slab_len)
    band_reach = max(-(-(2 * RAD + 1) // band_width), (band_width + 2 * RAD) // band_width)
    density, velocity = moments(populations)
    velocity = jnp.stack(velocity)
    partials = jnp.sum(discs[:, 1:-1, 1:-1, :] * velocity[0][None], axis=(1, 2, 3))
    for repeat in range(ITERS):
        totals = window_sum(window_sum(partials, "band", band_reach), "len", len_reach)
        strength = fan_gain * (jet_speed - totals / float(disc_count()))
        extended = extended_2(populations, (("len", 1), ("band", 2)), 1)
        last = repeat == ITERS - 1
        stepped = lattice_step(strength, extended, discs, solid_rim, not last)
        rimmed = extended_2(smoke_field, (("len", 0), ("band", 1)), 1)
        ahead_x = rimmed[2:, 1:-1]
        behind_x = rimmed[:-2, 1:-1]
        ahead_y = rimmed[1:-1, 2:]
        behind_y = rimmed[1:-1, :-2]
        smoke_field = advance(
            smoke_field,
            ahead_x,
            behind_x,
            ahead_y,
            behind_y,
            shift_height(smoke_field, -1),
            shift_height(smoke_field, 1),
            velocity,
            solid_flag,
        )
        smoke_field = smoke_field + released
        populations = stepped[0]
        if not last:
            velocity = stepped[1]
            partials = jnp.sum(stepped[2], axis=(1, 2))
    return (populations, smoke_field)


def solution(mesh):
    placed = (
        P(None, "len", "band", None),
        P("len", "band", None),
        P("len", "band", None),
        P(),
        P(),
        P(),
        P(),
        P(),
    )
    return jax.shard_map(
        body,
        mesh=mesh,
        in_specs=placed,
        out_specs=(P(None, "len", "band", None), P("len", "band", None)),
        check_vma=False,
    )
```

```python
import functools

import jax
import jax.numpy as jnp
from jax import lax
from jax.experimental import pallas as pl
from jax.experimental.pallas import tpu as pltpu
from jax.sharding import PartitionSpec as P

RAD = 3
FAN_LEN = 16
ITERS = 3


VELOCITIES = (
    (0, 0, 0),
    (1, 0, 0),
    (-1, 0, 0),
    (0, 1, 0),
    (0, -1, 0),
    (0, 0, 1),
    (0, 0, -1),
    (1, 1, 0),
    (-1, -1, 0),
    (1, -1, 0),
    (-1, 1, 0),
    (1, 0, 1),
    (-1, 0, -1),
    (1, 0, -1),
    (-1, 0, 1),
    (0, 1, 1),
    (0, -1, -1),
    (0, 1, -1),
    (0, -1, 1),
)
WEIGHTS = (1.0 / 3.0,) + (1.0 / 18.0,) * 6 + (1.0 / 36.0,) * 12
OPPOSITE = (0, 2, 1, 4, 3, 6, 5, 8, 7, 10, 9, 12, 11, 14, 13, 16, 15, 18, 17)
RELAX_RATE = 1.0 / 0.6
DIFFUSIVITY = 0.12


def extended_2(cells, sides, width):
    for axis, dim in sides:
        count = lax.axis_size(axis)
        head = lax.slice_in_dim(cells, 0, width, axis=dim)
        tail = lax.slice_in_dim(cells, cells.shape[dim] - width, cells.shape[dim], axis=dim)
        cells = jnp.concatenate(
            [
                lax.ppermute(tail, axis, [(i, (i + 1) % count) for i in range(count)]),
                cells,
                lax.ppermute(head, axis, [((i + 1) % count, i) for i in range(count)]),
            ],
            axis=dim,
        )
    return cells


def moments(populations):
    density = jnp.sum(populations, axis=0)
    velocity = []
    for dimension in range(3):
        forward = [populations[which] for which in range(19) if VELOCITIES[which][dimension] == 1]
        backward = [populations[which] for which in range(19) if VELOCITIES[which][dimension] == -1]
        velocity.append((sum(forward) - sum(backward)) / density)
    return (density, velocity)


def plane_moments(populations):
    density = sum(populations[1:], populations[0])
    velocity = []
    for dimension in range(3):
        forward = [populations[which] for which in range(19) if VELOCITIES[which][dimension] == 1]
        backward = [populations[which] for which in range(19) if VELOCITIES[which][dimension] == -1]
        velocity.append((sum(forward) - sum(backward)) / density)
    return (density, velocity)


def step_kernel(with_moments, strength_ref, populations_ref, discs_ref, solid_ref, *rest):
    if with_moments:
        out_ref, velocity_ref, flow_ref, posts_ref = rest
    else:
        out_ref, posts_ref = rest
    fans = discs_ref.shape[0]
    slab_len, band_width, height = out_ref.shape[1:]

    def collide_plane(index, carry):
        populations = [populations_ref[which, index] for which in range(19)]
        density, velocity = plane_moments(populations)
        force_field = strength_ref[0] * discs_ref[0, index]
        for fan_number in range(1, fans):
            force_field = force_field + strength_ref[fan_number] * discs_ref[fan_number, index]
        solid_flag = solid_ref[index] != 0.0
        speed_sq = velocity[0] * velocity[0] + velocity[1] * velocity[1] + velocity[2] * velocity[2]
        for which in range(19):
            shift_x, shift_y, shift_z = VELOCITIES[which]
            along = shift_x * velocity[0] + shift_y * velocity[1] + shift_z * velocity[2]
            balance = (
                WEIGHTS[which] * density * (1.0 + 3.0 * along + 4.5 * along * along - 1.5 * speed_sq)
            )
            relaxed = populations[which] - RELAX_RATE * (populations[which] - balance)
            if shift_x != 0:
                relaxed = relaxed + 3.0 * WEIGHTS[which] * shift_x * force_field
            posts_ref[which, index] = jnp.where(solid_flag, populations[OPPOSITE[which]], relaxed)
        return carry

    lax.fori_loop(0, populations_ref.shape[1], collide_plane, 0)
    lane = lax.broadcasted_iota(jnp.int32, (slab_len, band_width, height), 2)
    for which in range(19):
        shift_x, shift_y, shift_z = VELOCITIES[which]
        piece = posts_ref[
            which, 1 - shift_x : 1 - shift_x + slab_len, 1 - shift_y : 1 - shift_y + band_width, :
        ]
        if shift_z == 1:
            piece = jnp.where(lane == 0, 0.0, pltpu.roll(piece, 1, 2))
        elif shift_z == -1:
            piece = jnp.where(lane == height - 1, 0.0, pltpu.roll(piece, height - 1, 2))
        out_ref[which] = piece
    if not with_moments:
        return
    flow_ref[...] = jnp.zeros(flow_ref.shape, jnp.float32)

    def moment_plane(index, carry):
        density, velocity = plane_moments([out_ref[which, index] for which in range(19)])
        for dimension in range(3):
            velocity_ref[dimension, index] = velocity[dimension]
        for fan_number in range(fans):
            flow_ref[fan_number] += (
                discs_ref[fan_number, index + 1, 1 : 1 + band_width, :] * velocity[0]
            )
        return carry

    lax.fori_loop(0, slab_len, moment_plane, 0)


def lattice_step(strength, extended, discs, solid_rim, with_moments):
    slab_len = extended.shape[1] - 2
    band_width = extended.shape[2] - 2
    height = extended.shape[3]
    fans = discs.shape[0]
    out_shape = [jax.ShapeDtypeStruct((19, slab_len, band_width, height), jnp.float32)]
    if with_moments:
        out_shape.append(jax.ShapeDtypeStruct((3, slab_len, band_width, height), jnp.float32))
        out_shape.append(jax.ShapeDtypeStruct((fans, band_width, height), jnp.float32))
    vmem = pl.BlockSpec(memory_space=pltpu.VMEM)
    return pl.pallas_call(
        functools.partial(step_kernel, with_moments),
        out_shape=tuple(out_shape),
        in_specs=[pl.BlockSpec(memory_space=pltpu.SMEM), vmem, vmem, vmem],
        out_specs=tuple([vmem] * len(out_shape)),
        scratch_shapes=[pltpu.VMEM(extended.shape, jnp.float32)],
        cost_estimate=pl.CostEstimate(
            flops=300 * solid_rim.size, transcendentals=0, bytes_accessed=12 * extended.size
        ),
    )(strength, extended, discs, solid_rim)


def disc_count():
    inside = 0
    for offset_a in range(-RAD, RAD + 1):
        for offset_b in range(-RAD, RAD + 1):
            if offset_a * offset_a + offset_b * offset_b <= RAD * RAD:
                inside = inside + 1
    return FAN_LEN * inside


def fan_discs(fan_hubs, coord_x, coord_y, coord_z, length_total):
    discs = []
    for fan_number in range(fan_hubs.shape[0]):
        offset_x = jnp.mod(coord_x - fan_hubs[fan_number, 0], length_total)
        offset_y = coord_y - fan_hubs[fan_number, 1]
        offset_z = coord_z - fan_hubs[fan_number, 2]
        discs.append(
            (offset_x < FAN_LEN) & (offset_y * offset_y + offset_z * offset_z <= RAD * RAD)
        )
    return discs


def partial_flow(discs, velocity, solid_flag):
    return jnp.stack(
        [
            jnp.sum(jnp.where(disc_nodes & jnp.logical_not(solid_flag), velocity[0], 0.0))
            for disc_nodes in discs
        ]
    )


def force_from(discs, totals, fan_gain, jet_speed):
    strength = fan_gain * (jet_speed - totals / float(disc_count()))
    force_field = jnp.zeros(discs[0].shape, jnp.float32)
    for fan_number in range(len(discs)):
        force_field = force_field + jnp.where(discs[fan_number], strength[fan_number], 0.0)
    return force_field


def advance(center, ahead_x, behind_x, ahead_y, behind_y, ahead_z, behind_z, velocity, solid_flag):
    laplace = ahead_x + behind_x + ahead_y + behind_y + ahead_z + behind_z - 6.0 * center
    advect = 0.5 * (
        velocity[0] * (ahead_x - behind_x)
        + velocity[1] * (ahead_y - behind_y)
        + velocity[2] * (ahead_z - behind_z)
    )
    return jnp.where(solid_flag, 0.0, center + DIFFUSIVITY * laplace - advect)


def shift_height(field, shift_z):
    if shift_z == 0:
        return field
    zero_layer = jnp.zeros(field.shape[:-1] + (1,), field.dtype)
    if shift_z == 1:
        return jnp.concatenate([zero_layer, field[..., :-1]], axis=-1)
    return jnp.concatenate([field[..., 1:], zero_layer], axis=-1)


def rim_round(populations, smoke, flow, axis, dim, reach):
    count = lax.axis_size(axis)
    fans = flow.shape[0]

    def piece(start):
        cells = lax.slice_in_dim(populations, start, start + 1, axis=dim)
        fumes = lax.slice_in_dim(smoke, start, start + 1, axis=dim - 1)[None]
        carrier = jnp.zeros(cells.shape[1:], jnp.float32).at[0, 0, :fans].set(flow)[None]
        return jnp.concatenate([cells, fumes, carrier], axis=0)

    head = piece(0)
    tail = piece(populations.shape[dim] - 1)
    forward = [(i, (i + 1) % count) for i in range(count)]
    backward = [((i + 1) % count, i) for i in range(count)]
    if count == 2:
        both = lax.ppermute(jnp.concatenate([tail, head], axis=0), axis, forward)
        from_left = both[: tail.shape[0]]
        from_right = both[tail.shape[0] :]
        total = flow + from_left[-1, 0, 0, :fans]
    else:
        from_left = lax.ppermute(tail, axis, forward)
        from_right = lax.ppermute(head, axis, backward)
        total = flow + from_left[-1, 0, 0, :fans] + from_right[-1, 0, 0, :fans]
    for offset in sorted(set(step % count for step in range(-reach, reach + 1)) - {0, 1, count - 1}):
        total = total + lax.ppermute(flow, axis, [(i, (i + offset) % count) for i in range(count)])
    populations = jnp.concatenate([from_left[:19], populations, from_right[:19]], axis=dim)
    smoke = jnp.concatenate([from_left[19], smoke, from_right[19]], axis=dim - 1)
    return (populations, smoke, total)


def window_sum(values, axis, width):
    count = lax.axis_size(axis)
    total = values
    for offset in sorted(set(step % count for step in range(-width, width + 1)) - {0}):
        total = total + lax.ppermute(
            values, axis, [(i, (i + offset) % count) for i in range(count)]
        )
    return total


def source_release(sources, source_rate, offset_len, offset_band, slab_len, band_width, height):
    local_x = sources[:, 0] - offset_len
    local_y = sources[:, 1] - offset_band
    pick_x = (local_x[:, None] == jnp.arange(slab_len, dtype=jnp.int32)[None, :]).astype(
        jnp.float32
    )
    pick_y = (local_y[:, None] == jnp.arange(band_width, dtype=jnp.int32)[None, :]).astype(
        jnp.float32
    )
    pick_z = (sources[:, 2][:, None] == jnp.arange(height, dtype=jnp.int32)[None, :]).astype(
        jnp.float32
    )
    weighted = source_rate[:, None] * pick_x
    cross_table = (pick_y[:, :, None] * pick_z[:, None, :]).reshape(
        sources.shape[0], band_width * height
    )
    released = jnp.dot(
        weighted.T, cross_table, precision=lax.Precision.HIGHEST, preferred_element_type=jnp.float32
    )
    return released.reshape(slab_len, band_width, height)


def body(populations, solid_mask, smoke_field, fan_hubs, fan_gain, jet_speed, sources, source_rate):
    slab_len = populations.shape[1]
    band_width = populations.shape[2]
    height = populations.shape[3]
    offset_len = lax.axis_index("len") * slab_len
    offset_band = lax.axis_index("band") * band_width
    length_total = slab_len * lax.axis_size("len")
    breadth_total = band_width * lax.axis_size("band")
    solid_flag = solid_mask == 1
    solid_rim = extended_2(solid_flag.astype(jnp.float32), (("len", 0), ("band", 1)), 1)
    coord_x = offset_len - 1 + jnp.arange(slab_len + 2, dtype=jnp.int32)[:, None, None]
    coord_y = jnp.mod(
        offset_band - 1 + jnp.arange(band_width + 2, dtype=jnp.int32)[None, :, None], breadth_total
    )
    coord_z = jnp.arange(height, dtype=jnp.int32)[None, None, :]
    air_rim = solid_rim == 0.0
    discs = jnp.stack(
        [
            (disc_nodes & air_rim).astype(jnp.float32)
            for disc_nodes in fan_discs(fan_hubs, coord_x, coord_y, coord_z, length_total)
        ]
    )
    released = source_release(
        sources, source_rate, offset_len, offset_band, slab_len, band_width, height
    )
    len_reach = max(-(-FAN_LEN // slab_len), (slab_len + FAN_LEN - 1) // slab_len)
    band_reach = max(-(-(2 * RAD + 1) // band_width), (band_width + 2 * RAD) // band_width)
    density, velocity = moments(populations)
    velocity = jnp.stack(velocity)
    partials = jnp.sum(discs[:, 1:-1, 1:-1, :] * velocity[0][None], axis=(1, 2, 3))
    for repeat in range(ITERS):
        extended, rimmed, totals = rim_round(populations, smoke_field, partials, "len", 1, len_reach)
        extended, rimmed, totals = rim_round(extended, rimmed, totals, "band", 2, band_reach)
        strength = fan_gain * (jet_speed - totals / float(disc_count()))
        last = repeat == ITERS - 1
        stepped = lattice_step(strength, extended, discs, solid_rim, not last)
        ahead_x = rimmed[2:, 1:-1]
        behind_x = rimmed[:-2, 1:-1]
        ahead_y = rimmed[1:-1, 2:]
        behind_y = rimmed[1:-1, :-2]
        smoke_field = advance(
            smoke_field,
            ahead_x,
            behind_x,
            ahead_y,
            behind_y,
            shift_height(smoke_field, -1),
            shift_height(smoke_field, 1),
            velocity,
            solid_flag,
        )
        smoke_field = smoke_field + released
        populations = stepped[0]
        if not last:
            velocity = stepped[1]
            partials = jnp.sum(stepped[2], axis=(1, 2))
    return (populations, smoke_field)


def solution(mesh):
    placed = (
        P(None, "len", "band", None),
        P("len", "band", None),
        P("len", "band", None),
        P(),
        P(),
        P(),
        P(),
        P(),
    )
    return jax.shard_map(
        body,
        mesh=mesh,
        in_specs=placed,
        out_specs=(P(None, "len", "band", None), P("len", "band", None)),
        check_vma=False,
    )
```

```python
import functools

import jax
import jax.numpy as jnp
from jax import lax
from jax.experimental import pallas as pl
from jax.experimental.pallas import tpu as pltpu
from jax.sharding import PartitionSpec as P

RAD = 3
FAN_LEN = 16
ITERS = 3


VELOCITIES = (
    (0, 0, 0),
    (1, 0, 0),
    (-1, 0, 0),
    (0, 1, 0),
    (0, -1, 0),
    (0, 0, 1),
    (0, 0, -1),
    (1, 1, 0),
    (-1, -1, 0),
    (1, -1, 0),
    (-1, 1, 0),
    (1, 0, 1),
    (-1, 0, -1),
    (1, 0, -1),
    (-1, 0, 1),
    (0, 1, 1),
    (0, -1, -1),
    (0, 1, -1),
    (0, -1, 1),
)
WEIGHTS = (1.0 / 3.0,) + (1.0 / 18.0,) * 6 + (1.0 / 36.0,) * 12
OPPOSITE = (0, 2, 1, 4, 3, 6, 5, 8, 7, 10, 9, 12, 11, 14, 13, 16, 15, 18, 17)
RELAX_RATE = 1.0 / 0.6
DIFFUSIVITY = 0.12


def extended_2(cells, sides, width):
    for axis, dim in sides:
        count = lax.axis_size(axis)
        head = lax.slice_in_dim(cells, 0, width, axis=dim)
        tail = lax.slice_in_dim(cells, cells.shape[dim] - width, cells.shape[dim], axis=dim)
        cells = jnp.concatenate(
            [
                lax.ppermute(tail, axis, [(i, (i + 1) % count) for i in range(count)]),
                cells,
                lax.ppermute(head, axis, [((i + 1) % count, i) for i in range(count)]),
            ],
            axis=dim,
        )
    return cells


def moments(populations):
    density = jnp.sum(populations, axis=0)
    velocity = []
    for dimension in range(3):
        forward = [populations[which] for which in range(19) if VELOCITIES[which][dimension] == 1]
        backward = [populations[which] for which in range(19) if VELOCITIES[which][dimension] == -1]
        velocity.append((sum(forward) - sum(backward)) / density)
    return (density, velocity)


def plane_moments(populations):
    density = sum(populations[1:], populations[0])
    velocity = []
    for dimension in range(3):
        forward = [populations[which] for which in range(19) if VELOCITIES[which][dimension] == 1]
        backward = [populations[which] for which in range(19) if VELOCITIES[which][dimension] == -1]
        velocity.append((sum(forward) - sum(backward)) / density)
    return (density, velocity)


def step_kernel(with_moments, strength_ref, populations_ref, discs_ref, solid_ref, *rest):
    if with_moments:
        out_ref, velocity_ref, flow_ref, posts_ref = rest
    else:
        out_ref, posts_ref = rest
    fans = discs_ref.shape[0]
    slab_len, band_width, height = out_ref.shape[1:]

    def collide_plane(index, carry):
        populations = [populations_ref[which, index] for which in range(19)]
        density, velocity = plane_moments(populations)
        force_field = strength_ref[0] * discs_ref[0, index]
        for fan_number in range(1, fans):
            force_field = force_field + strength_ref[fan_number] * discs_ref[fan_number, index]
        solid_flag = solid_ref[index] != 0.0
        speed_sq = velocity[0] * velocity[0] + velocity[1] * velocity[1] + velocity[2] * velocity[2]
        for which in range(19):
            shift_x, shift_y, shift_z = VELOCITIES[which]
            along = shift_x * velocity[0] + shift_y * velocity[1] + shift_z * velocity[2]
            balance = (
                WEIGHTS[which] * density * (1.0 + 3.0 * along + 4.5 * along * along - 1.5 * speed_sq)
            )
            relaxed = populations[which] - RELAX_RATE * (populations[which] - balance)
            if shift_x != 0:
                relaxed = relaxed + 3.0 * WEIGHTS[which] * shift_x * force_field
            posts_ref[which, index] = jnp.where(solid_flag, populations[OPPOSITE[which]], relaxed)
        return carry

    lax.fori_loop(0, populations_ref.shape[1], collide_plane, 0)
    lane = lax.broadcasted_iota(jnp.int32, (slab_len, band_width, height), 2)
    for which in range(19):
        shift_x, shift_y, shift_z = VELOCITIES[which]
        piece = posts_ref[
            which, 1 - shift_x : 1 - shift_x + slab_len, 1 - shift_y : 1 - shift_y + band_width, :
        ]
        if shift_z == 1:
            piece = jnp.where(lane == 0, 0.0, pltpu.roll(piece, 1, 2))
        elif shift_z == -1:
            piece = jnp.where(lane == height - 1, 0.0, pltpu.roll(piece, height - 1, 2))
        out_ref[which] = piece
    if not with_moments:
        return
    moments_into(out_ref, discs_ref, 1, velocity_ref, flow_ref)


def moments_into(populations_ref, discs_ref, rim, velocity_ref, flow_ref):
    fans = discs_ref.shape[0]
    band_width = populations_ref.shape[2]
    flow_ref[...] = jnp.zeros(flow_ref.shape, jnp.float32)

    def moment_plane(index, carry):
        density, velocity = plane_moments([populations_ref[which, index] for which in range(19)])
        for dimension in range(3):
            velocity_ref[dimension, index] = velocity[dimension]
        for fan_number in range(fans):
            flow_ref[fan_number] += (
                discs_ref[fan_number, index + rim, rim : rim + band_width, :] * velocity[0]
            )
        return carry

    lax.fori_loop(0, populations_ref.shape[1], moment_plane, 0)


def first_moments(populations, discs):
    fans, slab_len, band_width, height = discs.shape
    vmem = pl.BlockSpec(memory_space=pltpu.VMEM)
    return pl.pallas_call(
        lambda populations_ref, discs_ref, velocity_ref, flow_ref: moments_into(
            populations_ref, discs_ref, 0, velocity_ref, flow_ref
        ),
        out_shape=(
            jax.ShapeDtypeStruct((3, slab_len, band_width, height), jnp.float32),
            jax.ShapeDtypeStruct((fans, band_width, height), jnp.float32),
        ),
        in_specs=[vmem, vmem],
        out_specs=(vmem, vmem),
        cost_estimate=pl.CostEstimate(
            flops=60 * discs[0].size, transcendentals=0, bytes_accessed=4 * populations.size
        ),
    )(populations, discs)


def lattice_step(strength, extended, discs, solid_rim, with_moments):
    slab_len = extended.shape[1] - 2
    band_width = extended.shape[2] - 2
    height = extended.shape[3]
    fans = discs.shape[0]
    out_shape = [jax.ShapeDtypeStruct((19, slab_len, band_width, height), jnp.float32)]
    if with_moments:
        out_shape.append(jax.ShapeDtypeStruct((3, slab_len, band_width, height), jnp.float32))
        out_shape.append(jax.ShapeDtypeStruct((fans, band_width, height), jnp.float32))
    vmem = pl.BlockSpec(memory_space=pltpu.VMEM)
    return pl.pallas_call(
        functools.partial(step_kernel, with_moments),
        out_shape=tuple(out_shape),
        in_specs=[pl.BlockSpec(memory_space=pltpu.SMEM), vmem, vmem, vmem],
        out_specs=tuple([vmem] * len(out_shape)),
        scratch_shapes=[pltpu.VMEM(extended.shape, jnp.float32)],
        cost_estimate=pl.CostEstimate(
            flops=300 * solid_rim.size, transcendentals=0, bytes_accessed=12 * extended.size
        ),
    )(strength, extended, discs, solid_rim)


def disc_count():
    inside = 0
    for offset_a in range(-RAD, RAD + 1):
        for offset_b in range(-RAD, RAD + 1):
            if offset_a * offset_a + offset_b * offset_b <= RAD * RAD:
                inside = inside + 1
    return FAN_LEN * inside


def fan_discs(fan_hubs, coord_x, coord_y, coord_z, length_total):
    discs = []
    for fan_number in range(fan_hubs.shape[0]):
        offset_x = jnp.mod(coord_x - fan_hubs[fan_number, 0], length_total)
        offset_y = coord_y - fan_hubs[fan_number, 1]
        offset_z = coord_z - fan_hubs[fan_number, 2]
        discs.append(
            (offset_x < FAN_LEN) & (offset_y * offset_y + offset_z * offset_z <= RAD * RAD)
        )
    return discs


def partial_flow(discs, velocity, solid_flag):
    return jnp.stack(
        [
            jnp.sum(jnp.where(disc_nodes & jnp.logical_not(solid_flag), velocity[0], 0.0))
            for disc_nodes in discs
        ]
    )


def force_from(discs, totals, fan_gain, jet_speed):
    strength = fan_gain * (jet_speed - totals / float(disc_count()))
    force_field = jnp.zeros(discs[0].shape, jnp.float32)
    for fan_number in range(len(discs)):
        force_field = force_field + jnp.where(discs[fan_number], strength[fan_number], 0.0)
    return force_field


def advance(center, ahead_x, behind_x, ahead_y, behind_y, ahead_z, behind_z, velocity, solid_flag):
    laplace = ahead_x + behind_x + ahead_y + behind_y + ahead_z + behind_z - 6.0 * center
    advect = 0.5 * (
        velocity[0] * (ahead_x - behind_x)
        + velocity[1] * (ahead_y - behind_y)
        + velocity[2] * (ahead_z - behind_z)
    )
    return jnp.where(solid_flag, 0.0, center + DIFFUSIVITY * laplace - advect)


def shift_height(field, shift_z):
    if shift_z == 0:
        return field
    zero_layer = jnp.zeros(field.shape[:-1] + (1,), field.dtype)
    if shift_z == 1:
        return jnp.concatenate([zero_layer, field[..., :-1]], axis=-1)
    return jnp.concatenate([field[..., 1:], zero_layer], axis=-1)


def rim_round(populations, smoke, flow, axis, dim, reach):
    count = lax.axis_size(axis)
    fans = flow.shape[0]

    def piece(start):
        cells = lax.slice_in_dim(populations, start, start + 1, axis=dim)
        fumes = lax.slice_in_dim(smoke, start, start + 1, axis=dim - 1)[None]
        carrier = jnp.zeros(cells.shape[1:], jnp.float32).at[0, 0, :fans].set(flow)[None]
        return jnp.concatenate([cells, fumes, carrier], axis=0)

    head = piece(0)
    tail = piece(populations.shape[dim] - 1)
    forward = [(i, (i + 1) % count) for i in range(count)]
    backward = [((i + 1) % count, i) for i in range(count)]
    if count == 2:
        both = lax.ppermute(jnp.concatenate([tail, head], axis=0), axis, forward)
        from_left = both[: tail.shape[0]]
        from_right = both[tail.shape[0] :]
        total = flow + from_left[-1, 0, 0, :fans]
    else:
        from_left = lax.ppermute(tail, axis, forward)
        from_right = lax.ppermute(head, axis, backward)
        total = flow + from_left[-1, 0, 0, :fans] + from_right[-1, 0, 0, :fans]
    for offset in sorted(set(step % count for step in range(-reach, reach + 1)) - {0, 1, count - 1}):
        total = total + lax.ppermute(flow, axis, [(i, (i + offset) % count) for i in range(count)])
    populations = jnp.concatenate([from_left[:19], populations, from_right[:19]], axis=dim)
    smoke = jnp.concatenate([from_left[19], smoke, from_right[19]], axis=dim - 1)
    return (populations, smoke, total)


def window_sum(values, axis, width):
    count = lax.axis_size(axis)
    total = values
    for offset in sorted(set(step % count for step in range(-width, width + 1)) - {0}):
        total = total + lax.ppermute(
            values, axis, [(i, (i + offset) % count) for i in range(count)]
        )
    return total


def source_release(sources, source_rate, offset_len, offset_band, slab_len, band_width, height):
    local_x = sources[:, 0] - offset_len
    local_y = sources[:, 1] - offset_band
    pick_x = (local_x[:, None] == jnp.arange(slab_len, dtype=jnp.int32)[None, :]).astype(
        jnp.float32
    )
    pick_y = (local_y[:, None] == jnp.arange(band_width, dtype=jnp.int32)[None, :]).astype(
        jnp.float32
    )
    pick_z = (sources[:, 2][:, None] == jnp.arange(height, dtype=jnp.int32)[None, :]).astype(
        jnp.float32
    )
    weighted = source_rate[:, None] * pick_x
    cross_table = (pick_y[:, :, None] * pick_z[:, None, :]).reshape(
        sources.shape[0], band_width * height
    )
    released = jnp.dot(
        weighted.T, cross_table, precision=lax.Precision.HIGHEST, preferred_element_type=jnp.float32
    )
    return released.reshape(slab_len, band_width, height)


def body(populations, solid_mask, smoke_field, fan_hubs, fan_gain, jet_speed, sources, source_rate):
    slab_len = populations.shape[1]
    band_width = populations.shape[2]
    height = populations.shape[3]
    offset_len = lax.axis_index("len") * slab_len
    offset_band = lax.axis_index("band") * band_width
    length_total = slab_len * lax.axis_size("len")
    breadth_total = band_width * lax.axis_size("band")
    solid_flag = solid_mask == 1
    solid_rim = extended_2(solid_flag.astype(jnp.float32), (("len", 0), ("band", 1)), 1)
    coord_x = offset_len - 1 + jnp.arange(slab_len + 2, dtype=jnp.int32)[:, None, None]
    coord_y = jnp.mod(
        offset_band - 1 + jnp.arange(band_width + 2, dtype=jnp.int32)[None, :, None], breadth_total
    )
    coord_z = jnp.arange(height, dtype=jnp.int32)[None, None, :]
    air_rim = solid_rim == 0.0
    discs = jnp.stack(
        [
            (disc_nodes & air_rim).astype(jnp.float32)
            for disc_nodes in fan_discs(fan_hubs, coord_x, coord_y, coord_z, length_total)
        ]
    )
    released = source_release(
        sources, source_rate, offset_len, offset_band, slab_len, band_width, height
    )
    len_reach = max(-(-FAN_LEN // slab_len), (slab_len + FAN_LEN - 1) // slab_len)
    band_reach = max(-(-(2 * RAD + 1) // band_width), (band_width + 2 * RAD) // band_width)
    inner_x = offset_len + jnp.arange(slab_len, dtype=jnp.int32)[:, None, None]
    inner_y = offset_band + jnp.arange(band_width, dtype=jnp.int32)[None, :, None]
    air = jnp.logical_not(solid_flag)
    inner_discs = jnp.stack(
        [
            (disc_nodes & air).astype(jnp.float32)
            for disc_nodes in fan_discs(fan_hubs, inner_x, inner_y, coord_z, length_total)
        ]
    )
    velocity, flow = first_moments(populations, inner_discs)
    partials = jnp.sum(flow, axis=(1, 2))
    for repeat in range(ITERS):
        extended, rimmed, totals = rim_round(populations, smoke_field, partials, "len", 1, len_reach)
        extended, rimmed, totals = rim_round(extended, rimmed, totals, "band", 2, band_reach)
        strength = fan_gain * (jet_speed - totals / float(disc_count()))
        last = repeat == ITERS - 1
        stepped = lattice_step(strength, extended, discs, solid_rim, not last)
        ahead_x = rimmed[2:, 1:-1]
        behind_x = rimmed[:-2, 1:-1]
        ahead_y = rimmed[1:-1, 2:]
        behind_y = rimmed[1:-1, :-2]
        smoke_field = advance(
            smoke_field,
            ahead_x,
            behind_x,
            ahead_y,
            behind_y,
            shift_height(smoke_field, -1),
            shift_height(smoke_field, 1),
            velocity,
            solid_flag,
        )
        smoke_field = smoke_field + released
        populations = stepped[0]
        if not last:
            velocity = stepped[1]
            partials = jnp.sum(stepped[2], axis=(1, 2))
    return (populations, smoke_field)


def solution(mesh):
    placed = (
        P(None, "len", "band", None),
        P("len", "band", None),
        P("len", "band", None),
        P(),
        P(),
        P(),
        P(),
        P(),
    )
    return jax.shard_map(
        body,
        mesh=mesh,
        in_specs=placed,
        out_specs=(P(None, "len", "band", None), P("len", "band", None)),
        check_vma=False,
    )
```

```python
import functools

import jax
import jax.numpy as jnp
from jax import lax
from jax.experimental import pallas as pl
from jax.experimental.pallas import tpu as pltpu
from jax.sharding import PartitionSpec as P

RAD = 3
FAN_LEN = 16
ITERS = 3


VELOCITIES = (
    (0, 0, 0),
    (1, 0, 0),
    (-1, 0, 0),
    (0, 1, 0),
    (0, -1, 0),
    (0, 0, 1),
    (0, 0, -1),
    (1, 1, 0),
    (-1, -1, 0),
    (1, -1, 0),
    (-1, 1, 0),
    (1, 0, 1),
    (-1, 0, -1),
    (1, 0, -1),
    (-1, 0, 1),
    (0, 1, 1),
    (0, -1, -1),
    (0, 1, -1),
    (0, -1, 1),
)
WEIGHTS = (1.0 / 3.0,) + (1.0 / 18.0,) * 6 + (1.0 / 36.0,) * 12
OPPOSITE = (0, 2, 1, 4, 3, 6, 5, 8, 7, 10, 9, 12, 11, 14, 13, 16, 15, 18, 17)
RELAX_RATE = 1.0 / 0.6
DIFFUSIVITY = 0.12


def extended_2(cells, sides, width):
    for axis, dim in sides:
        count = lax.axis_size(axis)
        head = lax.slice_in_dim(cells, 0, width, axis=dim)
        tail = lax.slice_in_dim(cells, cells.shape[dim] - width, cells.shape[dim], axis=dim)
        cells = jnp.concatenate(
            [
                lax.ppermute(tail, axis, [(i, (i + 1) % count) for i in range(count)]),
                cells,
                lax.ppermute(head, axis, [((i + 1) % count, i) for i in range(count)]),
            ],
            axis=dim,
        )
    return cells


def moments(populations):
    density = jnp.sum(populations, axis=0)
    velocity = []
    for dimension in range(3):
        forward = [populations[which] for which in range(19) if VELOCITIES[which][dimension] == 1]
        backward = [populations[which] for which in range(19) if VELOCITIES[which][dimension] == -1]
        velocity.append((sum(forward) - sum(backward)) / density)
    return (density, velocity)


def plane_moments(populations):
    density = sum(populations[1:], populations[0])
    velocity = []
    for dimension in range(3):
        forward = [populations[which] for which in range(19) if VELOCITIES[which][dimension] == 1]
        backward = [populations[which] for which in range(19) if VELOCITIES[which][dimension] == -1]
        velocity.append((sum(forward) - sum(backward)) / density)
    return (density, velocity)


def step_kernel(with_moments, strength_ref, populations_ref, discs_ref, solid_ref, *rest):
    if with_moments:
        out_ref, velocity_ref, flow_ref, posts_ref = rest
    else:
        out_ref, posts_ref = rest
    fans = discs_ref.shape[0]
    slab_len, band_width, height = out_ref.shape[1:]

    def collide_plane(index, carry):
        populations = [populations_ref[which, index] for which in range(19)]
        density, velocity = plane_moments(populations)
        force_field = strength_ref[0] * discs_ref[0, index]
        for fan_number in range(1, fans):
            force_field = force_field + strength_ref[fan_number] * discs_ref[fan_number, index]
        solid_flag = solid_ref[index] != 0.0
        speed_sq = velocity[0] * velocity[0] + velocity[1] * velocity[1] + velocity[2] * velocity[2]
        for which in range(19):
            shift_x, shift_y, shift_z = VELOCITIES[which]
            along = shift_x * velocity[0] + shift_y * velocity[1] + shift_z * velocity[2]
            balance = (
                WEIGHTS[which] * density * (1.0 + 3.0 * along + 4.5 * along * along - 1.5 * speed_sq)
            )
            relaxed = populations[which] - RELAX_RATE * (populations[which] - balance)
            if shift_x != 0:
                relaxed = relaxed + 3.0 * WEIGHTS[which] * shift_x * force_field
            posts_ref[which, index] = jnp.where(solid_flag, populations[OPPOSITE[which]], relaxed)
        return carry

    lax.fori_loop(0, populations_ref.shape[1], collide_plane, 0)
    lane = lax.broadcasted_iota(jnp.int32, (slab_len, band_width, height), 2)
    for which in range(19):
        shift_x, shift_y, shift_z = VELOCITIES[which]
        piece = posts_ref[
            which, 1 - shift_x : 1 - shift_x + slab_len, 1 - shift_y : 1 - shift_y + band_width, :
        ]
        if shift_z == 1:
            piece = jnp.where(lane == 0, 0.0, pltpu.roll(piece, 1, 2))
        elif shift_z == -1:
            piece = jnp.where(lane == height - 1, 0.0, pltpu.roll(piece, height - 1, 2))
        out_ref[which] = piece
    if not with_moments:
        return
    moments_into(out_ref, discs_ref, 1, velocity_ref, flow_ref)


def moments_into(populations_ref, discs_ref, rim, velocity_ref, flow_ref):
    fans = discs_ref.shape[0]
    band_width = populations_ref.shape[2]
    flow_ref[...] = jnp.zeros(flow_ref.shape, jnp.float32)

    def moment_plane(index, carry):
        density, velocity = plane_moments([populations_ref[which, index] for which in range(19)])
        for dimension in range(3):
            velocity_ref[dimension, index] = velocity[dimension]
        for fan_number in range(fans):
            flow_ref[fan_number] += (
                discs_ref[fan_number, index + rim, rim : rim + band_width, :] * velocity[0]
            )
        return carry

    lax.fori_loop(0, populations_ref.shape[1], moment_plane, 0)


def first_moments(populations, discs):
    fans, slab_len, band_width, height = discs.shape
    vmem = pl.BlockSpec(memory_space=pltpu.VMEM)
    return pl.pallas_call(
        lambda populations_ref, discs_ref, velocity_ref, flow_ref: moments_into(
            populations_ref, discs_ref, 0, velocity_ref, flow_ref
        ),
        out_shape=(
            jax.ShapeDtypeStruct((3, slab_len, band_width, height), jnp.float32),
            jax.ShapeDtypeStruct((fans, band_width, height), jnp.float32),
        ),
        in_specs=[vmem, vmem],
        out_specs=(vmem, vmem),
        cost_estimate=pl.CostEstimate(
            flops=60 * discs[0].size, transcendentals=0, bytes_accessed=4 * populations.size
        ),
    )(populations, discs)


def lattice_step(strength, extended, discs, solid_rim, with_moments):
    slab_len = extended.shape[1] - 2
    band_width = extended.shape[2] - 2
    height = extended.shape[3]
    fans = discs.shape[0]
    out_shape = [jax.ShapeDtypeStruct((19, slab_len, band_width, height), jnp.float32)]
    if with_moments:
        out_shape.append(jax.ShapeDtypeStruct((3, slab_len, band_width, height), jnp.float32))
        out_shape.append(jax.ShapeDtypeStruct((fans, band_width, height), jnp.float32))
    vmem = pl.BlockSpec(memory_space=pltpu.VMEM)
    return pl.pallas_call(
        functools.partial(step_kernel, with_moments),
        out_shape=tuple(out_shape),
        in_specs=[pl.BlockSpec(memory_space=pltpu.SMEM), vmem, vmem, vmem],
        out_specs=tuple([vmem] * len(out_shape)),
        scratch_shapes=[pltpu.VMEM(extended.shape, jnp.float32)],
        cost_estimate=pl.CostEstimate(
            flops=300 * solid_rim.size, transcendentals=0, bytes_accessed=12 * extended.size
        ),
    )(strength, extended, discs, solid_rim)


def disc_count():
    inside = 0
    for offset_a in range(-RAD, RAD + 1):
        for offset_b in range(-RAD, RAD + 1):
            if offset_a * offset_a + offset_b * offset_b <= RAD * RAD:
                inside = inside + 1
    return FAN_LEN * inside


def fan_discs(fan_hubs, coord_x, coord_y, coord_z, length_total):
    discs = []
    for fan_number in range(fan_hubs.shape[0]):
        offset_x = jnp.mod(coord_x - fan_hubs[fan_number, 0], length_total)
        offset_y = coord_y - fan_hubs[fan_number, 1]
        offset_z = coord_z - fan_hubs[fan_number, 2]
        discs.append(
            (offset_x < FAN_LEN) & (offset_y * offset_y + offset_z * offset_z <= RAD * RAD)
        )
    return discs


def partial_flow(discs, velocity, solid_flag):
    return jnp.stack(
        [
            jnp.sum(jnp.where(disc_nodes & jnp.logical_not(solid_flag), velocity[0], 0.0))
            for disc_nodes in discs
        ]
    )


def force_from(discs, totals, fan_gain, jet_speed):
    strength = fan_gain * (jet_speed - totals / float(disc_count()))
    force_field = jnp.zeros(discs[0].shape, jnp.float32)
    for fan_number in range(len(discs)):
        force_field = force_field + jnp.where(discs[fan_number], strength[fan_number], 0.0)
    return force_field


def advance(center, ahead_x, behind_x, ahead_y, behind_y, ahead_z, behind_z, velocity, solid_flag):
    laplace = ahead_x + behind_x + ahead_y + behind_y + ahead_z + behind_z - 6.0 * center
    advect = 0.5 * (
        velocity[0] * (ahead_x - behind_x)
        + velocity[1] * (ahead_y - behind_y)
        + velocity[2] * (ahead_z - behind_z)
    )
    return jnp.where(solid_flag, 0.0, center + DIFFUSIVITY * laplace - advect)


def shift_height(field, shift_z):
    if shift_z == 0:
        return field
    zero_layer = jnp.zeros(field.shape[:-1] + (1,), field.dtype)
    if shift_z == 1:
        return jnp.concatenate([zero_layer, field[..., :-1]], axis=-1)
    return jnp.concatenate([field[..., 1:], zero_layer], axis=-1)


def rim_round(populations, smoke, flow, axis, dim, reach):
    count = lax.axis_size(axis)
    fans = flow.shape[0]

    def piece(start):
        cells = lax.slice_in_dim(populations, start, start + 1, axis=dim)
        fumes = lax.slice_in_dim(smoke, start, start + 1, axis=dim - 1)[None]
        carrier = jnp.zeros(cells.shape[1:], jnp.float32).at[0, 0, :fans].set(flow)[None]
        return jnp.concatenate([cells, fumes, carrier], axis=0)

    head = piece(0)
    tail = piece(populations.shape[dim] - 1)
    forward = [(i, (i + 1) % count) for i in range(count)]
    backward = [((i + 1) % count, i) for i in range(count)]
    if count == 2:
        both = lax.ppermute(jnp.concatenate([tail, head], axis=0), axis, forward)
        from_left = both[: tail.shape[0]]
        from_right = both[tail.shape[0] :]
        total = flow + from_left[-1, 0, 0, :fans]
    else:
        from_left = lax.ppermute(tail, axis, forward)
        from_right = lax.ppermute(head, axis, backward)
        total = flow + from_left[-1, 0, 0, :fans] + from_right[-1, 0, 0, :fans]
    for offset in sorted(set(step % count for step in range(-reach, reach + 1)) - {0, 1, count - 1}):
        total = total + lax.ppermute(flow, axis, [(i, (i + offset) % count) for i in range(count)])
    populations = jnp.concatenate([from_left[:19], populations, from_right[:19]], axis=dim)
    smoke = jnp.concatenate([from_left[19], smoke, from_right[19]], axis=dim - 1)
    return (populations, smoke, total)


def window_sum(values, axis, width):
    count = lax.axis_size(axis)
    total = values
    for offset in sorted(set(step % count for step in range(-width, width + 1)) - {0}):
        total = total + lax.ppermute(
            values, axis, [(i, (i + offset) % count) for i in range(count)]
        )
    return total


def source_release(sources, source_rate, offset_len, offset_band, slab_len, band_width, height):
    local_x = sources[:, 0] - offset_len
    local_y = sources[:, 1] - offset_band
    pick_x = (local_x[:, None] == jnp.arange(slab_len, dtype=jnp.int32)[None, :]).astype(
        jnp.float32
    )
    pick_y = (local_y[:, None] == jnp.arange(band_width, dtype=jnp.int32)[None, :]).astype(
        jnp.float32
    )
    pick_z = (sources[:, 2][:, None] == jnp.arange(height, dtype=jnp.int32)[None, :]).astype(
        jnp.float32
    )
    weighted = source_rate[:, None] * pick_x
    cross_table = (pick_y[:, :, None] * pick_z[:, None, :]).reshape(
        sources.shape[0], band_width * height
    )
    released = jnp.dot(
        weighted.T, cross_table, precision=lax.Precision.HIGHEST, preferred_element_type=jnp.float32
    )
    return released.reshape(slab_len, band_width, height)


def body(populations, solid_mask, smoke_field, fan_hubs, fan_gain, jet_speed, sources, source_rate):
    slab_len = populations.shape[1]
    band_width = populations.shape[2]
    height = populations.shape[3]
    offset_len = lax.axis_index("len") * slab_len
    offset_band = lax.axis_index("band") * band_width
    length_total = slab_len * lax.axis_size("len")
    breadth_total = band_width * lax.axis_size("band")
    solid_flag = solid_mask == 1
    solid_rim = extended_2(solid_flag.astype(jnp.float32), (("len", 0), ("band", 1)), 1)
    coord_x = offset_len - 1 + jnp.arange(slab_len + 2, dtype=jnp.int32)
    coord_y = jnp.mod(offset_band - 1 + jnp.arange(band_width + 2, dtype=jnp.int32), breadth_total)
    coord_z = jnp.arange(height, dtype=jnp.int32)
    along_in = jnp.mod(coord_x[None, :] - fan_hubs[:, 0:1], length_total) < FAN_LEN
    offset_y = coord_y[None, :] - fan_hubs[:, 1:2]
    offset_z = coord_z[None, :] - fan_hubs[:, 2:3]
    across_in = (
        offset_y[:, :, None] * offset_y[:, :, None] + offset_z[:, None, :] * offset_z[:, None, :]
        <= RAD * RAD
    )
    air_rim = solid_rim == 0.0
    discs = (along_in[:, :, None, None] & across_in[:, None] & air_rim[None]).astype(jnp.float32)
    released = source_release(
        sources, source_rate, offset_len, offset_band, slab_len, band_width, height
    )
    len_reach = max(-(-FAN_LEN // slab_len), (slab_len + FAN_LEN - 1) // slab_len)
    band_reach = max(-(-(2 * RAD + 1) // band_width), (band_width + 2 * RAD) // band_width)
    inner_discs = (
        along_in[:, 1:-1, None, None]
        & across_in[:, None, 1:-1]
        & jnp.logical_not(solid_flag)[None]
    ).astype(jnp.float32)
    velocity, flow = first_moments(populations, inner_discs)
    partials = jnp.sum(flow, axis=(1, 2))
    for repeat in range(ITERS):
        extended, rimmed, totals = rim_round(populations, smoke_field, partials, "len", 1, len_reach)
        extended, rimmed, totals = rim_round(extended, rimmed, totals, "band", 2, band_reach)
        strength = fan_gain * (jet_speed - totals / float(disc_count()))
        last = repeat == ITERS - 1
        stepped = lattice_step(strength, extended, discs, solid_rim, not last)
        ahead_x = rimmed[2:, 1:-1]
        behind_x = rimmed[:-2, 1:-1]
        ahead_y = rimmed[1:-1, 2:]
        behind_y = rimmed[1:-1, :-2]
        smoke_field = advance(
            smoke_field,
            ahead_x,
            behind_x,
            ahead_y,
            behind_y,
            shift_height(smoke_field, -1),
            shift_height(smoke_field, 1),
            velocity,
            solid_flag,
        )
        smoke_field = smoke_field + released
        populations = stepped[0]
        if not last:
            velocity = stepped[1]
            partials = jnp.sum(stepped[2], axis=(1, 2))
    return (populations, smoke_field)


def solution(mesh):
    placed = (
        P(None, "len", "band", None),
        P("len", "band", None),
        P("len", "band", None),
        P(),
        P(),
        P(),
        P(),
        P(),
    )
    return jax.shard_map(
        body,
        mesh=mesh,
        in_specs=placed,
        out_specs=(P(None, "len", "band", None), P("len", "band", None)),
        check_vma=False,
    )
```

```python
import functools

import jax
import jax.numpy as jnp
from jax import lax
from jax.experimental import pallas as pl
from jax.experimental.pallas import tpu as pltpu
from jax.sharding import PartitionSpec as P

RAD = 3
FAN_LEN = 16
ITERS = 3


VELOCITIES = (
    (0, 0, 0),
    (1, 0, 0),
    (-1, 0, 0),
    (0, 1, 0),
    (0, -1, 0),
    (0, 0, 1),
    (0, 0, -1),
    (1, 1, 0),
    (-1, -1, 0),
    (1, -1, 0),
    (-1, 1, 0),
    (1, 0, 1),
    (-1, 0, -1),
    (1, 0, -1),
    (-1, 0, 1),
    (0, 1, 1),
    (0, -1, -1),
    (0, 1, -1),
    (0, -1, 1),
)
WEIGHTS = (1.0 / 3.0,) + (1.0 / 18.0,) * 6 + (1.0 / 36.0,) * 12
OPPOSITE = (0, 2, 1, 4, 3, 6, 5, 8, 7, 10, 9, 12, 11, 14, 13, 16, 15, 18, 17)
RELAX_RATE = 1.0 / 0.6
DIFFUSIVITY = 0.12


def extended_2(cells, sides, width):
    for axis, dim in sides:
        count = lax.axis_size(axis)
        head = lax.slice_in_dim(cells, 0, width, axis=dim)
        tail = lax.slice_in_dim(cells, cells.shape[dim] - width, cells.shape[dim], axis=dim)
        cells = jnp.concatenate(
            [
                lax.ppermute(tail, axis, [(i, (i + 1) % count) for i in range(count)]),
                cells,
                lax.ppermute(head, axis, [((i + 1) % count, i) for i in range(count)]),
            ],
            axis=dim,
        )
    return cells


def moments(populations):
    density = jnp.sum(populations, axis=0)
    velocity = []
    for dimension in range(3):
        forward = [populations[which] for which in range(19) if VELOCITIES[which][dimension] == 1]
        backward = [populations[which] for which in range(19) if VELOCITIES[which][dimension] == -1]
        velocity.append((sum(forward) - sum(backward)) / density)
    return (density, velocity)


def plane_moments(populations):
    density = sum(populations[1:], populations[0])
    velocity = []
    for dimension in range(3):
        forward = [populations[which] for which in range(19) if VELOCITIES[which][dimension] == 1]
        backward = [populations[which] for which in range(19) if VELOCITIES[which][dimension] == -1]
        velocity.append((sum(forward) - sum(backward)) / density)
    return (density, velocity)


def step_kernel(with_moments, strength_ref, populations_ref, discs_ref, solid_ref, *rest):
    if with_moments:
        out_ref, velocity_ref, flow_ref, posts_ref = rest
    else:
        out_ref, posts_ref = rest
    fans = discs_ref.shape[0]
    slab_len, band_width, height = out_ref.shape[1:]

    def collide_plane(index, carry):
        populations = [populations_ref[which, index] for which in range(19)]
        density, velocity = plane_moments(populations)
        force_field = strength_ref[0] * discs_ref[0, index]
        for fan_number in range(1, fans):
            force_field = force_field + strength_ref[fan_number] * discs_ref[fan_number, index]
        solid_flag = solid_ref[index] != 0.0
        speed_sq = velocity[0] * velocity[0] + velocity[1] * velocity[1] + velocity[2] * velocity[2]
        for which in range(19):
            shift_x, shift_y, shift_z = VELOCITIES[which]
            along = shift_x * velocity[0] + shift_y * velocity[1] + shift_z * velocity[2]
            balance = (
                WEIGHTS[which] * density * (1.0 + 3.0 * along + 4.5 * along * along - 1.5 * speed_sq)
            )
            relaxed = populations[which] - RELAX_RATE * (populations[which] - balance)
            if shift_x != 0:
                relaxed = relaxed + 3.0 * WEIGHTS[which] * shift_x * force_field
            posts_ref[which, index] = jnp.where(solid_flag, populations[OPPOSITE[which]], relaxed)
        return carry

    lax.fori_loop(0, populations_ref.shape[1], collide_plane, 0)
    lane = lax.broadcasted_iota(jnp.int32, (slab_len, band_width, height), 2)
    for which in range(19):
        shift_x, shift_y, shift_z = VELOCITIES[which]
        piece = posts_ref[
            which, 1 - shift_x : 1 - shift_x + slab_len, 1 - shift_y : 1 - shift_y + band_width, :
        ]
        if shift_z == 1:
            piece = jnp.where(lane == 0, 0.0, pltpu.roll(piece, 1, 2))
        elif shift_z == -1:
            piece = jnp.where(lane == height - 1, 0.0, pltpu.roll(piece, height - 1, 2))
        out_ref[which] = piece
    if not with_moments:
        return
    moments_into(out_ref, discs_ref, 1, velocity_ref, flow_ref)


def moments_into(populations_ref, discs_ref, rim, velocity_ref, flow_ref):
    fans = discs_ref.shape[0]
    band_width = populations_ref.shape[2]
    flow_ref[...] = jnp.zeros(flow_ref.shape, jnp.float32)

    def moment_plane(index, carry):
        density, velocity = plane_moments([populations_ref[which, index] for which in range(19)])
        for dimension in range(3):
            velocity_ref[dimension, index] = velocity[dimension]
        for fan_number in range(fans):
            flow_ref[fan_number] += (
                discs_ref[fan_number, index + rim, rim : rim + band_width, :] * velocity[0]
            )
        return carry

    lax.fori_loop(0, populations_ref.shape[1], moment_plane, 0)


def first_moments(populations, discs):
    fans, slab_len, band_width, height = discs.shape
    vmem = pl.BlockSpec(memory_space=pltpu.VMEM)
    return pl.pallas_call(
        lambda populations_ref, discs_ref, velocity_ref, flow_ref: moments_into(
            populations_ref, discs_ref, 0, velocity_ref, flow_ref
        ),
        out_shape=(
            jax.ShapeDtypeStruct((3, slab_len, band_width, height), jnp.float32),
            jax.ShapeDtypeStruct((fans, band_width, height), jnp.float32),
        ),
        in_specs=[vmem, vmem],
        out_specs=(vmem, vmem),
        cost_estimate=pl.CostEstimate(
            flops=60 * discs[0].size, transcendentals=0, bytes_accessed=4 * populations.size
        ),
    )(populations, discs)


def lattice_step(strength, extended, discs, solid_rim, with_moments):
    slab_len = extended.shape[1] - 2
    band_width = extended.shape[2] - 2
    height = extended.shape[3]
    fans = discs.shape[0]
    out_shape = [jax.ShapeDtypeStruct((19, slab_len, band_width, height), jnp.float32)]
    if with_moments:
        out_shape.append(jax.ShapeDtypeStruct((3, slab_len, band_width, height), jnp.float32))
        out_shape.append(jax.ShapeDtypeStruct((fans, band_width, height), jnp.float32))
    vmem = pl.BlockSpec(memory_space=pltpu.VMEM)
    return pl.pallas_call(
        functools.partial(step_kernel, with_moments),
        out_shape=tuple(out_shape),
        in_specs=[pl.BlockSpec(memory_space=pltpu.SMEM), vmem, vmem, vmem],
        out_specs=tuple([vmem] * len(out_shape)),
        scratch_shapes=[pltpu.VMEM(extended.shape, jnp.float32)],
        cost_estimate=pl.CostEstimate(
            flops=300 * solid_rim.size, transcendentals=0, bytes_accessed=12 * extended.size
        ),
    )(strength, extended, discs, solid_rim)


def disc_count():
    inside = 0
    for offset_a in range(-RAD, RAD + 1):
        for offset_b in range(-RAD, RAD + 1):
            if offset_a * offset_a + offset_b * offset_b <= RAD * RAD:
                inside = inside + 1
    return FAN_LEN * inside


def fan_discs(fan_hubs, coord_x, coord_y, coord_z, length_total):
    discs = []
    for fan_number in range(fan_hubs.shape[0]):
        offset_x = jnp.mod(coord_x - fan_hubs[fan_number, 0], length_total)
        offset_y = coord_y - fan_hubs[fan_number, 1]
        offset_z = coord_z - fan_hubs[fan_number, 2]
        discs.append(
            (offset_x < FAN_LEN) & (offset_y * offset_y + offset_z * offset_z <= RAD * RAD)
        )
    return discs


def partial_flow(discs, velocity, solid_flag):
    return jnp.stack(
        [
            jnp.sum(jnp.where(disc_nodes & jnp.logical_not(solid_flag), velocity[0], 0.0))
            for disc_nodes in discs
        ]
    )


def force_from(discs, totals, fan_gain, jet_speed):
    strength = fan_gain * (jet_speed - totals / float(disc_count()))
    force_field = jnp.zeros(discs[0].shape, jnp.float32)
    for fan_number in range(len(discs)):
        force_field = force_field + jnp.where(discs[fan_number], strength[fan_number], 0.0)
    return force_field


def advance(center, ahead_x, behind_x, ahead_y, behind_y, ahead_z, behind_z, velocity, solid_flag):
    laplace = ahead_x + behind_x + ahead_y + behind_y + ahead_z + behind_z - 6.0 * center
    advect = 0.5 * (
        velocity[0] * (ahead_x - behind_x)
        + velocity[1] * (ahead_y - behind_y)
        + velocity[2] * (ahead_z - behind_z)
    )
    return jnp.where(solid_flag, 0.0, center + DIFFUSIVITY * laplace - advect)


def shift_height(field, shift_z):
    if shift_z == 0:
        return field
    zero_layer = jnp.zeros(field.shape[:-1] + (1,), field.dtype)
    if shift_z == 1:
        return jnp.concatenate([zero_layer, field[..., :-1]], axis=-1)
    return jnp.concatenate([field[..., 1:], zero_layer], axis=-1)


def rim_round(fields, flow, axis, dim, reach):
    count = lax.axis_size(axis)
    fans = flow.shape[0]
    channels = [field.shape[0] for field in fields]

    def piece(start):
        cells = [lax.slice_in_dim(field, start, start + 1, axis=dim) for field in fields]
        carrier = jnp.zeros(cells[0].shape[1:], jnp.float32).at[0, 0, :fans].set(flow)[None]
        return jnp.concatenate(cells + [carrier], axis=0)

    head = piece(0)
    tail = piece(fields[0].shape[dim] - 1)
    forward = [(i, (i + 1) % count) for i in range(count)]
    backward = [((i + 1) % count, i) for i in range(count)]
    if count == 2:
        both = lax.ppermute(jnp.concatenate([tail, head], axis=0), axis, forward)
        from_left = both[: tail.shape[0]]
        from_right = both[tail.shape[0] :]
        total = flow + from_left[-1, 0, 0, :fans]
    else:
        from_left = lax.ppermute(tail, axis, forward)
        from_right = lax.ppermute(head, axis, backward)
        total = flow + from_left[-1, 0, 0, :fans] + from_right[-1, 0, 0, :fans]
    for offset in sorted(set(step % count for step in range(-reach, reach + 1)) - {0, 1, count - 1}):
        total = total + lax.ppermute(flow, axis, [(i, (i + offset) % count) for i in range(count)])
    extended = []
    first = 0
    for field, channel in zip(fields, channels):
        extended.append(
            jnp.concatenate(
                [from_left[first : first + channel], field, from_right[first : first + channel]],
                axis=dim,
            )
        )
        first = first + channel
    return (extended, total)


def window_sum(values, axis, width):
    count = lax.axis_size(axis)
    total = values
    for offset in sorted(set(step % count for step in range(-width, width + 1)) - {0}):
        total = total + lax.ppermute(
            values, axis, [(i, (i + offset) % count) for i in range(count)]
        )
    return total


def source_release(sources, source_rate, offset_len, offset_band, slab_len, band_width, height):
    local_x = sources[:, 0] - offset_len
    local_y = sources[:, 1] - offset_band
    pick_x = (local_x[:, None] == jnp.arange(slab_len, dtype=jnp.int32)[None, :]).astype(
        jnp.float32
    )
    pick_y = (local_y[:, None] == jnp.arange(band_width, dtype=jnp.int32)[None, :]).astype(
        jnp.float32
    )
    pick_z = (sources[:, 2][:, None] == jnp.arange(height, dtype=jnp.int32)[None, :]).astype(
        jnp.float32
    )
    weighted = source_rate[:, None] * pick_x
    cross_table = (pick_y[:, :, None] * pick_z[:, None, :]).reshape(
        sources.shape[0], band_width * height
    )
    released = jnp.dot(
        weighted.T, cross_table, precision=lax.Precision.HIGHEST, preferred_element_type=jnp.float32
    )
    return released.reshape(slab_len, band_width, height)


def body(populations, solid_mask, smoke_field, fan_hubs, fan_gain, jet_speed, sources, source_rate):
    slab_len = populations.shape[1]
    band_width = populations.shape[2]
    height = populations.shape[3]
    offset_len = lax.axis_index("len") * slab_len
    offset_band = lax.axis_index("band") * band_width
    length_total = slab_len * lax.axis_size("len")
    breadth_total = band_width * lax.axis_size("band")
    solid_flag = solid_mask == 1
    coord_x = offset_len - 1 + jnp.arange(slab_len + 2, dtype=jnp.int32)
    coord_y = jnp.mod(offset_band - 1 + jnp.arange(band_width + 2, dtype=jnp.int32), breadth_total)
    coord_z = jnp.arange(height, dtype=jnp.int32)
    along_in = jnp.mod(coord_x[None, :] - fan_hubs[:, 0:1], length_total) < FAN_LEN
    offset_y = coord_y[None, :] - fan_hubs[:, 1:2]
    offset_z = coord_z[None, :] - fan_hubs[:, 2:3]
    across_in = (
        offset_y[:, :, None] * offset_y[:, :, None] + offset_z[:, None, :] * offset_z[:, None, :]
        <= RAD * RAD
    )
    released = source_release(
        sources, source_rate, offset_len, offset_band, slab_len, band_width, height
    )
    len_reach = max(-(-FAN_LEN // slab_len), (slab_len + FAN_LEN - 1) // slab_len)
    band_reach = max(-(-(2 * RAD + 1) // band_width), (band_width + 2 * RAD) // band_width)
    inner_discs = (
        along_in[:, 1:-1, None, None]
        & across_in[:, None, 1:-1]
        & jnp.logical_not(solid_flag)[None]
    ).astype(jnp.float32)
    velocity, flow = first_moments(populations, inner_discs)
    partials = jnp.sum(flow, axis=(1, 2))
    for repeat in range(ITERS):
        fields = [populations, smoke_field[None]]
        if repeat == 0:
            fields.append(solid_flag.astype(jnp.float32)[None])
        fields, totals = rim_round(fields, partials, "len", 1, len_reach)
        fields, totals = rim_round(fields, totals, "band", 2, band_reach)
        extended = fields[0]
        rimmed = fields[1][0]
        if repeat == 0:
            solid_rim = fields[2][0]
            air_rim = solid_rim == 0.0
            discs = (along_in[:, :, None, None] & across_in[:, None] & air_rim[None]).astype(
                jnp.float32
            )
        strength = fan_gain * (jet_speed - totals / float(disc_count()))
        last = repeat == ITERS - 1
        stepped = lattice_step(strength, extended, discs, solid_rim, not last)
        ahead_x = rimmed[2:, 1:-1]
        behind_x = rimmed[:-2, 1:-1]
        ahead_y = rimmed[1:-1, 2:]
        behind_y = rimmed[1:-1, :-2]
        smoke_field = advance(
            smoke_field,
            ahead_x,
            behind_x,
            ahead_y,
            behind_y,
            shift_height(smoke_field, -1),
            shift_height(smoke_field, 1),
            velocity,
            solid_flag,
        )
        smoke_field = smoke_field + released
        populations = stepped[0]
        if not last:
            velocity = stepped[1]
            partials = jnp.sum(stepped[2], axis=(1, 2))
    return (populations, smoke_field)


def solution(mesh):
    placed = (
        P(None, "len", "band", None),
        P("len", "band", None),
        P("len", "band", None),
        P(),
        P(),
        P(),
        P(),
        P(),
    )
    return jax.shard_map(
        body,
        mesh=mesh,
        in_specs=placed,
        out_specs=(P(None, "len", "band", None), P("len", "band", None)),
        check_vma=False,
    )
```

```python
import functools

import jax
import jax.numpy as jnp
from jax import lax
from jax.experimental import pallas as pl
from jax.experimental.pallas import tpu as pltpu
from jax.sharding import PartitionSpec as P

RAD = 3
FAN_LEN = 16
ITERS = 3


VELOCITIES = (
    (0, 0, 0),
    (1, 0, 0),
    (-1, 0, 0),
    (0, 1, 0),
    (0, -1, 0),
    (0, 0, 1),
    (0, 0, -1),
    (1, 1, 0),
    (-1, -1, 0),
    (1, -1, 0),
    (-1, 1, 0),
    (1, 0, 1),
    (-1, 0, -1),
    (1, 0, -1),
    (-1, 0, 1),
    (0, 1, 1),
    (0, -1, -1),
    (0, 1, -1),
    (0, -1, 1),
)
WEIGHTS = (1.0 / 3.0,) + (1.0 / 18.0,) * 6 + (1.0 / 36.0,) * 12
OPPOSITE = (0, 2, 1, 4, 3, 6, 5, 8, 7, 10, 9, 12, 11, 14, 13, 16, 15, 18, 17)
RELAX_RATE = 1.0 / 0.6
DIFFUSIVITY = 0.12


def extended_2(cells, sides, width):
    for axis, dim in sides:
        count = lax.axis_size(axis)
        head = lax.slice_in_dim(cells, 0, width, axis=dim)
        tail = lax.slice_in_dim(cells, cells.shape[dim] - width, cells.shape[dim], axis=dim)
        cells = jnp.concatenate(
            [
                lax.ppermute(tail, axis, [(i, (i + 1) % count) for i in range(count)]),
                cells,
                lax.ppermute(head, axis, [((i + 1) % count, i) for i in range(count)]),
            ],
            axis=dim,
        )
    return cells


def moments(populations):
    density = jnp.sum(populations, axis=0)
    velocity = []
    for dimension in range(3):
        forward = [populations[which] for which in range(19) if VELOCITIES[which][dimension] == 1]
        backward = [populations[which] for which in range(19) if VELOCITIES[which][dimension] == -1]
        velocity.append((sum(forward) - sum(backward)) / density)
    return (density, velocity)


def plane_moments(populations):
    density = sum(populations[1:], populations[0])
    velocity = []
    for dimension in range(3):
        forward = [populations[which] for which in range(19) if VELOCITIES[which][dimension] == 1]
        backward = [populations[which] for which in range(19) if VELOCITIES[which][dimension] == -1]
        velocity.append((sum(forward) - sum(backward)) / density)
    return (density, velocity)


def step_kernel(
    with_moments,
    strength_ref,
    populations_ref,
    discs_ref,
    solid_ref,
    smoke_ref,
    motion_ref,
    released_ref,
    *rest,
):
    if with_moments:
        out_ref, smoke_out_ref, velocity_ref, flow_ref, posts_ref, sums_ref = rest
    else:
        out_ref, smoke_out_ref, posts_ref = rest
    fans = discs_ref.shape[0]
    slab_len, band_width, height = out_ref.shape[1:]

    def collide_plane(index, carry):
        populations = [populations_ref[which, index] for which in range(19)]
        density, velocity = plane_moments(populations)
        force_field = strength_ref[0] * discs_ref[0, index]
        for fan_number in range(1, fans):
            force_field = force_field + strength_ref[fan_number] * discs_ref[fan_number, index]
        solid_flag = solid_ref[index] != 0.0
        speed_sq = velocity[0] * velocity[0] + velocity[1] * velocity[1] + velocity[2] * velocity[2]
        for which in range(19):
            shift_x, shift_y, shift_z = VELOCITIES[which]
            along = shift_x * velocity[0] + shift_y * velocity[1] + shift_z * velocity[2]
            balance = (
                WEIGHTS[which] * density * (1.0 + 3.0 * along + 4.5 * along * along - 1.5 * speed_sq)
            )
            relaxed = populations[which] - RELAX_RATE * (populations[which] - balance)
            if shift_x != 0:
                relaxed = relaxed + 3.0 * WEIGHTS[which] * shift_x * force_field
            posts_ref[which, index] = jnp.where(solid_flag, populations[OPPOSITE[which]], relaxed)
        return carry

    lax.fori_loop(0, populations_ref.shape[1], collide_plane, 0)
    lane_plane = lax.broadcasted_iota(jnp.int32, (band_width, height), 1)

    def smoke_plane(index, carry):
        center = smoke_ref[index + 1, 1 : 1 + band_width, :]
        ahead_x = smoke_ref[index + 2, 1 : 1 + band_width, :]
        behind_x = smoke_ref[index, 1 : 1 + band_width, :]
        ahead_y = smoke_ref[index + 1, 2 : 2 + band_width, :]
        behind_y = smoke_ref[index + 1, 0:band_width, :]
        ahead_z = jnp.where(lane_plane == height - 1, 0.0, pltpu.roll(center, height - 1, 1))
        behind_z = jnp.where(lane_plane == 0, 0.0, pltpu.roll(center, 1, 1))
        laplace = ahead_x + behind_x + ahead_y + behind_y + ahead_z + behind_z - 6.0 * center
        advect = 0.5 * (
            motion_ref[0, index] * (ahead_x - behind_x)
            + motion_ref[1, index] * (ahead_y - behind_y)
            + motion_ref[2, index] * (ahead_z - behind_z)
        )
        solid_flag = solid_ref[index + 1, 1 : 1 + band_width, :] != 0.0
        fresh = jnp.where(solid_flag, 0.0, center + DIFFUSIVITY * laplace - advect)
        smoke_out_ref[index] = fresh + released_ref[index]
        return carry

    lax.fori_loop(0, slab_len, smoke_plane, 0)
    lane = lax.broadcasted_iota(jnp.int32, (slab_len, band_width, height), 2)
    for which in range(19):
        shift_x, shift_y, shift_z = VELOCITIES[which]
        piece = posts_ref[
            which, 1 - shift_x : 1 - shift_x + slab_len, 1 - shift_y : 1 - shift_y + band_width, :
        ]
        if shift_z == 1:
            piece = jnp.where(lane == 0, 0.0, pltpu.roll(piece, 1, 2))
        elif shift_z == -1:
            piece = jnp.where(lane == height - 1, 0.0, pltpu.roll(piece, height - 1, 2))
        out_ref[which] = piece
    if with_moments:
        moments_into(out_ref, discs_ref, 1, velocity_ref, flow_ref, sums_ref)


def moments_into(populations_ref, discs_ref, rim, velocity_ref, flow_ref, sums_ref):
    fans = discs_ref.shape[0]
    band_width = populations_ref.shape[2]
    sums_ref[...] = jnp.zeros(sums_ref.shape, jnp.float32)

    def moment_plane(index, carry):
        density, velocity = plane_moments([populations_ref[which, index] for which in range(19)])
        for dimension in range(3):
            velocity_ref[dimension, index] = velocity[dimension]
        for fan_number in range(fans):
            sums_ref[fan_number] += (
                discs_ref[fan_number, index + rim, rim : rim + band_width, :] * velocity[0]
            )
        return carry

    lax.fori_loop(0, populations_ref.shape[1], moment_plane, 0)
    for fan_number in range(fans):
        flow_ref[fan_number : fan_number + 1, :] = jnp.sum(sums_ref[fan_number], axis=0, keepdims=True)


def first_moments(populations, discs):
    fans, slab_len, band_width, height = discs.shape
    vmem = pl.BlockSpec(memory_space=pltpu.VMEM)
    return pl.pallas_call(
        lambda populations_ref, discs_ref, velocity_ref, flow_ref, sums_ref: moments_into(
            populations_ref, discs_ref, 0, velocity_ref, flow_ref, sums_ref
        ),
        out_shape=(
            jax.ShapeDtypeStruct((3, slab_len, band_width, height), jnp.float32),
            jax.ShapeDtypeStruct((fans, height), jnp.float32),
        ),
        in_specs=[vmem, vmem],
        out_specs=(vmem, vmem),
        scratch_shapes=[pltpu.VMEM((fans, band_width, height), jnp.float32)],
        cost_estimate=pl.CostEstimate(
            flops=60 * discs[0].size, transcendentals=0, bytes_accessed=4 * populations.size
        ),
    )(populations, discs)


def lattice_step(strength, extended, discs, solid_rim, smoke_rim, velocity, released, with_moments):
    slab_len = extended.shape[1] - 2
    band_width = extended.shape[2] - 2
    height = extended.shape[3]
    fans = discs.shape[0]
    out_shape = [
        jax.ShapeDtypeStruct((19, slab_len, band_width, height), jnp.float32),
        jax.ShapeDtypeStruct((slab_len, band_width, height), jnp.float32),
    ]
    scratch = [pltpu.VMEM(extended.shape, jnp.float32)]
    if with_moments:
        out_shape.append(jax.ShapeDtypeStruct((3, slab_len, band_width, height), jnp.float32))
        out_shape.append(jax.ShapeDtypeStruct((fans, height), jnp.float32))
        scratch.append(pltpu.VMEM((fans, band_width, height), jnp.float32))
    vmem = pl.BlockSpec(memory_space=pltpu.VMEM)
    return pl.pallas_call(
        functools.partial(step_kernel, with_moments),
        out_shape=tuple(out_shape),
        in_specs=[pl.BlockSpec(memory_space=pltpu.SMEM)] + [vmem] * 6,
        out_specs=tuple([vmem] * len(out_shape)),
        scratch_shapes=scratch,
        cost_estimate=pl.CostEstimate(
            flops=300 * solid_rim.size, transcendentals=0, bytes_accessed=12 * extended.size
        ),
    )(strength, extended, discs, solid_rim, smoke_rim, velocity, released)


def disc_count():
    inside = 0
    for offset_a in range(-RAD, RAD + 1):
        for offset_b in range(-RAD, RAD + 1):
            if offset_a * offset_a + offset_b * offset_b <= RAD * RAD:
                inside = inside + 1
    return FAN_LEN * inside


def fan_discs(fan_hubs, coord_x, coord_y, coord_z, length_total):
    discs = []
    for fan_number in range(fan_hubs.shape[0]):
        offset_x = jnp.mod(coord_x - fan_hubs[fan_number, 0], length_total)
        offset_y = coord_y - fan_hubs[fan_number, 1]
        offset_z = coord_z - fan_hubs[fan_number, 2]
        discs.append(
            (offset_x < FAN_LEN) & (offset_y * offset_y + offset_z * offset_z <= RAD * RAD)
        )
    return discs


def partial_flow(discs, velocity, solid_flag):
    return jnp.stack(
        [
            jnp.sum(jnp.where(disc_nodes & jnp.logical_not(solid_flag), velocity[0], 0.0))
            for disc_nodes in discs
        ]
    )


def force_from(discs, totals, fan_gain, jet_speed):
    strength = fan_gain * (jet_speed - totals / float(disc_count()))
    force_field = jnp.zeros(discs[0].shape, jnp.float32)
    for fan_number in range(len(discs)):
        force_field = force_field + jnp.where(discs[fan_number], strength[fan_number], 0.0)
    return force_field


def advance(center, ahead_x, behind_x, ahead_y, behind_y, ahead_z, behind_z, velocity, solid_flag):
    laplace = ahead_x + behind_x + ahead_y + behind_y + ahead_z + behind_z - 6.0 * center
    advect = 0.5 * (
        velocity[0] * (ahead_x - behind_x)
        + velocity[1] * (ahead_y - behind_y)
        + velocity[2] * (ahead_z - behind_z)
    )
    return jnp.where(solid_flag, 0.0, center + DIFFUSIVITY * laplace - advect)


def shift_height(field, shift_z):
    if shift_z == 0:
        return field
    zero_layer = jnp.zeros(field.shape[:-1] + (1,), field.dtype)
    if shift_z == 1:
        return jnp.concatenate([zero_layer, field[..., :-1]], axis=-1)
    return jnp.concatenate([field[..., 1:], zero_layer], axis=-1)


def rim_round(fields, flow, axis, dim, reach):
    count = lax.axis_size(axis)
    fans = flow.shape[0]
    channels = [field.shape[0] for field in fields]

    def piece(start):
        cells = [lax.slice_in_dim(field, start, start + 1, axis=dim) for field in fields]
        carrier = jnp.zeros(cells[0].shape[1:], jnp.float32).at[0, 0, :fans].set(flow)[None]
        return jnp.concatenate(cells + [carrier], axis=0)

    head = piece(0)
    tail = piece(fields[0].shape[dim] - 1)
    forward = [(i, (i + 1) % count) for i in range(count)]
    backward = [((i + 1) % count, i) for i in range(count)]
    if count == 2:
        both = lax.ppermute(jnp.concatenate([tail, head], axis=0), axis, forward)
        from_left = both[: tail.shape[0]]
        from_right = both[tail.shape[0] :]
        total = flow + from_left[-1, 0, 0, :fans]
    else:
        from_left = lax.ppermute(tail, axis, forward)
        from_right = lax.ppermute(head, axis, backward)
        total = flow + from_left[-1, 0, 0, :fans] + from_right[-1, 0, 0, :fans]
    for offset in sorted(set(step % count for step in range(-reach, reach + 1)) - {0, 1, count - 1}):
        total = total + lax.ppermute(flow, axis, [(i, (i + offset) % count) for i in range(count)])
    extended = []
    first = 0
    for field, channel in zip(fields, channels):
        extended.append(
            jnp.concatenate(
                [from_left[first : first + channel], field, from_right[first : first + channel]],
                axis=dim,
            )
        )
        first = first + channel
    return (extended, total)


def window_sum(values, axis, width):
    count = lax.axis_size(axis)
    total = values
    for offset in sorted(set(step % count for step in range(-width, width + 1)) - {0}):
        total = total + lax.ppermute(
            values, axis, [(i, (i + offset) % count) for i in range(count)]
        )
    return total


def source_release(sources, source_rate, offset_len, offset_band, slab_len, band_width, height):
    local_x = sources[:, 0] - offset_len
    local_y = sources[:, 1] - offset_band
    pick_x = (local_x[:, None] == jnp.arange(slab_len, dtype=jnp.int32)[None, :]).astype(
        jnp.float32
    )
    pick_y = (local_y[:, None] == jnp.arange(band_width, dtype=jnp.int32)[None, :]).astype(
        jnp.float32
    )
    pick_z = (sources[:, 2][:, None] == jnp.arange(height, dtype=jnp.int32)[None, :]).astype(
        jnp.float32
    )
    weighted = source_rate[:, None] * pick_x
    cross_table = (pick_y[:, :, None] * pick_z[:, None, :]).reshape(
        sources.shape[0], band_width * height
    )
    released = jnp.dot(
        weighted.T, cross_table, precision=lax.Precision.HIGHEST, preferred_element_type=jnp.float32
    )
    return released.reshape(slab_len, band_width, height)


def body(populations, solid_mask, smoke_field, fan_hubs, fan_gain, jet_speed, sources, source_rate):
    slab_len = populations.shape[1]
    band_width = populations.shape[2]
    height = populations.shape[3]
    offset_len = lax.axis_index("len") * slab_len
    offset_band = lax.axis_index("band") * band_width
    length_total = slab_len * lax.axis_size("len")
    breadth_total = band_width * lax.axis_size("band")
    solid_flag = solid_mask == 1
    coord_x = offset_len - 1 + jnp.arange(slab_len + 2, dtype=jnp.int32)
    coord_y = jnp.mod(offset_band - 1 + jnp.arange(band_width + 2, dtype=jnp.int32), breadth_total)
    coord_z = jnp.arange(height, dtype=jnp.int32)
    along_in = jnp.mod(coord_x[None, :] - fan_hubs[:, 0:1], length_total) < FAN_LEN
    offset_y = coord_y[None, :] - fan_hubs[:, 1:2]
    offset_z = coord_z[None, :] - fan_hubs[:, 2:3]
    across_in = (
        offset_y[:, :, None] * offset_y[:, :, None] + offset_z[:, None, :] * offset_z[:, None, :]
        <= RAD * RAD
    )
    released = source_release(
        sources, source_rate, offset_len, offset_band, slab_len, band_width, height
    )
    len_reach = max(-(-FAN_LEN // slab_len), (slab_len + FAN_LEN - 1) // slab_len)
    band_reach = max(-(-(2 * RAD + 1) // band_width), (band_width + 2 * RAD) // band_width)
    inner_discs = (
        along_in[:, 1:-1, None, None]
        & across_in[:, None, 1:-1]
        & jnp.logical_not(solid_flag)[None]
    ).astype(jnp.float32)
    velocity, flow = first_moments(populations, inner_discs)
    partials = jnp.sum(flow, axis=1)
    for repeat in range(ITERS):
        fields = [populations, smoke_field[None]]
        if repeat == 0:
            fields.append(solid_flag.astype(jnp.float32)[None])
        fields, totals = rim_round(fields, partials, "len", 1, len_reach)
        fields, totals = rim_round(fields, totals, "band", 2, band_reach)
        extended = fields[0]
        rimmed = fields[1][0]
        if repeat == 0:
            solid_rim = fields[2][0]
            air_rim = solid_rim == 0.0
            discs = (along_in[:, :, None, None] & across_in[:, None] & air_rim[None]).astype(
                jnp.float32
            )
        strength = fan_gain * (jet_speed - totals / float(disc_count()))
        last = repeat == ITERS - 1
        stepped = lattice_step(
            strength, extended, discs, solid_rim, rimmed, velocity, released, not last
        )
        populations = stepped[0]
        smoke_field = stepped[1]
        if not last:
            velocity = stepped[2]
            partials = jnp.sum(stepped[3], axis=1)
    return (populations, smoke_field)


def solution(mesh):
    placed = (
        P(None, "len", "band", None),
        P("len", "band", None),
        P("len", "band", None),
        P(),
        P(),
        P(),
        P(),
        P(),
    )
    return jax.shard_map(
        body,
        mesh=mesh,
        in_specs=placed,
        out_specs=(P(None, "len", "band", None), P("len", "band", None)),
        check_vma=False,
    )
```

```python
import functools

import jax
import jax.numpy as jnp
from jax import lax
from jax.experimental import pallas as pl
from jax.experimental.pallas import tpu as pltpu
from jax.sharding import PartitionSpec as P

RAD = 3
FAN_LEN = 16
ITERS = 3


VELOCITIES = (
    (0, 0, 0),
    (1, 0, 0),
    (-1, 0, 0),
    (0, 1, 0),
    (0, -1, 0),
    (0, 0, 1),
    (0, 0, -1),
    (1, 1, 0),
    (-1, -1, 0),
    (1, -1, 0),
    (-1, 1, 0),
    (1, 0, 1),
    (-1, 0, -1),
    (1, 0, -1),
    (-1, 0, 1),
    (0, 1, 1),
    (0, -1, -1),
    (0, 1, -1),
    (0, -1, 1),
)
WEIGHTS = (1.0 / 3.0,) + (1.0 / 18.0,) * 6 + (1.0 / 36.0,) * 12
OPPOSITE = (0, 2, 1, 4, 3, 6, 5, 8, 7, 10, 9, 12, 11, 14, 13, 16, 15, 18, 17)
RELAX_RATE = 1.0 / 0.6
DIFFUSIVITY = 0.12


def extended_2(cells, sides, width):
    for axis, dim in sides:
        count = lax.axis_size(axis)
        head = lax.slice_in_dim(cells, 0, width, axis=dim)
        tail = lax.slice_in_dim(cells, cells.shape[dim] - width, cells.shape[dim], axis=dim)
        cells = jnp.concatenate(
            [
                lax.ppermute(tail, axis, [(i, (i + 1) % count) for i in range(count)]),
                cells,
                lax.ppermute(head, axis, [((i + 1) % count, i) for i in range(count)]),
            ],
            axis=dim,
        )
    return cells


def moments(populations):
    density = jnp.sum(populations, axis=0)
    velocity = []
    for dimension in range(3):
        forward = [populations[which] for which in range(19) if VELOCITIES[which][dimension] == 1]
        backward = [populations[which] for which in range(19) if VELOCITIES[which][dimension] == -1]
        velocity.append((sum(forward) - sum(backward)) / density)
    return (density, velocity)


def plane_moments(populations):
    density = sum(populations[1:], populations[0])
    velocity = []
    for dimension in range(3):
        forward = [populations[which] for which in range(19) if VELOCITIES[which][dimension] == 1]
        backward = [populations[which] for which in range(19) if VELOCITIES[which][dimension] == -1]
        velocity.append((sum(forward) - sum(backward)) / density)
    return (density, velocity)


def step_kernel(with_moments, strength_ref, populations_ref, discs_ref, solid_ref, *rest):
    if with_moments:
        out_ref, velocity_ref, flow_ref, posts_ref, sums_ref = rest
    else:
        out_ref, posts_ref = rest
    fans = discs_ref.shape[0]
    slab_len, band_width, height = out_ref.shape[1:]

    def collide_plane(index, carry):
        populations = [populations_ref[which, index] for which in range(19)]
        density, velocity = plane_moments(populations)
        force_field = strength_ref[0] * discs_ref[0, index]
        for fan_number in range(1, fans):
            force_field = force_field + strength_ref[fan_number] * discs_ref[fan_number, index]
        solid_flag = solid_ref[index] != 0.0
        speed_sq = velocity[0] * velocity[0] + velocity[1] * velocity[1] + velocity[2] * velocity[2]
        for which in range(19):
            shift_x, shift_y, shift_z = VELOCITIES[which]
            along = shift_x * velocity[0] + shift_y * velocity[1] + shift_z * velocity[2]
            balance = (
                WEIGHTS[which] * density * (1.0 + 3.0 * along + 4.5 * along * along - 1.5 * speed_sq)
            )
            relaxed = populations[which] - RELAX_RATE * (populations[which] - balance)
            if shift_x != 0:
                relaxed = relaxed + 3.0 * WEIGHTS[which] * shift_x * force_field
            posts_ref[which, index] = jnp.where(solid_flag, populations[OPPOSITE[which]], relaxed)
        return carry

    lax.fori_loop(0, populations_ref.shape[1], collide_plane, 0)
    lane = lax.broadcasted_iota(jnp.int32, (slab_len, band_width, height), 2)
    for which in range(19):
        shift_x, shift_y, shift_z = VELOCITIES[which]
        piece = posts_ref[
            which, 1 - shift_x : 1 - shift_x + slab_len, 1 - shift_y : 1 - shift_y + band_width, :
        ]
        if shift_z == 1:
            piece = jnp.where(lane == 0, 0.0, pltpu.roll(piece, 1, 2))
        elif shift_z == -1:
            piece = jnp.where(lane == height - 1, 0.0, pltpu.roll(piece, height - 1, 2))
        out_ref[which] = piece
    if not with_moments:
        return
    moments_into(out_ref, discs_ref, 1, velocity_ref, flow_ref, sums_ref)


def moments_into(populations_ref, discs_ref, rim, velocity_ref, flow_ref, sums_ref):
    fans = discs_ref.shape[0]
    band_width = populations_ref.shape[2]
    sums_ref[...] = jnp.zeros(sums_ref.shape, jnp.float32)

    def moment_plane(index, carry):
        density, velocity = plane_moments([populations_ref[which, index] for which in range(19)])
        for dimension in range(3):
            velocity_ref[dimension, index] = velocity[dimension]
        for fan_number in range(fans):
            sums_ref[fan_number] += (
                discs_ref[fan_number, index + rim, rim : rim + band_width, :] * velocity[0]
            )
        return carry

    lax.fori_loop(0, populations_ref.shape[1], moment_plane, 0)
    for fan_number in range(fans):
        flow_ref[fan_number : fan_number + 1, :] = jnp.sum(sums_ref[fan_number], axis=0, keepdims=True)


def first_moments(populations, discs):
    fans, slab_len, band_width, height = discs.shape
    vmem = pl.BlockSpec(memory_space=pltpu.VMEM)
    return pl.pallas_call(
        lambda populations_ref, discs_ref, velocity_ref, flow_ref, sums_ref: moments_into(
            populations_ref, discs_ref, 0, velocity_ref, flow_ref, sums_ref
        ),
        out_shape=(
            jax.ShapeDtypeStruct((3, slab_len, band_width, height), jnp.float32),
            jax.ShapeDtypeStruct((fans, height), jnp.float32),
        ),
        in_specs=[vmem, vmem],
        out_specs=(vmem, vmem),
        scratch_shapes=[pltpu.VMEM((fans, band_width, height), jnp.float32)],
        cost_estimate=pl.CostEstimate(
            flops=60 * discs[0].size, transcendentals=0, bytes_accessed=4 * populations.size
        ),
    )(populations, discs)


def lattice_step(strength, extended, discs, solid_rim, with_moments):
    slab_len = extended.shape[1] - 2
    band_width = extended.shape[2] - 2
    height = extended.shape[3]
    fans = discs.shape[0]
    out_shape = [jax.ShapeDtypeStruct((19, slab_len, band_width, height), jnp.float32)]
    if with_moments:
        out_shape.append(jax.ShapeDtypeStruct((3, slab_len, band_width, height), jnp.float32))
        out_shape.append(jax.ShapeDtypeStruct((fans, height), jnp.float32))
    scratch = [pltpu.VMEM(extended.shape, jnp.float32)]
    if with_moments:
        scratch.append(pltpu.VMEM((fans, band_width, height), jnp.float32))
    vmem = pl.BlockSpec(memory_space=pltpu.VMEM)
    return pl.pallas_call(
        functools.partial(step_kernel, with_moments),
        out_shape=tuple(out_shape),
        in_specs=[pl.BlockSpec(memory_space=pltpu.SMEM), vmem, vmem, vmem],
        out_specs=tuple([vmem] * len(out_shape)),
        scratch_shapes=scratch,
        cost_estimate=pl.CostEstimate(
            flops=300 * solid_rim.size, transcendentals=0, bytes_accessed=12 * extended.size
        ),
    )(strength, extended, discs, solid_rim)


def disc_count():
    inside = 0
    for offset_a in range(-RAD, RAD + 1):
        for offset_b in range(-RAD, RAD + 1):
            if offset_a * offset_a + offset_b * offset_b <= RAD * RAD:
                inside = inside + 1
    return FAN_LEN * inside


def fan_discs(fan_hubs, coord_x, coord_y, coord_z, length_total):
    discs = []
    for fan_number in range(fan_hubs.shape[0]):
        offset_x = jnp.mod(coord_x - fan_hubs[fan_number, 0], length_total)
        offset_y = coord_y - fan_hubs[fan_number, 1]
        offset_z = coord_z - fan_hubs[fan_number, 2]
        discs.append(
            (offset_x < FAN_LEN) & (offset_y * offset_y + offset_z * offset_z <= RAD * RAD)
        )
    return discs


def partial_flow(discs, velocity, solid_flag):
    return jnp.stack(
        [
            jnp.sum(jnp.where(disc_nodes & jnp.logical_not(solid_flag), velocity[0], 0.0))
            for disc_nodes in discs
        ]
    )


def force_from(discs, totals, fan_gain, jet_speed):
    strength = fan_gain * (jet_speed - totals / float(disc_count()))
    force_field = jnp.zeros(discs[0].shape, jnp.float32)
    for fan_number in range(len(discs)):
        force_field = force_field + jnp.where(discs[fan_number], strength[fan_number], 0.0)
    return force_field


def advance(center, ahead_x, behind_x, ahead_y, behind_y, ahead_z, behind_z, velocity, solid_flag):
    laplace = ahead_x + behind_x + ahead_y + behind_y + ahead_z + behind_z - 6.0 * center
    advect = 0.5 * (
        velocity[0] * (ahead_x - behind_x)
        + velocity[1] * (ahead_y - behind_y)
        + velocity[2] * (ahead_z - behind_z)
    )
    return jnp.where(solid_flag, 0.0, center + DIFFUSIVITY * laplace - advect)


def shift_height(field, shift_z):
    if shift_z == 0:
        return field
    zero_layer = jnp.zeros(field.shape[:-1] + (1,), field.dtype)
    if shift_z == 1:
        return jnp.concatenate([zero_layer, field[..., :-1]], axis=-1)
    return jnp.concatenate([field[..., 1:], zero_layer], axis=-1)


def rim_round(fields, flow, axis, dim, reach):
    count = lax.axis_size(axis)
    fans = flow.shape[0]
    channels = [field.shape[0] for field in fields]

    def piece(start):
        cells = [lax.slice_in_dim(field, start, start + 1, axis=dim) for field in fields]
        carrier = jnp.zeros(cells[0].shape[1:], jnp.float32)
        carrier = lax.dynamic_update_slice_in_dim(
            carrier, jnp.expand_dims(flow, dim - 1), 0, axis=2 - dim
        )[None]
        return jnp.concatenate(cells + [carrier], axis=0)

    def pick(received):
        return jnp.squeeze(
            lax.slice_in_dim(received[-1], 0, fans, axis=2 - dim), axis=dim - 1
        )

    head = piece(0)
    tail = piece(fields[0].shape[dim] - 1)
    forward = [(i, (i + 1) % count) for i in range(count)]
    backward = [((i + 1) % count, i) for i in range(count)]
    if count == 2:
        both = lax.ppermute(jnp.concatenate([tail, head], axis=0), axis, forward)
        from_left = both[: tail.shape[0]]
        from_right = both[tail.shape[0] :]
        total = flow + pick(from_left)
    else:
        from_left = lax.ppermute(tail, axis, forward)
        from_right = lax.ppermute(head, axis, backward)
        total = flow + pick(from_left) + pick(from_right)
    for offset in sorted(set(step % count for step in range(-reach, reach + 1)) - {0, 1, count - 1}):
        total = total + lax.ppermute(flow, axis, [(i, (i + offset) % count) for i in range(count)])
    extended = []
    first = 0
    for field, channel in zip(fields, channels):
        extended.append(
            jnp.concatenate(
                [from_left[first : first + channel], field, from_right[first : first + channel]],
                axis=dim,
            )
        )
        first = first + channel
    return (extended, total)


def window_sum(values, axis, width):
    count = lax.axis_size(axis)
    total = values
    for offset in sorted(set(step % count for step in range(-width, width + 1)) - {0}):
        total = total + lax.ppermute(
            values, axis, [(i, (i + offset) % count) for i in range(count)]
        )
    return total


def source_release(sources, source_rate, offset_len, offset_band, slab_len, band_width, height):
    local_x = sources[:, 0] - offset_len
    local_y = sources[:, 1] - offset_band
    pick_x = (local_x[:, None] == jnp.arange(slab_len, dtype=jnp.int32)[None, :]).astype(
        jnp.float32
    )
    pick_y = (local_y[:, None] == jnp.arange(band_width, dtype=jnp.int32)[None, :]).astype(
        jnp.float32
    )
    pick_z = (sources[:, 2][:, None] == jnp.arange(height, dtype=jnp.int32)[None, :]).astype(
        jnp.float32
    )
    weighted = source_rate[:, None] * pick_x
    cross_table = (pick_y[:, :, None] * pick_z[:, None, :]).reshape(
        sources.shape[0], band_width * height
    )
    released = jnp.dot(
        weighted.T, cross_table, precision=lax.Precision.HIGHEST, preferred_element_type=jnp.float32
    )
    return released.reshape(slab_len, band_width, height)


def body(populations, solid_mask, smoke_field, fan_hubs, fan_gain, jet_speed, sources, source_rate):
    slab_len = populations.shape[1]
    band_width = populations.shape[2]
    height = populations.shape[3]
    offset_len = lax.axis_index("len") * slab_len
    offset_band = lax.axis_index("band") * band_width
    length_total = slab_len * lax.axis_size("len")
    breadth_total = band_width * lax.axis_size("band")
    solid_flag = solid_mask == 1
    coord_x = offset_len - 1 + jnp.arange(slab_len + 2, dtype=jnp.int32)
    coord_y = jnp.mod(offset_band - 1 + jnp.arange(band_width + 2, dtype=jnp.int32), breadth_total)
    coord_z = jnp.arange(height, dtype=jnp.int32)
    along_in = jnp.mod(coord_x[None, :] - fan_hubs[:, 0:1], length_total) < FAN_LEN
    offset_y = coord_y[None, :] - fan_hubs[:, 1:2]
    offset_z = coord_z[None, :] - fan_hubs[:, 2:3]
    across_in = (
        offset_y[:, :, None] * offset_y[:, :, None] + offset_z[:, None, :] * offset_z[:, None, :]
        <= RAD * RAD
    )
    released = source_release(
        sources, source_rate, offset_len, offset_band, slab_len, band_width, height
    )
    len_reach = max(-(-FAN_LEN // slab_len), (slab_len + FAN_LEN - 1) // slab_len)
    band_reach = max(-(-(2 * RAD + 1) // band_width), (band_width + 2 * RAD) // band_width)
    inner_discs = (
        along_in[:, 1:-1, None, None]
        & across_in[:, None, 1:-1]
        & jnp.logical_not(solid_flag)[None]
    ).astype(jnp.float32)
    velocity, flow = first_moments(populations, inner_discs)
    partials = flow
    for repeat in range(ITERS):
        fields = [populations, smoke_field[None]]
        if repeat == 0:
            fields.append(solid_flag.astype(jnp.float32)[None])
        fields, totals = rim_round(fields, partials, "len", 1, len_reach)
        fields, totals = rim_round(fields, totals, "band", 2, band_reach)
        extended = fields[0]
        rimmed = fields[1][0]
        if repeat == 0:
            solid_rim = fields[2][0]
            air_rim = solid_rim == 0.0
            discs = (along_in[:, :, None, None] & across_in[:, None] & air_rim[None]).astype(
                jnp.float32
            )
        strength = fan_gain * (jet_speed - jnp.sum(totals, axis=1) / float(disc_count()))
        last = repeat == ITERS - 1
        stepped = lattice_step(strength, extended, discs, solid_rim, not last)
        ahead_x = rimmed[2:, 1:-1]
        behind_x = rimmed[:-2, 1:-1]
        ahead_y = rimmed[1:-1, 2:]
        behind_y = rimmed[1:-1, :-2]
        smoke_field = advance(
            smoke_field,
            ahead_x,
            behind_x,
            ahead_y,
            behind_y,
            shift_height(smoke_field, -1),
            shift_height(smoke_field, 1),
            velocity,
            solid_flag,
        )
        smoke_field = smoke_field + released
        populations = stepped[0]
        if not last:
            velocity = stepped[1]
            partials = stepped[2]
    return (populations, smoke_field)


def solution(mesh):
    placed = (
        P(None, "len", "band", None),
        P("len", "band", None),
        P("len", "band", None),
        P(),
        P(),
        P(),
        P(),
        P(),
    )
    return jax.shard_map(
        body,
        mesh=mesh,
        in_specs=placed,
        out_specs=(P(None, "len", "band", None), P("len", "band", None)),
        check_vma=False,
    )
```

```python
import functools

import jax
import jax.numpy as jnp
from jax import lax
from jax.experimental import pallas as pl
from jax.experimental.pallas import tpu as pltpu
from jax.sharding import PartitionSpec as P

RAD = 3
FAN_LEN = 16
ITERS = 3


VELOCITIES = (
    (0, 0, 0),
    (1, 0, 0),
    (-1, 0, 0),
    (0, 1, 0),
    (0, -1, 0),
    (0, 0, 1),
    (0, 0, -1),
    (1, 1, 0),
    (-1, -1, 0),
    (1, -1, 0),
    (-1, 1, 0),
    (1, 0, 1),
    (-1, 0, -1),
    (1, 0, -1),
    (-1, 0, 1),
    (0, 1, 1),
    (0, -1, -1),
    (0, 1, -1),
    (0, -1, 1),
)
WEIGHTS = (1.0 / 3.0,) + (1.0 / 18.0,) * 6 + (1.0 / 36.0,) * 12
OPPOSITE = (0, 2, 1, 4, 3, 6, 5, 8, 7, 10, 9, 12, 11, 14, 13, 16, 15, 18, 17)
RELAX_RATE = 1.0 / 0.6
DIFFUSIVITY = 0.12


def extended_2(cells, sides, width):
    for axis, dim in sides:
        count = lax.axis_size(axis)
        head = lax.slice_in_dim(cells, 0, width, axis=dim)
        tail = lax.slice_in_dim(cells, cells.shape[dim] - width, cells.shape[dim], axis=dim)
        cells = jnp.concatenate(
            [
                lax.ppermute(tail, axis, [(i, (i + 1) % count) for i in range(count)]),
                cells,
                lax.ppermute(head, axis, [((i + 1) % count, i) for i in range(count)]),
            ],
            axis=dim,
        )
    return cells


def moments(populations):
    density = jnp.sum(populations, axis=0)
    velocity = []
    for dimension in range(3):
        forward = [populations[which] for which in range(19) if VELOCITIES[which][dimension] == 1]
        backward = [populations[which] for which in range(19) if VELOCITIES[which][dimension] == -1]
        velocity.append((sum(forward) - sum(backward)) / density)
    return (density, velocity)


def plane_moments(populations):
    density = sum(populations[1:], populations[0])
    velocity = []
    for dimension in range(3):
        forward = [populations[which] for which in range(19) if VELOCITIES[which][dimension] == 1]
        backward = [populations[which] for which in range(19) if VELOCITIES[which][dimension] == -1]
        velocity.append((sum(forward) - sum(backward)) / density)
    return (density, velocity)


def step_kernel(with_moments, strength_ref, populations_ref, discs_ref, solid_ref, *rest):
    if with_moments:
        out_ref, velocity_ref, flow_ref, posts_ref = rest
    else:
        out_ref, posts_ref = rest
    fans = discs_ref.shape[0]
    slab_len, band_width, height = out_ref.shape[1:]

    def collide_plane(index, carry):
        populations = [populations_ref[which, index] for which in range(19)]
        density, velocity = plane_moments(populations)
        force_field = strength_ref[0] * discs_ref[0, index]
        for fan_number in range(1, fans):
            force_field = force_field + strength_ref[fan_number] * discs_ref[fan_number, index]
        solid_flag = solid_ref[index] != 0.0
        speed_sq = velocity[0] * velocity[0] + velocity[1] * velocity[1] + velocity[2] * velocity[2]
        for which in range(19):
            shift_x, shift_y, shift_z = VELOCITIES[which]
            along = shift_x * velocity[0] + shift_y * velocity[1] + shift_z * velocity[2]
            balance = (
                WEIGHTS[which] * density * (1.0 + 3.0 * along + 4.5 * along * along - 1.5 * speed_sq)
            )
            relaxed = populations[which] - RELAX_RATE * (populations[which] - balance)
            if shift_x != 0:
                relaxed = relaxed + 3.0 * WEIGHTS[which] * shift_x * force_field
            posts_ref[which, index] = jnp.where(solid_flag, populations[OPPOSITE[which]], relaxed)
        return carry

    lax.fori_loop(0, populations_ref.shape[1], collide_plane, 0)
    lane = lax.broadcasted_iota(jnp.int32, (slab_len, band_width, height), 2)
    row = lax.broadcasted_iota(jnp.int32, (slab_len, band_width, height), 1)
    for which in range(19):
        shift_x, shift_y, shift_z = VELOCITIES[which]
        planes = slice(1 - shift_x, 1 - shift_x + slab_len)
        piece = posts_ref[which, planes, 0:band_width, :]
        if shift_y == 1:
            rim_row = posts_ref[which, planes, band_width : band_width + 1, :]
            piece = jnp.where(row == 0, rim_row, pltpu.roll(piece, 1, 1))
        elif shift_y == -1:
            rim_row = posts_ref[which, planes, band_width + 1 : band_width + 2, :]
            piece = jnp.where(row == band_width - 1, rim_row, pltpu.roll(piece, band_width - 1, 1))
        if shift_z == 1:
            piece = jnp.where(lane == 0, 0.0, pltpu.roll(piece, 1, 2))
        elif shift_z == -1:
            piece = jnp.where(lane == height - 1, 0.0, pltpu.roll(piece, height - 1, 2))
        out_ref[which] = piece
    if not with_moments:
        return
    moments_into(out_ref, discs_ref, 1, velocity_ref, flow_ref)


def moments_into(populations_ref, discs_ref, rim, velocity_ref, flow_ref):
    fans = discs_ref.shape[0]
    band_width = populations_ref.shape[2]
    flow_ref[...] = jnp.zeros(flow_ref.shape, jnp.float32)

    def moment_plane(index, carry):
        density, velocity = plane_moments([populations_ref[which, index] for which in range(19)])
        for dimension in range(3):
            velocity_ref[dimension, index] = velocity[dimension]
        for fan_number in range(fans):
            flow_ref[fan_number] += (
                discs_ref[fan_number, index + rim, 0:band_width, :] * velocity[0]
            )
        return carry

    lax.fori_loop(0, populations_ref.shape[1], moment_plane, 0)


def first_moments(populations, discs):
    fans, slab_len, band_width, height = discs.shape
    vmem = pl.BlockSpec(memory_space=pltpu.VMEM)
    return pl.pallas_call(
        lambda populations_ref, discs_ref, velocity_ref, flow_ref: moments_into(
            populations_ref, discs_ref, 0, velocity_ref, flow_ref
        ),
        out_shape=(
            jax.ShapeDtypeStruct((3, slab_len, band_width, height), jnp.float32),
            jax.ShapeDtypeStruct((fans, band_width, height), jnp.float32),
        ),
        in_specs=[vmem, vmem],
        out_specs=(vmem, vmem),
        cost_estimate=pl.CostEstimate(
            flops=60 * discs[0].size, transcendentals=0, bytes_accessed=4 * populations.size
        ),
    )(populations, discs)


def lattice_step(strength, extended, discs, solid_rim, with_moments):
    slab_len = extended.shape[1] - 2
    band_width = extended.shape[2] - 2
    height = extended.shape[3]
    fans = discs.shape[0]
    out_shape = [jax.ShapeDtypeStruct((19, slab_len, band_width, height), jnp.float32)]
    if with_moments:
        out_shape.append(jax.ShapeDtypeStruct((3, slab_len, band_width, height), jnp.float32))
        out_shape.append(jax.ShapeDtypeStruct((fans, band_width, height), jnp.float32))
    vmem = pl.BlockSpec(memory_space=pltpu.VMEM)
    return pl.pallas_call(
        functools.partial(step_kernel, with_moments),
        out_shape=tuple(out_shape),
        in_specs=[pl.BlockSpec(memory_space=pltpu.SMEM), vmem, vmem, vmem],
        out_specs=tuple([vmem] * len(out_shape)),
        scratch_shapes=[pltpu.VMEM(extended.shape, jnp.float32)],
        cost_estimate=pl.CostEstimate(
            flops=300 * solid_rim.size, transcendentals=0, bytes_accessed=12 * extended.size
        ),
    )(strength, extended, discs, solid_rim)


def disc_count():
    inside = 0
    for offset_a in range(-RAD, RAD + 1):
        for offset_b in range(-RAD, RAD + 1):
            if offset_a * offset_a + offset_b * offset_b <= RAD * RAD:
                inside = inside + 1
    return FAN_LEN * inside


def fan_discs(fan_hubs, coord_x, coord_y, coord_z, length_total):
    discs = []
    for fan_number in range(fan_hubs.shape[0]):
        offset_x = jnp.mod(coord_x - fan_hubs[fan_number, 0], length_total)
        offset_y = coord_y - fan_hubs[fan_number, 1]
        offset_z = coord_z - fan_hubs[fan_number, 2]
        discs.append(
            (offset_x < FAN_LEN) & (offset_y * offset_y + offset_z * offset_z <= RAD * RAD)
        )
    return discs


def partial_flow(discs, velocity, solid_flag):
    return jnp.stack(
        [
            jnp.sum(jnp.where(disc_nodes & jnp.logical_not(solid_flag), velocity[0], 0.0))
            for disc_nodes in discs
        ]
    )


def force_from(discs, totals, fan_gain, jet_speed):
    strength = fan_gain * (jet_speed - totals / float(disc_count()))
    force_field = jnp.zeros(discs[0].shape, jnp.float32)
    for fan_number in range(len(discs)):
        force_field = force_field + jnp.where(discs[fan_number], strength[fan_number], 0.0)
    return force_field


def advance(center, ahead_x, behind_x, ahead_y, behind_y, ahead_z, behind_z, velocity, solid_flag):
    laplace = ahead_x + behind_x + ahead_y + behind_y + ahead_z + behind_z - 6.0 * center
    advect = 0.5 * (
        velocity[0] * (ahead_x - behind_x)
        + velocity[1] * (ahead_y - behind_y)
        + velocity[2] * (ahead_z - behind_z)
    )
    return jnp.where(solid_flag, 0.0, center + DIFFUSIVITY * laplace - advect)


def shift_height(field, shift_z):
    if shift_z == 0:
        return field
    zero_layer = jnp.zeros(field.shape[:-1] + (1,), field.dtype)
    if shift_z == 1:
        return jnp.concatenate([zero_layer, field[..., :-1]], axis=-1)
    return jnp.concatenate([field[..., 1:], zero_layer], axis=-1)


def rim_round(fields, flow, axis, dim, reach):
    count = lax.axis_size(axis)
    fans = flow.shape[0]
    channels = [field.shape[0] for field in fields]

    def piece(start):
        cells = [lax.slice_in_dim(field, start, start + 1, axis=dim) for field in fields]
        carrier = jnp.zeros(cells[0].shape[1:], jnp.float32).at[0, 0, :fans].set(flow)[None]
        return jnp.concatenate(cells + [carrier], axis=0)

    head = piece(0)
    tail = piece(fields[0].shape[dim] - 1)
    forward = [(i, (i + 1) % count) for i in range(count)]
    backward = [((i + 1) % count, i) for i in range(count)]
    if count == 2:
        both = lax.ppermute(jnp.concatenate([tail, head], axis=0), axis, forward)
        from_left = both[: tail.shape[0]]
        from_right = both[tail.shape[0] :]
        total = flow + from_left[-1, 0, 0, :fans]
    else:
        from_left = lax.ppermute(tail, axis, forward)
        from_right = lax.ppermute(head, axis, backward)
        total = flow + from_left[-1, 0, 0, :fans] + from_right[-1, 0, 0, :fans]
    for offset in sorted(set(step % count for step in range(-reach, reach + 1)) - {0, 1, count - 1}):
        total = total + lax.ppermute(flow, axis, [(i, (i + offset) % count) for i in range(count)])
    extended = []
    first = 0
    for field, channel in zip(fields, channels):
        left = from_left[first : first + channel]
        right = from_right[first : first + channel]
        if dim == 1:
            extended.append(jnp.concatenate([left, field, right], axis=dim))
        else:
            extended.append(jnp.concatenate([field, left, right], axis=dim))
        first = first + channel
    return (extended, total)


def window_sum(values, axis, width):
    count = lax.axis_size(axis)
    total = values
    for offset in sorted(set(step % count for step in range(-width, width + 1)) - {0}):
        total = total + lax.ppermute(
            values, axis, [(i, (i + offset) % count) for i in range(count)]
        )
    return total


def source_release(sources, source_rate, offset_len, offset_band, slab_len, band_width, height):
    local_x = sources[:, 0] - offset_len
    local_y = sources[:, 1] - offset_band
    pick_x = (local_x[:, None] == jnp.arange(slab_len, dtype=jnp.int32)[None, :]).astype(
        jnp.float32
    )
    pick_y = (local_y[:, None] == jnp.arange(band_width, dtype=jnp.int32)[None, :]).astype(
        jnp.float32
    )
    pick_z = (sources[:, 2][:, None] == jnp.arange(height, dtype=jnp.int32)[None, :]).astype(
        jnp.float32
    )
    weighted = source_rate[:, None] * pick_x
    cross_table = (pick_y[:, :, None] * pick_z[:, None, :]).reshape(
        sources.shape[0], band_width * height
    )
    released = jnp.dot(
        weighted.T, cross_table, precision=lax.Precision.HIGHEST, preferred_element_type=jnp.float32
    )
    return released.reshape(slab_len, band_width, height)


def body(populations, solid_mask, smoke_field, fan_hubs, fan_gain, jet_speed, sources, source_rate):
    slab_len = populations.shape[1]
    band_width = populations.shape[2]
    height = populations.shape[3]
    offset_len = lax.axis_index("len") * slab_len
    offset_band = lax.axis_index("band") * band_width
    length_total = slab_len * lax.axis_size("len")
    breadth_total = band_width * lax.axis_size("band")
    solid_flag = solid_mask == 1
    coord_x = offset_len - 1 + jnp.arange(slab_len + 2, dtype=jnp.int32)
    coord_y = jnp.mod(
        offset_band
        + jnp.concatenate(
            [jnp.arange(band_width, dtype=jnp.int32), jnp.array([-1, band_width], jnp.int32)]
        ),
        breadth_total,
    )
    coord_z = jnp.arange(height, dtype=jnp.int32)
    along_in = jnp.mod(coord_x[None, :] - fan_hubs[:, 0:1], length_total) < FAN_LEN
    offset_y = coord_y[None, :] - fan_hubs[:, 1:2]
    offset_z = coord_z[None, :] - fan_hubs[:, 2:3]
    across_in = (
        offset_y[:, :, None] * offset_y[:, :, None] + offset_z[:, None, :] * offset_z[:, None, :]
        <= RAD * RAD
    )
    released = source_release(
        sources, source_rate, offset_len, offset_band, slab_len, band_width, height
    )
    len_reach = max(-(-FAN_LEN // slab_len), (slab_len + FAN_LEN - 1) // slab_len)
    band_reach = max(-(-(2 * RAD + 1) // band_width), (band_width + 2 * RAD) // band_width)
    inner_discs = (
        along_in[:, 1:-1, None, None]
        & across_in[:, None, 0:band_width]
        & jnp.logical_not(solid_flag)[None]
    ).astype(jnp.float32)
    velocity, flow = first_moments(populations, inner_discs)
    partials = jnp.sum(flow, axis=(1, 2))
    for repeat in range(ITERS):
        fields = [populations, smoke_field[None]]
        if repeat == 0:
            fields.append(solid_flag.astype(jnp.float32)[None])
        fields, totals = rim_round(fields, partials, "len", 1, len_reach)
        fields, totals = rim_round(fields, totals, "band", 2, band_reach)
        extended = fields[0]
        rimmed = fields[1][0]
        if repeat == 0:
            solid_rim = fields[2][0]
            air_rim = solid_rim == 0.0
            discs = (along_in[:, :, None, None] & across_in[:, None] & air_rim[None]).astype(
                jnp.float32
            )
        strength = fan_gain * (jet_speed - totals / float(disc_count()))
        last = repeat == ITERS - 1
        stepped = lattice_step(strength, extended, discs, solid_rim, not last)
        ahead_x = rimmed[2:, 0:band_width]
        behind_x = rimmed[:-2, 0:band_width]
        ahead_y = jnp.concatenate(
            [rimmed[1:-1, 1:band_width], rimmed[1:-1, band_width + 1 : band_width + 2]], axis=1
        )
        behind_y = jnp.concatenate(
            [rimmed[1:-1, band_width : band_width + 1], rimmed[1:-1, 0 : band_width - 1]], axis=1
        )
        smoke_field = advance(
            smoke_field,
            ahead_x,
            behind_x,
            ahead_y,
            behind_y,
            shift_height(smoke_field, -1),
            shift_height(smoke_field, 1),
            velocity,
            solid_flag,
        )
        smoke_field = smoke_field + released
        populations = stepped[0]
        if not last:
            velocity = stepped[1]
            partials = jnp.sum(stepped[2], axis=(1, 2))
    return (populations, smoke_field)


def solution(mesh):
    placed = (
        P(None, "len", "band", None),
        P("len", "band", None),
        P("len", "band", None),
        P(),
        P(),
        P(),
        P(),
        P(),
    )
    return jax.shard_map(
        body,
        mesh=mesh,
        in_specs=placed,
        out_specs=(P(None, "len", "band", None), P("len", "band", None)),
        check_vma=False,
    )
```

```python
import functools

import jax
import jax.numpy as jnp
from jax import lax
from jax.experimental import pallas as pl
from jax.experimental.pallas import tpu as pltpu
from jax.sharding import PartitionSpec as P

RAD = 3
FAN_LEN = 16
ITERS = 3


VELOCITIES = (
    (0, 0, 0),
    (1, 0, 0),
    (-1, 0, 0),
    (0, 1, 0),
    (0, -1, 0),
    (0, 0, 1),
    (0, 0, -1),
    (1, 1, 0),
    (-1, -1, 0),
    (1, -1, 0),
    (-1, 1, 0),
    (1, 0, 1),
    (-1, 0, -1),
    (1, 0, -1),
    (-1, 0, 1),
    (0, 1, 1),
    (0, -1, -1),
    (0, 1, -1),
    (0, -1, 1),
)
WEIGHTS = (1.0 / 3.0,) + (1.0 / 18.0,) * 6 + (1.0 / 36.0,) * 12
OPPOSITE = (0, 2, 1, 4, 3, 6, 5, 8, 7, 10, 9, 12, 11, 14, 13, 16, 15, 18, 17)
RELAX_RATE = 1.0 / 0.6
DIFFUSIVITY = 0.12


def extended_2(cells, sides, width):
    for axis, dim in sides:
        count = lax.axis_size(axis)
        head = lax.slice_in_dim(cells, 0, width, axis=dim)
        tail = lax.slice_in_dim(cells, cells.shape[dim] - width, cells.shape[dim], axis=dim)
        cells = jnp.concatenate(
            [
                lax.ppermute(tail, axis, [(i, (i + 1) % count) for i in range(count)]),
                cells,
                lax.ppermute(head, axis, [((i + 1) % count, i) for i in range(count)]),
            ],
            axis=dim,
        )
    return cells


def moments(populations):
    density = jnp.sum(populations, axis=0)
    velocity = []
    for dimension in range(3):
        forward = [populations[which] for which in range(19) if VELOCITIES[which][dimension] == 1]
        backward = [populations[which] for which in range(19) if VELOCITIES[which][dimension] == -1]
        velocity.append((sum(forward) - sum(backward)) / density)
    return (density, velocity)


def plane_moments(populations):
    density = sum(populations[1:], populations[0])
    velocity = []
    for dimension in range(3):
        forward = [populations[which] for which in range(19) if VELOCITIES[which][dimension] == 1]
        backward = [populations[which] for which in range(19) if VELOCITIES[which][dimension] == -1]
        velocity.append((sum(forward) - sum(backward)) / density)
    return (density, velocity)


def step_kernel(with_moments, strength_ref, populations_ref, discs_ref, solid_ref, *rest):
    if with_moments:
        out_ref, velocity_ref, flow_ref, posts_ref = rest
    else:
        out_ref, posts_ref = rest
    fans = discs_ref.shape[0]
    slab_len, band_width, height = out_ref.shape[1:]

    def collide_at(index, chosen):
        populations = [populations_ref[which, index] for which in range(19)]
        density, velocity = plane_moments(populations)
        force_field = strength_ref[0] * discs_ref[0, index]
        for fan_number in range(1, fans):
            force_field = force_field + strength_ref[fan_number] * discs_ref[fan_number, index]
        solid_flag = solid_ref[index] != 0.0
        speed_sq = velocity[0] * velocity[0] + velocity[1] * velocity[1] + velocity[2] * velocity[2]
        for which in chosen:
            shift_x, shift_y, shift_z = VELOCITIES[which]
            along = shift_x * velocity[0] + shift_y * velocity[1] + shift_z * velocity[2]
            balance = (
                WEIGHTS[which] * density * (1.0 + 3.0 * along + 4.5 * along * along - 1.5 * speed_sq)
            )
            relaxed = populations[which] - RELAX_RATE * (populations[which] - balance)
            if shift_x != 0:
                relaxed = relaxed + 3.0 * WEIGHTS[which] * shift_x * force_field
            posts_ref[which, index] = jnp.where(solid_flag, populations[OPPOSITE[which]], relaxed)

    every = tuple(range(19))
    collide_at(0, tuple(which for which in every if VELOCITIES[which][0] == 1))

    def collide_plane(index, carry):
        collide_at(index, every)
        return carry

    lax.fori_loop(1, slab_len + 1, collide_plane, 0)
    collide_at(slab_len + 1, tuple(which for which in every if VELOCITIES[which][0] == -1))
    row = lax.broadcasted_iota(jnp.int32, (band_width, height), 0)
    lane = lax.broadcasted_iota(jnp.int32, (band_width, height), 1)
    if with_moments:
        flow_ref[...] = jnp.zeros(flow_ref.shape, jnp.float32)

    def stream_plane(index, carry):
        pieces = []
        for which in range(19):
            shift_x, shift_y, shift_z = VELOCITIES[which]
            plane = index + 1 - shift_x
            piece = posts_ref[which, plane, 0:band_width, :]
            if shift_y == 1:
                rim_row = posts_ref[which, plane, band_width : band_width + 1, :]
                piece = jnp.where(row == 0, rim_row, pltpu.roll(piece, 1, 0))
            elif shift_y == -1:
                rim_row = posts_ref[which, plane, band_width + 1 : band_width + 2, :]
                piece = jnp.where(
                    row == band_width - 1, rim_row, pltpu.roll(piece, band_width - 1, 0)
                )
            if shift_z == 1:
                piece = jnp.where(lane == 0, 0.0, pltpu.roll(piece, 1, 1))
            elif shift_z == -1:
                piece = jnp.where(lane == height - 1, 0.0, pltpu.roll(piece, height - 1, 1))
            out_ref[which, index] = piece
            pieces.append(piece)
        if with_moments:
            density, velocity = plane_moments(pieces)
            for dimension in range(3):
                velocity_ref[dimension, index] = velocity[dimension]
            for fan_number in range(fans):
                flow_ref[fan_number] += (
                    discs_ref[fan_number, index + 1, 0:band_width, :] * velocity[0]
                )
        return carry

    lax.fori_loop(0, slab_len, stream_plane, 0)


def moments_into(populations_ref, discs_ref, rim, velocity_ref, flow_ref):
    fans = discs_ref.shape[0]
    band_width = populations_ref.shape[2]
    flow_ref[...] = jnp.zeros(flow_ref.shape, jnp.float32)

    def moment_plane(index, carry):
        density, velocity = plane_moments([populations_ref[which, index] for which in range(19)])
        for dimension in range(3):
            velocity_ref[dimension, index] = velocity[dimension]
        for fan_number in range(fans):
            flow_ref[fan_number] += (
                discs_ref[fan_number, index + rim, 0:band_width, :] * velocity[0]
            )
        return carry

    lax.fori_loop(0, populations_ref.shape[1], moment_plane, 0)


def first_moments(populations, discs):
    fans, slab_len, band_width, height = discs.shape
    vmem = pl.BlockSpec(memory_space=pltpu.VMEM)
    return pl.pallas_call(
        lambda populations_ref, discs_ref, velocity_ref, flow_ref: moments_into(
            populations_ref, discs_ref, 0, velocity_ref, flow_ref
        ),
        out_shape=(
            jax.ShapeDtypeStruct((3, slab_len, band_width, height), jnp.float32),
            jax.ShapeDtypeStruct((fans, band_width, height), jnp.float32),
        ),
        in_specs=[vmem, vmem],
        out_specs=(vmem, vmem),
        cost_estimate=pl.CostEstimate(
            flops=60 * discs[0].size, transcendentals=0, bytes_accessed=4 * populations.size
        ),
    )(populations, discs)


def lattice_step(strength, extended, discs, solid_rim, with_moments):
    slab_len = extended.shape[1] - 2
    band_width = extended.shape[2] - 2
    height = extended.shape[3]
    fans = discs.shape[0]
    out_shape = [jax.ShapeDtypeStruct((19, slab_len, band_width, height), jnp.float32)]
    if with_moments:
        out_shape.append(jax.ShapeDtypeStruct((3, slab_len, band_width, height), jnp.float32))
        out_shape.append(jax.ShapeDtypeStruct((fans, band_width, height), jnp.float32))
    vmem = pl.BlockSpec(memory_space=pltpu.VMEM)
    return pl.pallas_call(
        functools.partial(step_kernel, with_moments),
        out_shape=tuple(out_shape),
        in_specs=[pl.BlockSpec(memory_space=pltpu.SMEM), vmem, vmem, vmem],
        out_specs=tuple([vmem] * len(out_shape)),
        scratch_shapes=[pltpu.VMEM(extended.shape, jnp.float32)],
        cost_estimate=pl.CostEstimate(
            flops=300 * solid_rim.size, transcendentals=0, bytes_accessed=12 * extended.size
        ),
    )(strength, extended, discs, solid_rim)


def disc_count():
    inside = 0
    for offset_a in range(-RAD, RAD + 1):
        for offset_b in range(-RAD, RAD + 1):
            if offset_a * offset_a + offset_b * offset_b <= RAD * RAD:
                inside = inside + 1
    return FAN_LEN * inside


def fan_discs(fan_hubs, coord_x, coord_y, coord_z, length_total):
    discs = []
    for fan_number in range(fan_hubs.shape[0]):
        offset_x = jnp.mod(coord_x - fan_hubs[fan_number, 0], length_total)
        offset_y = coord_y - fan_hubs[fan_number, 1]
        offset_z = coord_z - fan_hubs[fan_number, 2]
        discs.append(
            (offset_x < FAN_LEN) & (offset_y * offset_y + offset_z * offset_z <= RAD * RAD)
        )
    return discs


def partial_flow(discs, velocity, solid_flag):
    return jnp.stack(
        [
            jnp.sum(jnp.where(disc_nodes & jnp.logical_not(solid_flag), velocity[0], 0.0))
            for disc_nodes in discs
        ]
    )


def force_from(discs, totals, fan_gain, jet_speed):
    strength = fan_gain * (jet_speed - totals / float(disc_count()))
    force_field = jnp.zeros(discs[0].shape, jnp.float32)
    for fan_number in range(len(discs)):
        force_field = force_field + jnp.where(discs[fan_number], strength[fan_number], 0.0)
    return force_field


def advance(center, ahead_x, behind_x, ahead_y, behind_y, ahead_z, behind_z, velocity, solid_flag):
    laplace = ahead_x + behind_x + ahead_y + behind_y + ahead_z + behind_z - 6.0 * center
    advect = 0.5 * (
        velocity[0] * (ahead_x - behind_x)
        + velocity[1] * (ahead_y - behind_y)
        + velocity[2] * (ahead_z - behind_z)
    )
    return jnp.where(solid_flag, 0.0, center + DIFFUSIVITY * laplace - advect)


def shift_height(field, shift_z):
    if shift_z == 0:
        return field
    zero_layer = jnp.zeros(field.shape[:-1] + (1,), field.dtype)
    if shift_z == 1:
        return jnp.concatenate([zero_layer, field[..., :-1]], axis=-1)
    return jnp.concatenate([field[..., 1:], zero_layer], axis=-1)


def rim_round(fields, flow, axis, dim, reach):
    count = lax.axis_size(axis)
    fans = flow.shape[0]
    channels = [field.shape[0] for field in fields]

    def piece(start):
        cells = [lax.slice_in_dim(field, start, start + 1, axis=dim) for field in fields]
        carrier = jnp.zeros(cells[0].shape[1:], jnp.float32).at[0, 0, :fans].set(flow)[None]
        return jnp.concatenate(cells + [carrier], axis=0)

    head = piece(0)
    tail = piece(fields[0].shape[dim] - 1)
    forward = [(i, (i + 1) % count) for i in range(count)]
    backward = [((i + 1) % count, i) for i in range(count)]
    if count == 2:
        both = lax.ppermute(jnp.concatenate([tail, head], axis=0), axis, forward)
        from_left = both[: tail.shape[0]]
        from_right = both[tail.shape[0] :]
        total = flow + from_left[-1, 0, 0, :fans]
    else:
        from_left = lax.ppermute(tail, axis, forward)
        from_right = lax.ppermute(head, axis, backward)
        total = flow + from_left[-1, 0, 0, :fans] + from_right[-1, 0, 0, :fans]
    for offset in sorted(set(step % count for step in range(-reach, reach + 1)) - {0, 1, count - 1}):
        total = total + lax.ppermute(flow, axis, [(i, (i + offset) % count) for i in range(count)])
    extended = []
    first = 0
    for field, channel in zip(fields, channels):
        left = from_left[first : first + channel]
        right = from_right[first : first + channel]
        if dim == 1:
            extended.append(jnp.concatenate([left, field, right], axis=dim))
        else:
            extended.append(jnp.concatenate([field, left, right], axis=dim))
        first = first + channel
    return (extended, total)


def window_sum(values, axis, width):
    count = lax.axis_size(axis)
    total = values
    for offset in sorted(set(step % count for step in range(-width, width + 1)) - {0}):
        total = total + lax.ppermute(
            values, axis, [(i, (i + offset) % count) for i in range(count)]
        )
    return total


def source_release(sources, source_rate, offset_len, offset_band, slab_len, band_width, height):
    local_x = sources[:, 0] - offset_len
    local_y = sources[:, 1] - offset_band
    pick_x = (local_x[:, None] == jnp.arange(slab_len, dtype=jnp.int32)[None, :]).astype(
        jnp.float32
    )
    pick_y = (local_y[:, None] == jnp.arange(band_width, dtype=jnp.int32)[None, :]).astype(
        jnp.float32
    )
    pick_z = (sources[:, 2][:, None] == jnp.arange(height, dtype=jnp.int32)[None, :]).astype(
        jnp.float32
    )
    weighted = source_rate[:, None] * pick_x
    cross_table = (pick_y[:, :, None] * pick_z[:, None, :]).reshape(
        sources.shape[0], band_width * height
    )
    released = jnp.dot(
        weighted.T, cross_table, precision=lax.Precision.HIGHEST, preferred_element_type=jnp.float32
    )
    return released.reshape(slab_len, band_width, height)


def body(populations, solid_mask, smoke_field, fan_hubs, fan_gain, jet_speed, sources, source_rate):
    slab_len = populations.shape[1]
    band_width = populations.shape[2]
    height = populations.shape[3]
    offset_len = lax.axis_index("len") * slab_len
    offset_band = lax.axis_index("band") * band_width
    length_total = slab_len * lax.axis_size("len")
    breadth_total = band_width * lax.axis_size("band")
    solid_flag = solid_mask == 1
    coord_x = offset_len - 1 + jnp.arange(slab_len + 2, dtype=jnp.int32)
    coord_y = jnp.mod(
        offset_band
        + jnp.concatenate(
            [jnp.arange(band_width, dtype=jnp.int32), jnp.array([-1, band_width], jnp.int32)]
        ),
        breadth_total,
    )
    coord_z = jnp.arange(height, dtype=jnp.int32)
    along_in = jnp.mod(coord_x[None, :] - fan_hubs[:, 0:1], length_total) < FAN_LEN
    offset_y = coord_y[None, :] - fan_hubs[:, 1:2]
    offset_z = coord_z[None, :] - fan_hubs[:, 2:3]
    across_in = (
        offset_y[:, :, None] * offset_y[:, :, None] + offset_z[:, None, :] * offset_z[:, None, :]
        <= RAD * RAD
    )
    released = source_release(
        sources, source_rate, offset_len, offset_band, slab_len, band_width, height
    )
    len_reach = max(-(-FAN_LEN // slab_len), (slab_len + FAN_LEN - 1) // slab_len)
    band_reach = max(-(-(2 * RAD + 1) // band_width), (band_width + 2 * RAD) // band_width)
    inner_discs = (
        along_in[:, 1:-1, None, None]
        & across_in[:, None, 0:band_width]
        & jnp.logical_not(solid_flag)[None]
    ).astype(jnp.float32)
    velocity, flow = first_moments(populations, inner_discs)
    partials = jnp.sum(flow, axis=(1, 2))
    for repeat in range(ITERS):
        fields = [populations, smoke_field[None]]
        if repeat == 0:
            fields.append(solid_flag.astype(jnp.float32)[None])
        fields, totals = rim_round(fields, partials, "len", 1, len_reach)
        fields, totals = rim_round(fields, totals, "band", 2, band_reach)
        extended = fields[0]
        rimmed = fields[1][0]
        if repeat == 0:
            solid_rim = fields[2][0]
            air_rim = solid_rim == 0.0
            discs = (along_in[:, :, None, None] & across_in[:, None] & air_rim[None]).astype(
                jnp.float32
            )
        strength = fan_gain * (jet_speed - totals / float(disc_count()))
        last = repeat == ITERS - 1
        stepped = lattice_step(strength, extended, discs, solid_rim, not last)
        ahead_x = rimmed[2:, 0:band_width]
        behind_x = rimmed[:-2, 0:band_width]
        ahead_y = jnp.concatenate(
            [rimmed[1:-1, 1:band_width], rimmed[1:-1, band_width + 1 : band_width + 2]], axis=1
        )
        behind_y = jnp.concatenate(
            [rimmed[1:-1, band_width : band_width + 1], rimmed[1:-1, 0 : band_width - 1]], axis=1
        )
        smoke_field = advance(
            smoke_field,
            ahead_x,
            behind_x,
            ahead_y,
            behind_y,
            shift_height(smoke_field, -1),
            shift_height(smoke_field, 1),
            velocity,
            solid_flag,
        )
        smoke_field = smoke_field + released
        populations = stepped[0]
        if not last:
            velocity = stepped[1]
            partials = jnp.sum(stepped[2], axis=(1, 2))
    return (populations, smoke_field)


def solution(mesh):
    placed = (
        P(None, "len", "band", None),
        P("len", "band", None),
        P("len", "band", None),
        P(),
        P(),
        P(),
        P(),
        P(),
    )
    return jax.shard_map(
        body,
        mesh=mesh,
        in_specs=placed,
        out_specs=(P(None, "len", "band", None), P("len", "band", None)),
        check_vma=False,
    )
```

```python
import functools

import jax
import jax.numpy as jnp
from jax import lax
from jax.experimental import pallas as pl
from jax.experimental.pallas import tpu as pltpu
from jax.sharding import PartitionSpec as P

RAD = 3
FAN_LEN = 16
ITERS = 3


VELOCITIES = (
    (0, 0, 0),
    (1, 0, 0),
    (-1, 0, 0),
    (0, 1, 0),
    (0, -1, 0),
    (0, 0, 1),
    (0, 0, -1),
    (1, 1, 0),
    (-1, -1, 0),
    (1, -1, 0),
    (-1, 1, 0),
    (1, 0, 1),
    (-1, 0, -1),
    (1, 0, -1),
    (-1, 0, 1),
    (0, 1, 1),
    (0, -1, -1),
    (0, 1, -1),
    (0, -1, 1),
)
WEIGHTS = (1.0 / 3.0,) + (1.0 / 18.0,) * 6 + (1.0 / 36.0,) * 12
OPPOSITE = (0, 2, 1, 4, 3, 6, 5, 8, 7, 10, 9, 12, 11, 14, 13, 16, 15, 18, 17)
RELAX_RATE = 1.0 / 0.6
DIFFUSIVITY = 0.12


def extended_2(cells, sides, width):
    for axis, dim in sides:
        count = lax.axis_size(axis)
        head = lax.slice_in_dim(cells, 0, width, axis=dim)
        tail = lax.slice_in_dim(cells, cells.shape[dim] - width, cells.shape[dim], axis=dim)
        cells = jnp.concatenate(
            [
                lax.ppermute(tail, axis, [(i, (i + 1) % count) for i in range(count)]),
                cells,
                lax.ppermute(head, axis, [((i + 1) % count, i) for i in range(count)]),
            ],
            axis=dim,
        )
    return cells


def moments(populations):
    density = jnp.sum(populations, axis=0)
    velocity = []
    for dimension in range(3):
        forward = [populations[which] for which in range(19) if VELOCITIES[which][dimension] == 1]
        backward = [populations[which] for which in range(19) if VELOCITIES[which][dimension] == -1]
        velocity.append((sum(forward) - sum(backward)) / density)
    return (density, velocity)


def plane_moments(populations):
    density = sum(populations[1:], populations[0])
    velocity = []
    for dimension in range(3):
        forward = [populations[which] for which in range(19) if VELOCITIES[which][dimension] == 1]
        backward = [populations[which] for which in range(19) if VELOCITIES[which][dimension] == -1]
        velocity.append((sum(forward) - sum(backward)) / density)
    return (density, velocity)


def step_kernel(with_moments, strength_ref, populations_ref, discs_ref, solid_ref, *rest):
    if with_moments:
        out_ref, velocity_ref, flow_ref, posts_ref = rest
    else:
        out_ref, posts_ref = rest
    fans = discs_ref.shape[0]
    slab_len, band_width, height = out_ref.shape[1:]

    def collide_plane(index, carry):
        populations = [populations_ref[which, index] for which in range(19)]
        density, velocity = plane_moments(populations)
        force_field = strength_ref[0] * discs_ref[0, index]
        for fan_number in range(1, fans):
            force_field = force_field + strength_ref[fan_number] * discs_ref[fan_number, index]
        solid_flag = solid_ref[index] != 0.0
        speed_sq = velocity[0] * velocity[0] + velocity[1] * velocity[1] + velocity[2] * velocity[2]
        for which in range(19):
            shift_x, shift_y, shift_z = VELOCITIES[which]
            along = shift_x * velocity[0] + shift_y * velocity[1] + shift_z * velocity[2]
            balance = (
                WEIGHTS[which] * density * (1.0 + 3.0 * along + 4.5 * along * along - 1.5 * speed_sq)
            )
            relaxed = populations[which] - RELAX_RATE * (populations[which] - balance)
            if shift_x != 0:
                relaxed = relaxed + 3.0 * WEIGHTS[which] * shift_x * force_field
            posts_ref[which, index] = jnp.where(solid_flag, populations[OPPOSITE[which]], relaxed)
        return carry

    lax.fori_loop(0, populations_ref.shape[1], collide_plane, 0)
    lane = lax.broadcasted_iota(jnp.int32, (slab_len, band_width, height), 2)
    row = lax.broadcasted_iota(jnp.int32, (slab_len, band_width, height), 1)
    for which in range(19):
        shift_x, shift_y, shift_z = VELOCITIES[which]
        planes = slice(1 - shift_x, 1 - shift_x + slab_len)
        piece = posts_ref[which, planes, 0:band_width, :]
        if shift_y == 1:
            rim_row = posts_ref[which, planes, band_width : band_width + 1, :]
            piece = jnp.where(row == 0, rim_row, pltpu.roll(piece, 1, 1))
        elif shift_y == -1:
            rim_row = posts_ref[which, planes, band_width + 1 : band_width + 2, :]
            piece = jnp.where(row == band_width - 1, rim_row, pltpu.roll(piece, band_width - 1, 1))
        if shift_z == 1:
            piece = jnp.where(lane == 0, 0.0, pltpu.roll(piece, 1, 2))
        elif shift_z == -1:
            piece = jnp.where(lane == height - 1, 0.0, pltpu.roll(piece, height - 1, 2))
        out_ref[which] = piece
    if not with_moments:
        return
    moments_into(out_ref, discs_ref, 1, velocity_ref, flow_ref)


def moments_into(populations_ref, discs_ref, rim, velocity_ref, flow_ref):
    fans = discs_ref.shape[0]
    band_width = populations_ref.shape[2]
    flow_ref[...] = jnp.zeros(flow_ref.shape, jnp.float32)

    def moment_plane(index, carry):
        density, velocity = plane_moments([populations_ref[which, index] for which in range(19)])
        for dimension in range(3):
            velocity_ref[dimension, index] = velocity[dimension]
        for fan_number in range(fans):
            flow_ref[fan_number] += (
                discs_ref[fan_number, index + rim, 0:band_width, :] * velocity[0]
            )
        return carry

    lax.fori_loop(0, populations_ref.shape[1], moment_plane, 0)


def first_moments(populations, discs):
    fans, slab_len, band_width, height = discs.shape
    vmem = pl.BlockSpec(memory_space=pltpu.VMEM)
    return pl.pallas_call(
        lambda populations_ref, discs_ref, velocity_ref, flow_ref: moments_into(
            populations_ref, discs_ref, 0, velocity_ref, flow_ref
        ),
        out_shape=(
            jax.ShapeDtypeStruct((3, slab_len, band_width, height), jnp.float32),
            jax.ShapeDtypeStruct((fans, band_width, height), jnp.float32),
        ),
        in_specs=[vmem, vmem],
        out_specs=(vmem, vmem),
        cost_estimate=pl.CostEstimate(
            flops=60 * discs[0].size, transcendentals=0, bytes_accessed=4 * populations.size
        ),
    )(populations, discs)


def lattice_step(strength, extended, discs, solid_rim, with_moments):
    slab_len = extended.shape[1] - 2
    band_width = extended.shape[2] - 2
    height = extended.shape[3]
    fans = discs.shape[0]
    out_shape = [jax.ShapeDtypeStruct((19, slab_len, band_width, height), jnp.float32)]
    if with_moments:
        out_shape.append(jax.ShapeDtypeStruct((3, slab_len, band_width, height), jnp.float32))
        out_shape.append(jax.ShapeDtypeStruct((fans, band_width, height), jnp.float32))
    vmem = pl.BlockSpec(memory_space=pltpu.VMEM)
    return pl.pallas_call(
        functools.partial(step_kernel, with_moments),
        out_shape=tuple(out_shape),
        in_specs=[pl.BlockSpec(memory_space=pltpu.SMEM), vmem, vmem, vmem],
        out_specs=tuple([vmem] * len(out_shape)),
        scratch_shapes=[pltpu.VMEM(extended.shape, jnp.float32)],
        cost_estimate=pl.CostEstimate(
            flops=300 * solid_rim.size, transcendentals=0, bytes_accessed=12 * extended.size
        ),
    )(strength, extended, discs, solid_rim)


def disc_count():
    inside = 0
    for offset_a in range(-RAD, RAD + 1):
        for offset_b in range(-RAD, RAD + 1):
            if offset_a * offset_a + offset_b * offset_b <= RAD * RAD:
                inside = inside + 1
    return FAN_LEN * inside


def fan_discs(fan_hubs, coord_x, coord_y, coord_z, length_total):
    discs = []
    for fan_number in range(fan_hubs.shape[0]):
        offset_x = jnp.mod(coord_x - fan_hubs[fan_number, 0], length_total)
        offset_y = coord_y - fan_hubs[fan_number, 1]
        offset_z = coord_z - fan_hubs[fan_number, 2]
        discs.append(
            (offset_x < FAN_LEN) & (offset_y * offset_y + offset_z * offset_z <= RAD * RAD)
        )
    return discs


def partial_flow(discs, velocity, solid_flag):
    return jnp.stack(
        [
            jnp.sum(jnp.where(disc_nodes & jnp.logical_not(solid_flag), velocity[0], 0.0))
            for disc_nodes in discs
        ]
    )


def force_from(discs, totals, fan_gain, jet_speed):
    strength = fan_gain * (jet_speed - totals / float(disc_count()))
    force_field = jnp.zeros(discs[0].shape, jnp.float32)
    for fan_number in range(len(discs)):
        force_field = force_field + jnp.where(discs[fan_number], strength[fan_number], 0.0)
    return force_field


def advance(center, ahead_x, behind_x, ahead_y, behind_y, ahead_z, behind_z, velocity, solid_flag):
    laplace = ahead_x + behind_x + ahead_y + behind_y + ahead_z + behind_z - 6.0 * center
    advect = 0.5 * (
        velocity[0] * (ahead_x - behind_x)
        + velocity[1] * (ahead_y - behind_y)
        + velocity[2] * (ahead_z - behind_z)
    )
    return jnp.where(solid_flag, 0.0, center + DIFFUSIVITY * laplace - advect)


def shift_height(field, shift_z):
    if shift_z == 0:
        return field
    zero_layer = jnp.zeros(field.shape[:-1] + (1,), field.dtype)
    if shift_z == 1:
        return jnp.concatenate([zero_layer, field[..., :-1]], axis=-1)
    return jnp.concatenate([field[..., 1:], zero_layer], axis=-1)


def pack_plane(plane, solid_plane, chosen):
    cells = [plane[which] for which in range(19)]
    kept = [jnp.where(solid_plane, cells[OPPOSITE[which]], cells[which]) for which in chosen]
    density, _ = plane_moments(cells)
    momentum = []
    for dimension in range(3):
        forward = [cells[which] for which in range(19) if VELOCITIES[which][dimension] == 1]
        backward = [cells[which] for which in range(19) if VELOCITIES[which][dimension] == -1]
        momentum.append(sum(forward) - sum(backward))
    return jnp.stack(kept + [density] + momentum)


def unpack_plane(packed, solid_plane, chosen):
    kept = {which: packed[slot] for slot, which in enumerate(chosen)}
    density = packed[len(chosen)]
    zero = jnp.zeros_like(density)
    cells = [kept.get(which, zero) for which in range(19)]
    for dimension in range(3):
        rest = packed[len(chosen) + 1 + dimension]
        for which in chosen:
            if VELOCITIES[which][dimension] == 1:
                rest = rest - kept[which]
            elif VELOCITIES[which][dimension] == -1:
                rest = rest + kept[which]
        spare = [
            which
            for which in range(1, 7)
            if VELOCITIES[which][dimension] != 0 and which not in chosen
        ][0]
        cells[spare] = rest if VELOCITIES[spare][dimension] == 1 else -rest
    cells[0] = density - sum(cells[1:])
    for which in chosen:
        cells[OPPOSITE[which]] = jnp.where(solid_plane, kept[which], cells[OPPOSITE[which]])
    return jnp.stack(cells)


def len_round(populations, smoke, solid_planes, flow, reach, inner_solid, halo_solid):
    count = lax.axis_size("len")
    fans = flow.shape[0]
    slab_len = populations.shape[1]
    ahead = tuple(which for which in range(19) if VELOCITIES[which][0] == 1)
    behind = tuple(which for which in range(19) if VELOCITIES[which][0] == -1)
    packed = len(ahead) + 4

    def piece(start, chosen):
        cells = [
            pack_plane(populations[:, start : start + 1], inner_solid[start : start + 1], chosen),
            smoke[None, start : start + 1],
        ]
        if solid_planes is not None:
            cells.append(solid_planes[:, start : start + 1])
        carrier = jnp.zeros(cells[1].shape[1:], jnp.float32).at[0, 0, :fans].set(flow)[None]
        return jnp.concatenate(cells + [carrier], axis=0)

    head = piece(0, behind)
    tail = piece(slab_len - 1, ahead)
    forward = [(i, (i + 1) % count) for i in range(count)]
    backward = [((i + 1) % count, i) for i in range(count)]
    from_left = lax.ppermute(tail, "len", forward)
    from_right = lax.ppermute(head, "len", backward)
    total = flow + from_left[-1, 0, 0, :fans] + from_right[-1, 0, 0, :fans]
    for offset in sorted(set(step % count for step in range(-reach, reach + 1)) - {0, 1, count - 1}):
        total = total + lax.ppermute(flow, "len", [(i, (i + offset) % count) for i in range(count)])
    if solid_planes is not None:
        solid_ext = jnp.concatenate(
            [from_left[packed + 1 : packed + 2], solid_planes, from_right[packed + 1 : packed + 2]],
            axis=1,
        )
        halo_solid = (from_left[packed + 1] != 0.0, from_right[packed + 1] != 0.0)
    else:
        solid_ext = None
    left_cells = unpack_plane(from_left[:packed], halo_solid[0], ahead)
    right_cells = unpack_plane(from_right[:packed], halo_solid[1], behind)
    populations = jnp.concatenate([left_cells, populations, right_cells], axis=1)
    smoke = jnp.concatenate(
        [from_left[packed : packed + 1], smoke[None], from_right[packed : packed + 1]], axis=1
    )
    return (populations, smoke, solid_ext, total)


def rim_round(fields, flow, axis, dim, reach):
    count = lax.axis_size(axis)
    fans = flow.shape[0]
    channels = [field.shape[0] for field in fields]

    def piece(start):
        cells = [lax.slice_in_dim(field, start, start + 1, axis=dim) for field in fields]
        carrier = jnp.zeros(cells[0].shape[1:], jnp.float32).at[0, 0, :fans].set(flow)[None]
        return jnp.concatenate(cells + [carrier], axis=0)

    head = piece(0)
    tail = piece(fields[0].shape[dim] - 1)
    forward = [(i, (i + 1) % count) for i in range(count)]
    backward = [((i + 1) % count, i) for i in range(count)]
    if count == 2:
        both = lax.ppermute(jnp.concatenate([tail, head], axis=0), axis, forward)
        from_left = both[: tail.shape[0]]
        from_right = both[tail.shape[0] :]
        total = flow + from_left[-1, 0, 0, :fans]
    else:
        from_left = lax.ppermute(tail, axis, forward)
        from_right = lax.ppermute(head, axis, backward)
        total = flow + from_left[-1, 0, 0, :fans] + from_right[-1, 0, 0, :fans]
    for offset in sorted(set(step % count for step in range(-reach, reach + 1)) - {0, 1, count - 1}):
        total = total + lax.ppermute(flow, axis, [(i, (i + offset) % count) for i in range(count)])
    extended = []
    first = 0
    for field, channel in zip(fields, channels):
        left = from_left[first : first + channel]
        right = from_right[first : first + channel]
        if dim == 1:
            extended.append(jnp.concatenate([left, field, right], axis=dim))
        else:
            extended.append(jnp.concatenate([field, left, right], axis=dim))
        first = first + channel
    return (extended, total)


def window_sum(values, axis, width):
    count = lax.axis_size(axis)
    total = values
    for offset in sorted(set(step % count for step in range(-width, width + 1)) - {0}):
        total = total + lax.ppermute(
            values, axis, [(i, (i + offset) % count) for i in range(count)]
        )
    return total


def source_release(sources, source_rate, offset_len, offset_band, slab_len, band_width, height):
    local_x = sources[:, 0] - offset_len
    local_y = sources[:, 1] - offset_band
    pick_x = (local_x[:, None] == jnp.arange(slab_len, dtype=jnp.int32)[None, :]).astype(
        jnp.float32
    )
    pick_y = (local_y[:, None] == jnp.arange(band_width, dtype=jnp.int32)[None, :]).astype(
        jnp.float32
    )
    pick_z = (sources[:, 2][:, None] == jnp.arange(height, dtype=jnp.int32)[None, :]).astype(
        jnp.float32
    )
    weighted = source_rate[:, None] * pick_x
    cross_table = (pick_y[:, :, None] * pick_z[:, None, :]).reshape(
        sources.shape[0], band_width * height
    )
    released = jnp.dot(
        weighted.T, cross_table, precision=lax.Precision.HIGHEST, preferred_element_type=jnp.float32
    )
    return released.reshape(slab_len, band_width, height)


def body(populations, solid_mask, smoke_field, fan_hubs, fan_gain, jet_speed, sources, source_rate):
    slab_len = populations.shape[1]
    band_width = populations.shape[2]
    height = populations.shape[3]
    offset_len = lax.axis_index("len") * slab_len
    offset_band = lax.axis_index("band") * band_width
    length_total = slab_len * lax.axis_size("len")
    breadth_total = band_width * lax.axis_size("band")
    solid_flag = solid_mask == 1
    coord_x = offset_len - 1 + jnp.arange(slab_len + 2, dtype=jnp.int32)
    coord_y = jnp.mod(
        offset_band
        + jnp.concatenate(
            [jnp.arange(band_width, dtype=jnp.int32), jnp.array([-1, band_width], jnp.int32)]
        ),
        breadth_total,
    )
    coord_z = jnp.arange(height, dtype=jnp.int32)
    along_in = jnp.mod(coord_x[None, :] - fan_hubs[:, 0:1], length_total) < FAN_LEN
    offset_y = coord_y[None, :] - fan_hubs[:, 1:2]
    offset_z = coord_z[None, :] - fan_hubs[:, 2:3]
    across_in = (
        offset_y[:, :, None] * offset_y[:, :, None] + offset_z[:, None, :] * offset_z[:, None, :]
        <= RAD * RAD
    )
    released = source_release(
        sources, source_rate, offset_len, offset_band, slab_len, band_width, height
    )
    len_reach = max(-(-FAN_LEN // slab_len), (slab_len + FAN_LEN - 1) // slab_len)
    band_reach = max(-(-(2 * RAD + 1) // band_width), (band_width + 2 * RAD) // band_width)
    inner_discs = (
        along_in[:, 1:-1, None, None]
        & across_in[:, None, 0:band_width]
        & jnp.logical_not(solid_flag)[None]
    ).astype(jnp.float32)
    velocity, flow = first_moments(populations, inner_discs)
    partials = jnp.sum(flow, axis=(1, 2))
    for repeat in range(ITERS):
        if repeat == 0:
            solid_planes = solid_flag.astype(jnp.float32)[None]
            halo_solid = None
        else:
            solid_planes = None
            halo_solid = (
                solid_rim[0:1, 0:band_width] != 0.0,
                solid_rim[slab_len + 1 : slab_len + 2, 0:band_width] != 0.0,
            )
        cells_ext, smoke_ext, solid_ext, totals = len_round(
            populations, smoke_field, solid_planes, partials, len_reach, solid_flag, halo_solid
        )
        fields = [cells_ext, smoke_ext]
        if repeat == 0:
            fields.append(solid_ext)
        fields, totals = rim_round(fields, totals, "band", 2, band_reach)
        extended = fields[0]
        rimmed = fields[1][0]
        if repeat == 0:
            solid_rim = fields[2][0]
            air_rim = solid_rim == 0.0
            discs = (along_in[:, :, None, None] & across_in[:, None] & air_rim[None]).astype(
                jnp.float32
            )
        strength = fan_gain * (jet_speed - totals / float(disc_count()))
        last = repeat == ITERS - 1
        stepped = lattice_step(strength, extended, discs, solid_rim, not last)
        ahead_x = rimmed[2:, 0:band_width]
        behind_x = rimmed[:-2, 0:band_width]
        ahead_y = jnp.concatenate(
            [rimmed[1:-1, 1:band_width], rimmed[1:-1, band_width + 1 : band_width + 2]], axis=1
        )
        behind_y = jnp.concatenate(
            [rimmed[1:-1, band_width : band_width + 1], rimmed[1:-1, 0 : band_width - 1]], axis=1
        )
        smoke_field = advance(
            smoke_field,
            ahead_x,
            behind_x,
            ahead_y,
            behind_y,
            shift_height(smoke_field, -1),
            shift_height(smoke_field, 1),
            velocity,
            solid_flag,
        )
        smoke_field = smoke_field + released
        populations = stepped[0]
        if not last:
            velocity = stepped[1]
            partials = jnp.sum(stepped[2], axis=(1, 2))
    return (populations, smoke_field)


def solution(mesh):
    placed = (
        P(None, "len", "band", None),
        P("len", "band", None),
        P("len", "band", None),
        P(),
        P(),
        P(),
        P(),
        P(),
    )
    return jax.shard_map(
        body,
        mesh=mesh,
        in_specs=placed,
        out_specs=(P(None, "len", "band", None), P("len", "band", None)),
        check_vma=False,
    )
```

```python
import functools

import jax
import jax.numpy as jnp
from jax import lax
from jax.experimental import pallas as pl
from jax.experimental.pallas import tpu as pltpu
from jax.sharding import PartitionSpec as P

RAD = 3
FAN_LEN = 16
ITERS = 3


VELOCITIES = (
    (0, 0, 0),
    (1, 0, 0),
    (-1, 0, 0),
    (0, 1, 0),
    (0, -1, 0),
    (0, 0, 1),
    (0, 0, -1),
    (1, 1, 0),
    (-1, -1, 0),
    (1, -1, 0),
    (-1, 1, 0),
    (1, 0, 1),
    (-1, 0, -1),
    (1, 0, -1),
    (-1, 0, 1),
    (0, 1, 1),
    (0, -1, -1),
    (0, 1, -1),
    (0, -1, 1),
)
WEIGHTS = (1.0 / 3.0,) + (1.0 / 18.0,) * 6 + (1.0 / 36.0,) * 12
OPPOSITE = (0, 2, 1, 4, 3, 6, 5, 8, 7, 10, 9, 12, 11, 14, 13, 16, 15, 18, 17)
RELAX_RATE = 1.0 / 0.6
DIFFUSIVITY = 0.12


def extended_2(cells, sides, width):
    for axis, dim in sides:
        count = lax.axis_size(axis)
        head = lax.slice_in_dim(cells, 0, width, axis=dim)
        tail = lax.slice_in_dim(cells, cells.shape[dim] - width, cells.shape[dim], axis=dim)
        cells = jnp.concatenate(
            [
                lax.ppermute(tail, axis, [(i, (i + 1) % count) for i in range(count)]),
                cells,
                lax.ppermute(head, axis, [((i + 1) % count, i) for i in range(count)]),
            ],
            axis=dim,
        )
    return cells


def moments(populations):
    density = jnp.sum(populations, axis=0)
    velocity = []
    for dimension in range(3):
        forward = [populations[which] for which in range(19) if VELOCITIES[which][dimension] == 1]
        backward = [populations[which] for which in range(19) if VELOCITIES[which][dimension] == -1]
        velocity.append((sum(forward) - sum(backward)) / density)
    return (density, velocity)


def plane_moments(populations):
    density = sum(populations[1:], populations[0])
    velocity = []
    for dimension in range(3):
        forward = [populations[which] for which in range(19) if VELOCITIES[which][dimension] == 1]
        backward = [populations[which] for which in range(19) if VELOCITIES[which][dimension] == -1]
        velocity.append((sum(forward) - sum(backward)) / density)
    return (density, velocity)


def step_kernel(
    with_moments, strength_ref, inner_ref, low_ref, high_ref, rows_ref, discs_ref, solid_ref, *rest
):
    if with_moments:
        out_ref, velocity_ref, flow_ref, posts_ref = rest
    else:
        out_ref, posts_ref = rest
    fans = discs_ref.shape[0]
    slab_len, band_width, height = out_ref.shape[1:]

    def collide_into(populations, index, rows):
        density, velocity = plane_moments(populations)
        force_field = strength_ref[0] * discs_ref[0, index, rows]
        for fan_number in range(1, fans):
            force_field = force_field + strength_ref[fan_number] * discs_ref[fan_number, index, rows]
        solid_flag = solid_ref[index, rows] != 0.0
        speed_sq = velocity[0] * velocity[0] + velocity[1] * velocity[1] + velocity[2] * velocity[2]
        for which in range(19):
            shift_x, shift_y, shift_z = VELOCITIES[which]
            along = shift_x * velocity[0] + shift_y * velocity[1] + shift_z * velocity[2]
            balance = (
                WEIGHTS[which] * density * (1.0 + 3.0 * along + 4.5 * along * along - 1.5 * speed_sq)
            )
            relaxed = populations[which] - RELAX_RATE * (populations[which] - balance)
            if shift_x != 0:
                relaxed = relaxed + 3.0 * WEIGHTS[which] * shift_x * force_field
            posts_ref[which, index, rows] = jnp.where(
                solid_flag, populations[OPPOSITE[which]], relaxed
            )

    inner = slice(0, band_width)
    rim = slice(band_width, band_width + 2)
    collide_into([low_ref[which, 0] for which in range(19)], 0, inner)
    collide_into([high_ref[which, 0] for which in range(19)], slab_len + 1, inner)

    def collide_plane(index, carry):
        collide_into([inner_ref[which, index - 1] for which in range(19)], index, inner)
        return carry

    lax.fori_loop(1, slab_len + 1, collide_plane, 0)

    def collide_rim(index, carry):
        collide_into([rows_ref[which, index] for which in range(19)], index, rim)
        return carry

    lax.fori_loop(0, slab_len + 2, collide_rim, 0)
    lane = lax.broadcasted_iota(jnp.int32, (slab_len, band_width, height), 2)
    row = lax.broadcasted_iota(jnp.int32, (slab_len, band_width, height), 1)
    for which in range(19):
        shift_x, shift_y, shift_z = VELOCITIES[which]
        planes = slice(1 - shift_x, 1 - shift_x + slab_len)
        piece = posts_ref[which, planes, 0:band_width, :]
        if shift_y == 1:
            rim_row = posts_ref[which, planes, band_width : band_width + 1, :]
            piece = jnp.where(row == 0, rim_row, pltpu.roll(piece, 1, 1))
        elif shift_y == -1:
            rim_row = posts_ref[which, planes, band_width + 1 : band_width + 2, :]
            piece = jnp.where(row == band_width - 1, rim_row, pltpu.roll(piece, band_width - 1, 1))
        if shift_z == 1:
            piece = jnp.where(lane == 0, 0.0, pltpu.roll(piece, 1, 2))
        elif shift_z == -1:
            piece = jnp.where(lane == height - 1, 0.0, pltpu.roll(piece, height - 1, 2))
        out_ref[which] = piece
    if not with_moments:
        return
    moments_into(out_ref, discs_ref, 1, velocity_ref, flow_ref)


def moments_into(populations_ref, discs_ref, rim, velocity_ref, flow_ref):
    fans = discs_ref.shape[0]
    band_width = populations_ref.shape[2]
    flow_ref[...] = jnp.zeros(flow_ref.shape, jnp.float32)

    def moment_plane(index, carry):
        density, velocity = plane_moments([populations_ref[which, index] for which in range(19)])
        for dimension in range(3):
            velocity_ref[dimension, index] = velocity[dimension]
        for fan_number in range(fans):
            flow_ref[fan_number] += (
                discs_ref[fan_number, index + rim, 0:band_width, :] * velocity[0]
            )
        return carry

    lax.fori_loop(0, populations_ref.shape[1], moment_plane, 0)


def first_moments(populations, discs):
    fans, slab_len, band_width, height = discs.shape
    vmem = pl.BlockSpec(memory_space=pltpu.VMEM)
    return pl.pallas_call(
        lambda populations_ref, discs_ref, velocity_ref, flow_ref: moments_into(
            populations_ref, discs_ref, 0, velocity_ref, flow_ref
        ),
        out_shape=(
            jax.ShapeDtypeStruct((3, slab_len, band_width, height), jnp.float32),
            jax.ShapeDtypeStruct((fans, band_width, height), jnp.float32),
        ),
        in_specs=[vmem, vmem],
        out_specs=(vmem, vmem),
        cost_estimate=pl.CostEstimate(
            flops=60 * discs[0].size, transcendentals=0, bytes_accessed=4 * populations.size
        ),
    )(populations, discs)


def lattice_step(strength, inner, low, high, rows, discs, solid_rim, with_moments):
    slab_len = inner.shape[1]
    band_width = inner.shape[2]
    height = inner.shape[3]
    fans = discs.shape[0]
    out_shape = [jax.ShapeDtypeStruct((19, slab_len, band_width, height), jnp.float32)]
    if with_moments:
        out_shape.append(jax.ShapeDtypeStruct((3, slab_len, band_width, height), jnp.float32))
        out_shape.append(jax.ShapeDtypeStruct((fans, band_width, height), jnp.float32))
    vmem = pl.BlockSpec(memory_space=pltpu.VMEM)
    return pl.pallas_call(
        functools.partial(step_kernel, with_moments),
        out_shape=tuple(out_shape),
        in_specs=[pl.BlockSpec(memory_space=pltpu.SMEM)] + [vmem] * 6,
        out_specs=tuple([vmem] * len(out_shape)),
        scratch_shapes=[
            pltpu.VMEM((19, slab_len + 2, band_width + 2, height), jnp.float32)
        ],
        cost_estimate=pl.CostEstimate(
            flops=300 * solid_rim.size, transcendentals=0, bytes_accessed=12 * inner.size
        ),
    )(strength, inner, low, high, rows, discs, solid_rim)


def disc_count():
    inside = 0
    for offset_a in range(-RAD, RAD + 1):
        for offset_b in range(-RAD, RAD + 1):
            if offset_a * offset_a + offset_b * offset_b <= RAD * RAD:
                inside = inside + 1
    return FAN_LEN * inside


def fan_discs(fan_hubs, coord_x, coord_y, coord_z, length_total):
    discs = []
    for fan_number in range(fan_hubs.shape[0]):
        offset_x = jnp.mod(coord_x - fan_hubs[fan_number, 0], length_total)
        offset_y = coord_y - fan_hubs[fan_number, 1]
        offset_z = coord_z - fan_hubs[fan_number, 2]
        discs.append(
            (offset_x < FAN_LEN) & (offset_y * offset_y + offset_z * offset_z <= RAD * RAD)
        )
    return discs


def partial_flow(discs, velocity, solid_flag):
    return jnp.stack(
        [
            jnp.sum(jnp.where(disc_nodes & jnp.logical_not(solid_flag), velocity[0], 0.0))
            for disc_nodes in discs
        ]
    )


def force_from(discs, totals, fan_gain, jet_speed):
    strength = fan_gain * (jet_speed - totals / float(disc_count()))
    force_field = jnp.zeros(discs[0].shape, jnp.float32)
    for fan_number in range(len(discs)):
        force_field = force_field + jnp.where(discs[fan_number], strength[fan_number], 0.0)
    return force_field


def advance(center, ahead_x, behind_x, ahead_y, behind_y, ahead_z, behind_z, velocity, solid_flag):
    laplace = ahead_x + behind_x + ahead_y + behind_y + ahead_z + behind_z - 6.0 * center
    advect = 0.5 * (
        velocity[0] * (ahead_x - behind_x)
        + velocity[1] * (ahead_y - behind_y)
        + velocity[2] * (ahead_z - behind_z)
    )
    return jnp.where(solid_flag, 0.0, center + DIFFUSIVITY * laplace - advect)


def shift_height(field, shift_z):
    if shift_z == 0:
        return field
    zero_layer = jnp.zeros(field.shape[:-1] + (1,), field.dtype)
    if shift_z == 1:
        return jnp.concatenate([zero_layer, field[..., :-1]], axis=-1)
    return jnp.concatenate([field[..., 1:], zero_layer], axis=-1)


def rim_round(fields, flow, axis, dim, reach):
    count = lax.axis_size(axis)
    fans = flow.shape[0]
    channels = [field.shape[0] for field in fields]

    def piece(start):
        cells = [lax.slice_in_dim(field, start, start + 1, axis=dim) for field in fields]
        carrier = jnp.zeros(cells[0].shape[1:], jnp.float32).at[0, 0, :fans].set(flow)[None]
        return jnp.concatenate(cells + [carrier], axis=0)

    head = piece(0)
    tail = piece(fields[0].shape[dim] - 1)
    forward = [(i, (i + 1) % count) for i in range(count)]
    backward = [((i + 1) % count, i) for i in range(count)]
    if count == 2:
        both = lax.ppermute(jnp.concatenate([tail, head], axis=0), axis, forward)
        from_left = both[: tail.shape[0]]
        from_right = both[tail.shape[0] :]
        total = flow + from_left[-1, 0, 0, :fans]
    else:
        from_left = lax.ppermute(tail, axis, forward)
        from_right = lax.ppermute(head, axis, backward)
        total = flow + from_left[-1, 0, 0, :fans] + from_right[-1, 0, 0, :fans]
    for offset in sorted(set(step % count for step in range(-reach, reach + 1)) - {0, 1, count - 1}):
        total = total + lax.ppermute(flow, axis, [(i, (i + offset) % count) for i in range(count)])
    extended = [(from_left[0 : channels[0]], from_right[0 : channels[0]])]
    first = channels[0]
    for field, channel in zip(fields[1:], channels[1:]):
        left = from_left[first : first + channel]
        right = from_right[first : first + channel]
        if dim == 1:
            extended.append(jnp.concatenate([left, field, right], axis=dim))
        else:
            extended.append(jnp.concatenate([field, left, right], axis=dim))
        first = first + channel
    return (extended, total)


def window_sum(values, axis, width):
    count = lax.axis_size(axis)
    total = values
    for offset in sorted(set(step % count for step in range(-width, width + 1)) - {0}):
        total = total + lax.ppermute(
            values, axis, [(i, (i + offset) % count) for i in range(count)]
        )
    return total


def source_release(sources, source_rate, offset_len, offset_band, slab_len, band_width, height):
    local_x = sources[:, 0] - offset_len
    local_y = sources[:, 1] - offset_band
    pick_x = (local_x[:, None] == jnp.arange(slab_len, dtype=jnp.int32)[None, :]).astype(
        jnp.float32
    )
    pick_y = (local_y[:, None] == jnp.arange(band_width, dtype=jnp.int32)[None, :]).astype(
        jnp.float32
    )
    pick_z = (sources[:, 2][:, None] == jnp.arange(height, dtype=jnp.int32)[None, :]).astype(
        jnp.float32
    )
    weighted = source_rate[:, None] * pick_x
    cross_table = (pick_y[:, :, None] * pick_z[:, None, :]).reshape(
        sources.shape[0], band_width * height
    )
    released = jnp.dot(
        weighted.T, cross_table, precision=lax.Precision.HIGHEST, preferred_element_type=jnp.float32
    )
    return released.reshape(slab_len, band_width, height)


def body(populations, solid_mask, smoke_field, fan_hubs, fan_gain, jet_speed, sources, source_rate):
    slab_len = populations.shape[1]
    band_width = populations.shape[2]
    height = populations.shape[3]
    offset_len = lax.axis_index("len") * slab_len
    offset_band = lax.axis_index("band") * band_width
    length_total = slab_len * lax.axis_size("len")
    breadth_total = band_width * lax.axis_size("band")
    solid_flag = solid_mask == 1
    coord_x = offset_len - 1 + jnp.arange(slab_len + 2, dtype=jnp.int32)
    coord_y = jnp.mod(
        offset_band
        + jnp.concatenate(
            [jnp.arange(band_width, dtype=jnp.int32), jnp.array([-1, band_width], jnp.int32)]
        ),
        breadth_total,
    )
    coord_z = jnp.arange(height, dtype=jnp.int32)
    along_in = jnp.mod(coord_x[None, :] - fan_hubs[:, 0:1], length_total) < FAN_LEN
    offset_y = coord_y[None, :] - fan_hubs[:, 1:2]
    offset_z = coord_z[None, :] - fan_hubs[:, 2:3]
    across_in = (
        offset_y[:, :, None] * offset_y[:, :, None] + offset_z[:, None, :] * offset_z[:, None, :]
        <= RAD * RAD
    )
    released = source_release(
        sources, source_rate, offset_len, offset_band, slab_len, band_width, height
    )
    len_reach = max(-(-FAN_LEN // slab_len), (slab_len + FAN_LEN - 1) // slab_len)
    band_reach = max(-(-(2 * RAD + 1) // band_width), (band_width + 2 * RAD) // band_width)
    inner_discs = (
        along_in[:, 1:-1, None, None]
        & across_in[:, None, 0:band_width]
        & jnp.logical_not(solid_flag)[None]
    ).astype(jnp.float32)
    velocity, flow = first_moments(populations, inner_discs)
    partials = jnp.sum(flow, axis=(1, 2))
    for repeat in range(ITERS):
        fields = [populations, smoke_field[None]]
        if repeat == 0:
            fields.append(solid_flag.astype(jnp.float32)[None])
        fields, totals = rim_round(fields, partials, "len", 1, len_reach)
        low, high = fields[0]
        fields[0] = jnp.concatenate([low, populations, high], axis=1)
        fields, totals = rim_round(fields, totals, "band", 2, band_reach)
        rows = jnp.concatenate(fields[0], axis=2)
        rimmed = fields[1][0]
        if repeat == 0:
            solid_rim = fields[2][0]
            air_rim = solid_rim == 0.0
            discs = (along_in[:, :, None, None] & across_in[:, None] & air_rim[None]).astype(
                jnp.float32
            )
        strength = fan_gain * (jet_speed - totals / float(disc_count()))
        last = repeat == ITERS - 1
        stepped = lattice_step(strength, populations, low, high, rows, discs, solid_rim, not last)
        ahead_x = rimmed[2:, 0:band_width]
        behind_x = rimmed[:-2, 0:band_width]
        ahead_y = jnp.concatenate(
            [rimmed[1:-1, 1:band_width], rimmed[1:-1, band_width + 1 : band_width + 2]], axis=1
        )
        behind_y = jnp.concatenate(
            [rimmed[1:-1, band_width : band_width + 1], rimmed[1:-1, 0 : band_width - 1]], axis=1
        )
        smoke_field = advance(
            smoke_field,
            ahead_x,
            behind_x,
            ahead_y,
            behind_y,
            shift_height(smoke_field, -1),
            shift_height(smoke_field, 1),
            velocity,
            solid_flag,
        )
        smoke_field = smoke_field + released
        populations = stepped[0]
        if not last:
            velocity = stepped[1]
            partials = jnp.sum(stepped[2], axis=(1, 2))
    return (populations, smoke_field)


def solution(mesh):
    placed = (
        P(None, "len", "band", None),
        P("len", "band", None),
        P("len", "band", None),
        P(),
        P(),
        P(),
        P(),
        P(),
    )
    return jax.shard_map(
        body,
        mesh=mesh,
        in_specs=placed,
        out_specs=(P(None, "len", "band", None), P("len", "band", None)),
        check_vma=False,
    )
```

```python
import functools

import jax
import jax.numpy as jnp
from jax import lax
from jax.experimental import pallas as pl
from jax.experimental.pallas import tpu as pltpu
from jax.sharding import PartitionSpec as P

RAD = 3
FAN_LEN = 16
ITERS = 3


VELOCITIES = (
    (0, 0, 0),
    (1, 0, 0),
    (-1, 0, 0),
    (0, 1, 0),
    (0, -1, 0),
    (0, 0, 1),
    (0, 0, -1),
    (1, 1, 0),
    (-1, -1, 0),
    (1, -1, 0),
    (-1, 1, 0),
    (1, 0, 1),
    (-1, 0, -1),
    (1, 0, -1),
    (-1, 0, 1),
    (0, 1, 1),
    (0, -1, -1),
    (0, 1, -1),
    (0, -1, 1),
)
WEIGHTS = (1.0 / 3.0,) + (1.0 / 18.0,) * 6 + (1.0 / 36.0,) * 12
OPPOSITE = (0, 2, 1, 4, 3, 6, 5, 8, 7, 10, 9, 12, 11, 14, 13, 16, 15, 18, 17)
RELAX_RATE = 1.0 / 0.6
DIFFUSIVITY = 0.12


def extended_2(cells, sides, width):
    for axis, dim in sides:
        count = lax.axis_size(axis)
        head = lax.slice_in_dim(cells, 0, width, axis=dim)
        tail = lax.slice_in_dim(cells, cells.shape[dim] - width, cells.shape[dim], axis=dim)
        cells = jnp.concatenate(
            [
                lax.ppermute(tail, axis, [(i, (i + 1) % count) for i in range(count)]),
                cells,
                lax.ppermute(head, axis, [((i + 1) % count, i) for i in range(count)]),
            ],
            axis=dim,
        )
    return cells


def moments(populations):
    density = jnp.sum(populations, axis=0)
    velocity = []
    for dimension in range(3):
        forward = [populations[which] for which in range(19) if VELOCITIES[which][dimension] == 1]
        backward = [populations[which] for which in range(19) if VELOCITIES[which][dimension] == -1]
        velocity.append((sum(forward) - sum(backward)) / density)
    return (density, velocity)


def plane_moments(populations):
    density = sum(populations[1:], populations[0])
    velocity = []
    for dimension in range(3):
        forward = [populations[which] for which in range(19) if VELOCITIES[which][dimension] == 1]
        backward = [populations[which] for which in range(19) if VELOCITIES[which][dimension] == -1]
        velocity.append((sum(forward) - sum(backward)) / density)
    return (density, velocity)


def step_kernel(
    with_moments, strength_ref, inner_ref, low_ref, high_ref, rows_ref, discs_ref, solid_ref, *rest
):
    if with_moments:
        out_ref, velocity_ref, flow_ref, posts_ref = rest
    else:
        out_ref, posts_ref = rest
    fans = discs_ref.shape[0]
    slab_len, band_width, height = out_ref.shape[1:]

    def collide_into(populations, index, rows):
        density, velocity = plane_moments(populations)
        force_field = strength_ref[0] * discs_ref[0, index, rows]
        for fan_number in range(1, fans):
            force_field = force_field + strength_ref[fan_number] * discs_ref[fan_number, index, rows]
        solid_flag = solid_ref[index, rows] != 0.0
        speed_sq = velocity[0] * velocity[0] + velocity[1] * velocity[1] + velocity[2] * velocity[2]
        for which in range(19):
            shift_x, shift_y, shift_z = VELOCITIES[which]
            along = shift_x * velocity[0] + shift_y * velocity[1] + shift_z * velocity[2]
            balance = (
                WEIGHTS[which] * density * (1.0 + 3.0 * along + 4.5 * along * along - 1.5 * speed_sq)
            )
            relaxed = populations[which] - RELAX_RATE * (populations[which] - balance)
            if shift_x != 0:
                relaxed = relaxed + 3.0 * WEIGHTS[which] * shift_x * force_field
            posts_ref[which, index, rows] = jnp.where(
                solid_flag, populations[OPPOSITE[which]], relaxed
            )

    inner = slice(0, band_width)
    rim = slice(band_width, band_width + 2)
    collide_into([low_ref[which, 0] for which in range(19)], 0, inner)
    collide_into([high_ref[which, 0] for which in range(19)], slab_len + 1, inner)

    def collide_plane(index, carry):
        collide_into([inner_ref[which, index - 1] for which in range(19)], index, inner)
        return carry

    lax.fori_loop(1, slab_len + 1, collide_plane, 0)

    def collide_rim(index, carry):
        collide_into([rows_ref[which, index] for which in range(19)], index, rim)
        return carry

    lax.fori_loop(0, slab_len + 2, collide_rim, 0)
    lane = lax.broadcasted_iota(jnp.int32, (slab_len, band_width, height), 2)
    row = lax.broadcasted_iota(jnp.int32, (slab_len, band_width, height), 1)
    for which in range(19):
        shift_x, shift_y, shift_z = VELOCITIES[which]
        planes = slice(1 - shift_x, 1 - shift_x + slab_len)
        piece = posts_ref[which, planes, 0:band_width, :]
        if shift_y == 1:
            rim_row = posts_ref[which, planes, band_width : band_width + 1, :]
            piece = jnp.where(row == 0, rim_row, pltpu.roll(piece, 1, 1))
        elif shift_y == -1:
            rim_row = posts_ref[which, planes, band_width + 1 : band_width + 2, :]
            piece = jnp.where(row == band_width - 1, rim_row, pltpu.roll(piece, band_width - 1, 1))
        if shift_z == 1:
            piece = jnp.where(lane == 0, 0.0, pltpu.roll(piece, 1, 2))
        elif shift_z == -1:
            piece = jnp.where(lane == height - 1, 0.0, pltpu.roll(piece, height - 1, 2))
        out_ref[which] = piece
    if not with_moments:
        return
    moments_into(out_ref, discs_ref, 1, velocity_ref, flow_ref)


def moments_into(populations_ref, discs_ref, rim, velocity_ref, flow_ref):
    fans = discs_ref.shape[0]
    band_width = populations_ref.shape[2]
    flow_ref[...] = jnp.zeros(flow_ref.shape, jnp.float32)

    def moment_plane(index, carry):
        density, velocity = plane_moments([populations_ref[which, index] for which in range(19)])
        for dimension in range(3):
            velocity_ref[dimension, index] = velocity[dimension]
        for fan_number in range(fans):
            flow_ref[fan_number] += (
                discs_ref[fan_number, index + rim, 0:band_width, :] * velocity[0]
            )
        return carry

    lax.fori_loop(0, populations_ref.shape[1], moment_plane, 0)


def first_moments(populations, discs):
    fans, slab_len, band_width, height = discs.shape
    vmem = pl.BlockSpec(memory_space=pltpu.VMEM)
    return pl.pallas_call(
        lambda populations_ref, discs_ref, velocity_ref, flow_ref: moments_into(
            populations_ref, discs_ref, 0, velocity_ref, flow_ref
        ),
        out_shape=(
            jax.ShapeDtypeStruct((3, slab_len, band_width, height), jnp.float32),
            jax.ShapeDtypeStruct((fans, band_width, height), jnp.float32),
        ),
        in_specs=[vmem, vmem],
        out_specs=(vmem, vmem),
        cost_estimate=pl.CostEstimate(
            flops=60 * discs[0].size, transcendentals=0, bytes_accessed=4 * populations.size
        ),
    )(populations, discs)


def lattice_step(strength, inner, low, high, rows, discs, solid_rim, with_moments):
    slab_len = inner.shape[1]
    band_width = inner.shape[2]
    height = inner.shape[3]
    fans = discs.shape[0]
    out_shape = [jax.ShapeDtypeStruct((19, slab_len, band_width, height), jnp.float32)]
    if with_moments:
        out_shape.append(jax.ShapeDtypeStruct((3, slab_len, band_width, height), jnp.float32))
        out_shape.append(jax.ShapeDtypeStruct((fans, band_width, height), jnp.float32))
    vmem = pl.BlockSpec(memory_space=pltpu.VMEM)
    return pl.pallas_call(
        functools.partial(step_kernel, with_moments),
        out_shape=tuple(out_shape),
        in_specs=[pl.BlockSpec(memory_space=pltpu.SMEM)] + [vmem] * 6,
        out_specs=tuple([vmem] * len(out_shape)),
        scratch_shapes=[
            pltpu.VMEM((19, slab_len + 2, band_width + 2, height), jnp.float32)
        ],
        cost_estimate=pl.CostEstimate(
            flops=300 * solid_rim.size, transcendentals=0, bytes_accessed=12 * inner.size
        ),
    )(strength, inner, low, high, rows, discs, solid_rim)


def disc_count():
    inside = 0
    for offset_a in range(-RAD, RAD + 1):
        for offset_b in range(-RAD, RAD + 1):
            if offset_a * offset_a + offset_b * offset_b <= RAD * RAD:
                inside = inside + 1
    return FAN_LEN * inside


def fan_discs(fan_hubs, coord_x, coord_y, coord_z, length_total):
    discs = []
    for fan_number in range(fan_hubs.shape[0]):
        offset_x = jnp.mod(coord_x - fan_hubs[fan_number, 0], length_total)
        offset_y = coord_y - fan_hubs[fan_number, 1]
        offset_z = coord_z - fan_hubs[fan_number, 2]
        discs.append(
            (offset_x < FAN_LEN) & (offset_y * offset_y + offset_z * offset_z <= RAD * RAD)
        )
    return discs


def partial_flow(discs, velocity, solid_flag):
    return jnp.stack(
        [
            jnp.sum(jnp.where(disc_nodes & jnp.logical_not(solid_flag), velocity[0], 0.0))
            for disc_nodes in discs
        ]
    )


def force_from(discs, totals, fan_gain, jet_speed):
    strength = fan_gain * (jet_speed - totals / float(disc_count()))
    force_field = jnp.zeros(discs[0].shape, jnp.float32)
    for fan_number in range(len(discs)):
        force_field = force_field + jnp.where(discs[fan_number], strength[fan_number], 0.0)
    return force_field


def advance(center, ahead_x, behind_x, ahead_y, behind_y, ahead_z, behind_z, velocity, solid_flag):
    laplace = ahead_x + behind_x + ahead_y + behind_y + ahead_z + behind_z - 6.0 * center
    advect = 0.5 * (
        velocity[0] * (ahead_x - behind_x)
        + velocity[1] * (ahead_y - behind_y)
        + velocity[2] * (ahead_z - behind_z)
    )
    return jnp.where(solid_flag, 0.0, center + DIFFUSIVITY * laplace - advect)


def shift_height(field, shift_z):
    if shift_z == 0:
        return field
    zero_layer = jnp.zeros(field.shape[:-1] + (1,), field.dtype)
    if shift_z == 1:
        return jnp.concatenate([zero_layer, field[..., :-1]], axis=-1)
    return jnp.concatenate([field[..., 1:], zero_layer], axis=-1)


def rim_round(fields, flow, axis, dim, reach):
    count = lax.axis_size(axis)
    fans = flow.shape[0]
    channels = [field.shape[0] for field in fields]

    def piece(start):
        cells = [lax.slice_in_dim(field, start, start + 1, axis=dim) for field in fields]
        carrier = jnp.zeros(cells[0].shape[1:], jnp.float32).at[0, 0, :fans].set(flow)[None]
        return jnp.concatenate(cells + [carrier], axis=0)

    head = piece(0)
    tail = piece(fields[0].shape[dim] - 1)
    forward = [(i, (i + 1) % count) for i in range(count)]
    backward = [((i + 1) % count, i) for i in range(count)]
    both = None
    if count == 2:
        both = lax.ppermute(jnp.concatenate([tail, head], axis=dim), axis, forward)
        from_left = lax.slice_in_dim(both, 0, 1, axis=dim)
        from_right = lax.slice_in_dim(both, 1, 2, axis=dim)
        total = flow + from_left[-1, 0, 0, :fans]
    else:
        from_left = lax.ppermute(tail, axis, forward)
        from_right = lax.ppermute(head, axis, backward)
        total = flow + from_left[-1, 0, 0, :fans] + from_right[-1, 0, 0, :fans]
    for offset in sorted(set(step % count for step in range(-reach, reach + 1)) - {0, 1, count - 1}):
        total = total + lax.ppermute(flow, axis, [(i, (i + offset) % count) for i in range(count)])
    pair = None if both is None else both[0 : channels[0]]
    extended = [(from_left[0 : channels[0]], from_right[0 : channels[0]], pair)]
    first = channels[0]
    for field, channel in zip(fields[1:], channels[1:]):
        left = from_left[first : first + channel]
        right = from_right[first : first + channel]
        if dim == 1:
            extended.append(jnp.concatenate([left, field, right], axis=dim))
        else:
            extended.append(jnp.concatenate([field, left, right], axis=dim))
        first = first + channel
    return (extended, total)


def window_sum(values, axis, width):
    count = lax.axis_size(axis)
    total = values
    for offset in sorted(set(step % count for step in range(-width, width + 1)) - {0}):
        total = total + lax.ppermute(
            values, axis, [(i, (i + offset) % count) for i in range(count)]
        )
    return total


def source_release(sources, source_rate, offset_len, offset_band, slab_len, band_width, height):
    local_x = sources[:, 0] - offset_len
    local_y = sources[:, 1] - offset_band
    pick_x = (local_x[:, None] == jnp.arange(slab_len, dtype=jnp.int32)[None, :]).astype(
        jnp.float32
    )
    pick_y = (local_y[:, None] == jnp.arange(band_width, dtype=jnp.int32)[None, :]).astype(
        jnp.float32
    )
    pick_z = (sources[:, 2][:, None] == jnp.arange(height, dtype=jnp.int32)[None, :]).astype(
        jnp.float32
    )
    weighted = source_rate[:, None] * pick_x
    cross_table = (pick_y[:, :, None] * pick_z[:, None, :]).reshape(
        sources.shape[0], band_width * height
    )
    released = jnp.dot(
        weighted.T, cross_table, precision=lax.Precision.HIGHEST, preferred_element_type=jnp.float32
    )
    return released.reshape(slab_len, band_width, height)


def body(populations, solid_mask, smoke_field, fan_hubs, fan_gain, jet_speed, sources, source_rate):
    slab_len = populations.shape[1]
    band_width = populations.shape[2]
    height = populations.shape[3]
    offset_len = lax.axis_index("len") * slab_len
    offset_band = lax.axis_index("band") * band_width
    length_total = slab_len * lax.axis_size("len")
    breadth_total = band_width * lax.axis_size("band")
    solid_flag = solid_mask == 1
    coord_x = offset_len - 1 + jnp.arange(slab_len + 2, dtype=jnp.int32)
    coord_y = jnp.mod(
        offset_band
        + jnp.concatenate(
            [jnp.arange(band_width, dtype=jnp.int32), jnp.array([-1, band_width], jnp.int32)]
        ),
        breadth_total,
    )
    coord_z = jnp.arange(height, dtype=jnp.int32)
    along_in = jnp.mod(coord_x[None, :] - fan_hubs[:, 0:1], length_total) < FAN_LEN
    offset_y = coord_y[None, :] - fan_hubs[:, 1:2]
    offset_z = coord_z[None, :] - fan_hubs[:, 2:3]
    across_in = (
        offset_y[:, :, None] * offset_y[:, :, None] + offset_z[:, None, :] * offset_z[:, None, :]
        <= RAD * RAD
    )
    released = source_release(
        sources, source_rate, offset_len, offset_band, slab_len, band_width, height
    )
    len_reach = max(-(-FAN_LEN // slab_len), (slab_len + FAN_LEN - 1) // slab_len)
    band_reach = max(-(-(2 * RAD + 1) // band_width), (band_width + 2 * RAD) // band_width)
    inner_discs = (
        along_in[:, 1:-1, None, None]
        & across_in[:, None, 0:band_width]
        & jnp.logical_not(solid_flag)[None]
    ).astype(jnp.float32)
    velocity, flow = first_moments(populations, inner_discs)
    partials = jnp.sum(flow, axis=(1, 2))
    for repeat in range(ITERS):
        fields = [populations, smoke_field[None]]
        if repeat == 0:
            fields.append(solid_flag.astype(jnp.float32)[None])
        fields, totals = rim_round(fields, partials, "len", 1, len_reach)
        low, high, _ = fields[0]
        fields[0] = jnp.concatenate([low, populations, high], axis=1)
        fields, totals = rim_round(fields, totals, "band", 2, band_reach)
        if fields[0][2] is None:
            rows = jnp.concatenate(fields[0][:2], axis=2)
        else:
            rows = fields[0][2]
        rimmed = fields[1][0]
        if repeat == 0:
            solid_rim = fields[2][0]
            air_rim = solid_rim == 0.0
            discs = (along_in[:, :, None, None] & across_in[:, None] & air_rim[None]).astype(
                jnp.float32
            )
        strength = fan_gain * (jet_speed - totals / float(disc_count()))
        last = repeat == ITERS - 1
        stepped = lattice_step(strength, populations, low, high, rows, discs, solid_rim, not last)
        ahead_x = rimmed[2:, 0:band_width]
        behind_x = rimmed[:-2, 0:band_width]
        ahead_y = jnp.concatenate(
            [rimmed[1:-1, 1:band_width], rimmed[1:-1, band_width + 1 : band_width + 2]], axis=1
        )
        behind_y = jnp.concatenate(
            [rimmed[1:-1, band_width : band_width + 1], rimmed[1:-1, 0 : band_width - 1]], axis=1
        )
        smoke_field = advance(
            smoke_field,
            ahead_x,
            behind_x,
            ahead_y,
            behind_y,
            shift_height(smoke_field, -1),
            shift_height(smoke_field, 1),
            velocity,
            solid_flag,
        )
        smoke_field = smoke_field + released
        populations = stepped[0]
        if not last:
            velocity = stepped[1]
            partials = jnp.sum(stepped[2], axis=(1, 2))
    return (populations, smoke_field)


def solution(mesh):
    placed = (
        P(None, "len", "band", None),
        P("len", "band", None),
        P("len", "band", None),
        P(),
        P(),
        P(),
        P(),
        P(),
    )
    return jax.shard_map(
        body,
        mesh=mesh,
        in_specs=placed,
        out_specs=(P(None, "len", "band", None), P("len", "band", None)),
        check_vma=False,
    )
```

```python
import functools

import jax
import jax.numpy as jnp
from jax import lax
from jax.experimental import pallas as pl
from jax.experimental.pallas import tpu as pltpu
from jax.sharding import PartitionSpec as P

RAD = 3
FAN_LEN = 16
ITERS = 3


VELOCITIES = (
    (0, 0, 0),
    (1, 0, 0),
    (-1, 0, 0),
    (0, 1, 0),
    (0, -1, 0),
    (0, 0, 1),
    (0, 0, -1),
    (1, 1, 0),
    (-1, -1, 0),
    (1, -1, 0),
    (-1, 1, 0),
    (1, 0, 1),
    (-1, 0, -1),
    (1, 0, -1),
    (-1, 0, 1),
    (0, 1, 1),
    (0, -1, -1),
    (0, 1, -1),
    (0, -1, 1),
)
WEIGHTS = (1.0 / 3.0,) + (1.0 / 18.0,) * 6 + (1.0 / 36.0,) * 12
OPPOSITE = (0, 2, 1, 4, 3, 6, 5, 8, 7, 10, 9, 12, 11, 14, 13, 16, 15, 18, 17)
RELAX_RATE = 1.0 / 0.6
DIFFUSIVITY = 0.12


def extended_2(cells, sides, width):
    for axis, dim in sides:
        count = lax.axis_size(axis)
        head = lax.slice_in_dim(cells, 0, width, axis=dim)
        tail = lax.slice_in_dim(cells, cells.shape[dim] - width, cells.shape[dim], axis=dim)
        cells = jnp.concatenate(
            [
                lax.ppermute(tail, axis, [(i, (i + 1) % count) for i in range(count)]),
                cells,
                lax.ppermute(head, axis, [((i + 1) % count, i) for i in range(count)]),
            ],
            axis=dim,
        )
    return cells


def moments(populations):
    density = jnp.sum(populations, axis=0)
    velocity = []
    for dimension in range(3):
        forward = [populations[which] for which in range(19) if VELOCITIES[which][dimension] == 1]
        backward = [populations[which] for which in range(19) if VELOCITIES[which][dimension] == -1]
        velocity.append((sum(forward) - sum(backward)) / density)
    return (density, velocity)


def plane_moments(populations):
    density = sum(populations[1:], populations[0])
    velocity = []
    for dimension in range(3):
        forward = [populations[which] for which in range(19) if VELOCITIES[which][dimension] == 1]
        backward = [populations[which] for which in range(19) if VELOCITIES[which][dimension] == -1]
        velocity.append((sum(forward) - sum(backward)) / density)
    return (density, velocity)


def step_kernel(
    with_moments, strength_ref, inner_ref, low_ref, high_ref, rows_ref, discs_ref, solid_ref, *rest
):
    if with_moments:
        out_ref, velocity_ref, flow_ref, posts_ref = rest
    else:
        out_ref, posts_ref = rest
    fans = discs_ref.shape[0]
    slab_len, band_width, height = out_ref.shape[1:]

    def collide_into(populations, index, rows):
        density, velocity = plane_moments(populations)
        force_field = strength_ref[0] * discs_ref[0, index, rows]
        for fan_number in range(1, fans):
            force_field = force_field + strength_ref[fan_number] * discs_ref[fan_number, index, rows]
        solid_flag = solid_ref[index, rows] != 0.0
        speed_sq = velocity[0] * velocity[0] + velocity[1] * velocity[1] + velocity[2] * velocity[2]
        for which in range(19):
            shift_x, shift_y, shift_z = VELOCITIES[which]
            along = shift_x * velocity[0] + shift_y * velocity[1] + shift_z * velocity[2]
            balance = (
                WEIGHTS[which] * density * (1.0 + 3.0 * along + 4.5 * along * along - 1.5 * speed_sq)
            )
            relaxed = populations[which] - RELAX_RATE * (populations[which] - balance)
            if shift_x != 0:
                relaxed = relaxed + 3.0 * WEIGHTS[which] * shift_x * force_field
            posts_ref[which, index, rows] = jnp.where(
                solid_flag, populations[OPPOSITE[which]], relaxed
            )

    inner = slice(0, band_width)
    rim = slice(band_width, band_width + 2)
    collide_into([low_ref[which, 0] for which in range(19)], 0, inner)
    collide_into([high_ref[which, 0] for which in range(19)], slab_len + 1, inner)

    def collide_plane(index, carry):
        collide_into([inner_ref[which, index - 1] for which in range(19)], index, inner)
        return carry

    lax.fori_loop(1, slab_len + 1, collide_plane, 0)

    def collide_rim(index, carry):
        collide_into([rows_ref[which, index] for which in range(19)], index, rim)
        return carry

    lax.fori_loop(0, slab_len + 2, collide_rim, 0)
    lane = lax.broadcasted_iota(jnp.int32, (slab_len, band_width, height), 2)
    row = lax.broadcasted_iota(jnp.int32, (slab_len, band_width, height), 1)
    for which in range(19):
        shift_x, shift_y, shift_z = VELOCITIES[which]
        planes = slice(1 - shift_x, 1 - shift_x + slab_len)
        piece = posts_ref[which, planes, 0:band_width, :]
        if shift_y == 1:
            rim_row = posts_ref[which, planes, band_width : band_width + 1, :]
            piece = jnp.where(row == 0, rim_row, pltpu.roll(piece, 1, 1))
        elif shift_y == -1:
            rim_row = posts_ref[which, planes, band_width + 1 : band_width + 2, :]
            piece = jnp.where(row == band_width - 1, rim_row, pltpu.roll(piece, band_width - 1, 1))
        if shift_z == 1:
            piece = jnp.where(lane == 0, 0.0, pltpu.roll(piece, 1, 2))
        elif shift_z == -1:
            piece = jnp.where(lane == height - 1, 0.0, pltpu.roll(piece, height - 1, 2))
        out_ref[which] = piece
    if not with_moments:
        return
    moments_into(out_ref, discs_ref, 1, velocity_ref, flow_ref)


def moments_into(populations_ref, discs_ref, rim, velocity_ref, flow_ref):
    fans = discs_ref.shape[0]
    band_width = populations_ref.shape[2]
    flow_ref[...] = jnp.zeros(flow_ref.shape, jnp.float32)

    def moment_plane(index, carry):
        density, velocity = plane_moments([populations_ref[which, index] for which in range(19)])
        for dimension in range(3):
            velocity_ref[dimension, index] = velocity[dimension]
        for fan_number in range(fans):
            flow_ref[fan_number] += (
                discs_ref[fan_number, index + rim, 0:band_width, :] * velocity[0]
            )
        return carry

    lax.fori_loop(0, populations_ref.shape[1], moment_plane, 0)


def first_moments(populations, discs):
    fans, slab_len, band_width, height = discs.shape
    vmem = pl.BlockSpec(memory_space=pltpu.VMEM)
    return pl.pallas_call(
        lambda populations_ref, discs_ref, velocity_ref, flow_ref: moments_into(
            populations_ref, discs_ref, 0, velocity_ref, flow_ref
        ),
        out_shape=(
            jax.ShapeDtypeStruct((3, slab_len, band_width, height), jnp.float32),
            jax.ShapeDtypeStruct((fans, band_width, height), jnp.float32),
        ),
        in_specs=[vmem, vmem],
        out_specs=(vmem, vmem),
        cost_estimate=pl.CostEstimate(
            flops=60 * discs[0].size, transcendentals=0, bytes_accessed=4 * populations.size
        ),
    )(populations, discs)


def lattice_step(strength, inner, low, high, rows, discs, solid_rim, with_moments):
    slab_len = inner.shape[1]
    band_width = inner.shape[2]
    height = inner.shape[3]
    fans = discs.shape[0]
    out_shape = [jax.ShapeDtypeStruct((19, slab_len, band_width, height), jnp.float32)]
    if with_moments:
        out_shape.append(jax.ShapeDtypeStruct((3, slab_len, band_width, height), jnp.float32))
        out_shape.append(jax.ShapeDtypeStruct((fans, band_width, height), jnp.float32))
    vmem = pl.BlockSpec(memory_space=pltpu.VMEM)
    return pl.pallas_call(
        functools.partial(step_kernel, with_moments),
        out_shape=tuple(out_shape),
        in_specs=[pl.BlockSpec(memory_space=pltpu.SMEM)] + [vmem] * 6,
        out_specs=tuple([vmem] * len(out_shape)),
        scratch_shapes=[
            pltpu.VMEM((19, slab_len + 2, band_width + 2, height), jnp.float32)
        ],
        cost_estimate=pl.CostEstimate(
            flops=300 * solid_rim.size, transcendentals=0, bytes_accessed=12 * inner.size
        ),
    )(strength, inner, low, high, rows, discs, solid_rim)


def disc_count():
    inside = 0
    for offset_a in range(-RAD, RAD + 1):
        for offset_b in range(-RAD, RAD + 1):
            if offset_a * offset_a + offset_b * offset_b <= RAD * RAD:
                inside = inside + 1
    return FAN_LEN * inside


def fan_discs(fan_hubs, coord_x, coord_y, coord_z, length_total):
    discs = []
    for fan_number in range(fan_hubs.shape[0]):
        offset_x = jnp.mod(coord_x - fan_hubs[fan_number, 0], length_total)
        offset_y = coord_y - fan_hubs[fan_number, 1]
        offset_z = coord_z - fan_hubs[fan_number, 2]
        discs.append(
            (offset_x < FAN_LEN) & (offset_y * offset_y + offset_z * offset_z <= RAD * RAD)
        )
    return discs


def partial_flow(discs, velocity, solid_flag):
    return jnp.stack(
        [
            jnp.sum(jnp.where(disc_nodes & jnp.logical_not(solid_flag), velocity[0], 0.0))
            for disc_nodes in discs
        ]
    )


def force_from(discs, totals, fan_gain, jet_speed):
    strength = fan_gain * (jet_speed - totals / float(disc_count()))
    force_field = jnp.zeros(discs[0].shape, jnp.float32)
    for fan_number in range(len(discs)):
        force_field = force_field + jnp.where(discs[fan_number], strength[fan_number], 0.0)
    return force_field


def advance(center, ahead_x, behind_x, ahead_y, behind_y, ahead_z, behind_z, velocity, solid_flag):
    laplace = ahead_x + behind_x + ahead_y + behind_y + ahead_z + behind_z - 6.0 * center
    advect = 0.5 * (
        velocity[0] * (ahead_x - behind_x)
        + velocity[1] * (ahead_y - behind_y)
        + velocity[2] * (ahead_z - behind_z)
    )
    return jnp.where(solid_flag, 0.0, center + DIFFUSIVITY * laplace - advect)


def shift_height(field, shift_z):
    if shift_z == 0:
        return field
    zero_layer = jnp.zeros(field.shape[:-1] + (1,), field.dtype)
    if shift_z == 1:
        return jnp.concatenate([zero_layer, field[..., :-1]], axis=-1)
    return jnp.concatenate([field[..., 1:], zero_layer], axis=-1)


def rim_round(fields, flow, axis, dim, reach):
    count = lax.axis_size(axis)
    fans = flow.shape[0]
    channels = [field.shape[0] for field in fields]

    def piece(start):
        cells = [lax.slice_in_dim(field, start, start + 1, axis=dim) for field in fields]
        carrier = jnp.zeros(cells[0].shape[1:], jnp.float32).at[0, 0, :fans].set(flow)[None]
        return jnp.concatenate(cells + [carrier], axis=0)

    head = piece(0)
    tail = piece(fields[0].shape[dim] - 1)
    forward = [(i, (i + 1) % count) for i in range(count)]
    backward = [((i + 1) % count, i) for i in range(count)]
    both = None
    if count == 2:
        both = lax.ppermute(jnp.concatenate([tail, head], axis=dim), axis, forward)
        from_left = lax.slice_in_dim(both, 0, 1, axis=dim)
        from_right = lax.slice_in_dim(both, 1, 2, axis=dim)
        total = flow + from_left[-1, 0, 0, :fans]
    else:
        from_left = lax.ppermute(tail, axis, forward)
        from_right = lax.ppermute(head, axis, backward)
        total = flow + from_left[-1, 0, 0, :fans] + from_right[-1, 0, 0, :fans]
    for offset in sorted(set(step % count for step in range(-reach, reach + 1)) - {0, 1, count - 1}):
        total = total + lax.ppermute(flow, axis, [(i, (i + offset) % count) for i in range(count)])
    extended = [(from_left, from_right, both)]
    first = channels[0]
    for field, channel in zip(fields[1:], channels[1:]):
        left = from_left[first : first + channel]
        right = from_right[first : first + channel]
        if dim == 1:
            extended.append(jnp.concatenate([left, field, right], axis=dim))
        else:
            extended.append(jnp.concatenate([field, left, right], axis=dim))
        first = first + channel
    return (extended, total)


def window_sum(values, axis, width):
    count = lax.axis_size(axis)
    total = values
    for offset in sorted(set(step % count for step in range(-width, width + 1)) - {0}):
        total = total + lax.ppermute(
            values, axis, [(i, (i + offset) % count) for i in range(count)]
        )
    return total


def source_release(sources, source_rate, offset_len, offset_band, slab_len, band_width, height):
    local_x = sources[:, 0] - offset_len
    local_y = sources[:, 1] - offset_band
    pick_x = (local_x[:, None] == jnp.arange(slab_len, dtype=jnp.int32)[None, :]).astype(
        jnp.float32
    )
    pick_y = (local_y[:, None] == jnp.arange(band_width, dtype=jnp.int32)[None, :]).astype(
        jnp.float32
    )
    pick_z = (sources[:, 2][:, None] == jnp.arange(height, dtype=jnp.int32)[None, :]).astype(
        jnp.float32
    )
    weighted = source_rate[:, None] * pick_x
    cross_table = (pick_y[:, :, None] * pick_z[:, None, :]).reshape(
        sources.shape[0], band_width * height
    )
    released = jnp.dot(
        weighted.T, cross_table, precision=lax.Precision.HIGHEST, preferred_element_type=jnp.float32
    )
    return released.reshape(slab_len, band_width, height)


def body(populations, solid_mask, smoke_field, fan_hubs, fan_gain, jet_speed, sources, source_rate):
    slab_len = populations.shape[1]
    band_width = populations.shape[2]
    height = populations.shape[3]
    offset_len = lax.axis_index("len") * slab_len
    offset_band = lax.axis_index("band") * band_width
    length_total = slab_len * lax.axis_size("len")
    breadth_total = band_width * lax.axis_size("band")
    solid_flag = solid_mask == 1
    coord_x = offset_len - 1 + jnp.arange(slab_len + 2, dtype=jnp.int32)
    coord_y = jnp.mod(
        offset_band
        + jnp.concatenate(
            [jnp.arange(band_width, dtype=jnp.int32), jnp.array([-1, band_width], jnp.int32)]
        ),
        breadth_total,
    )
    coord_z = jnp.arange(height, dtype=jnp.int32)
    along_in = jnp.mod(coord_x[None, :] - fan_hubs[:, 0:1], length_total) < FAN_LEN
    offset_y = coord_y[None, :] - fan_hubs[:, 1:2]
    offset_z = coord_z[None, :] - fan_hubs[:, 2:3]
    across_in = (
        offset_y[:, :, None] * offset_y[:, :, None] + offset_z[:, None, :] * offset_z[:, None, :]
        <= RAD * RAD
    )
    released = source_release(
        sources, source_rate, offset_len, offset_band, slab_len, band_width, height
    )
    len_reach = max(-(-FAN_LEN // slab_len), (slab_len + FAN_LEN - 1) // slab_len)
    band_reach = max(-(-(2 * RAD + 1) // band_width), (band_width + 2 * RAD) // band_width)
    inner_discs = (
        along_in[:, 1:-1, None, None]
        & across_in[:, None, 0:band_width]
        & jnp.logical_not(solid_flag)[None]
    ).astype(jnp.float32)
    velocity, flow = first_moments(populations, inner_discs)
    partials = jnp.sum(flow, axis=(1, 2))
    for repeat in range(ITERS):
        fields = [populations, smoke_field[None]]
        if repeat == 0:
            fields.append(solid_flag.astype(jnp.float32)[None])
        fields, totals = rim_round(fields, partials, "len", 1, len_reach)
        low, high, _ = fields[0]
        fields[0] = jnp.concatenate([low[:19], populations, high[:19]], axis=1)
        fields, totals = rim_round(fields, totals, "band", 2, band_reach)
        if fields[0][2] is None:
            rows = jnp.concatenate([fields[0][0][:19], fields[0][1][:19]], axis=2)
        else:
            rows = fields[0][2]
        rimmed = fields[1][0]
        if repeat == 0:
            solid_rim = fields[2][0]
            air_rim = solid_rim == 0.0
            discs = (along_in[:, :, None, None] & across_in[:, None] & air_rim[None]).astype(
                jnp.float32
            )
        strength = fan_gain * (jet_speed - totals / float(disc_count()))
        last = repeat == ITERS - 1
        stepped = lattice_step(strength, populations, low, high, rows, discs, solid_rim, not last)
        ahead_x = rimmed[2:, 0:band_width]
        behind_x = rimmed[:-2, 0:band_width]
        ahead_y = jnp.concatenate(
            [rimmed[1:-1, 1:band_width], rimmed[1:-1, band_width + 1 : band_width + 2]], axis=1
        )
        behind_y = jnp.concatenate(
            [rimmed[1:-1, band_width : band_width + 1], rimmed[1:-1, 0 : band_width - 1]], axis=1
        )
        smoke_field = advance(
            smoke_field,
            ahead_x,
            behind_x,
            ahead_y,
            behind_y,
            shift_height(smoke_field, -1),
            shift_height(smoke_field, 1),
            velocity,
            solid_flag,
        )
        smoke_field = smoke_field + released
        populations = stepped[0]
        if not last:
            velocity = stepped[1]
            partials = jnp.sum(stepped[2], axis=(1, 2))
    return (populations, smoke_field)


def solution(mesh):
    placed = (
        P(None, "len", "band", None),
        P("len", "band", None),
        P("len", "band", None),
        P(),
        P(),
        P(),
        P(),
        P(),
    )
    return jax.shard_map(
        body,
        mesh=mesh,
        in_specs=placed,
        out_specs=(P(None, "len", "band", None), P("len", "band", None)),
        check_vma=False,
    )
```

```python
import functools

import jax
import jax.numpy as jnp
from jax import lax
from jax.experimental import pallas as pl
from jax.experimental.pallas import tpu as pltpu
from jax.sharding import PartitionSpec as P

RAD = 3
FAN_LEN = 16
ITERS = 3


VELOCITIES = (
    (0, 0, 0),
    (1, 0, 0),
    (-1, 0, 0),
    (0, 1, 0),
    (0, -1, 0),
    (0, 0, 1),
    (0, 0, -1),
    (1, 1, 0),
    (-1, -1, 0),
    (1, -1, 0),
    (-1, 1, 0),
    (1, 0, 1),
    (-1, 0, -1),
    (1, 0, -1),
    (-1, 0, 1),
    (0, 1, 1),
    (0, -1, -1),
    (0, 1, -1),
    (0, -1, 1),
)
WEIGHTS = (1.0 / 3.0,) + (1.0 / 18.0,) * 6 + (1.0 / 36.0,) * 12
OPPOSITE = (0, 2, 1, 4, 3, 6, 5, 8, 7, 10, 9, 12, 11, 14, 13, 16, 15, 18, 17)
RELAX_RATE = 1.0 / 0.6
DIFFUSIVITY = 0.12


def extended_2(cells, sides, width):
    for axis, dim in sides:
        count = lax.axis_size(axis)
        head = lax.slice_in_dim(cells, 0, width, axis=dim)
        tail = lax.slice_in_dim(cells, cells.shape[dim] - width, cells.shape[dim], axis=dim)
        cells = jnp.concatenate(
            [
                lax.ppermute(tail, axis, [(i, (i + 1) % count) for i in range(count)]),
                cells,
                lax.ppermute(head, axis, [((i + 1) % count, i) for i in range(count)]),
            ],
            axis=dim,
        )
    return cells


def moments(populations):
    density = jnp.sum(populations, axis=0)
    velocity = []
    for dimension in range(3):
        forward = [populations[which] for which in range(19) if VELOCITIES[which][dimension] == 1]
        backward = [populations[which] for which in range(19) if VELOCITIES[which][dimension] == -1]
        velocity.append((sum(forward) - sum(backward)) / density)
    return (density, velocity)


def plane_moments(populations):
    density = sum(populations[1:], populations[0])
    velocity = []
    for dimension in range(3):
        forward = [populations[which] for which in range(19) if VELOCITIES[which][dimension] == 1]
        backward = [populations[which] for which in range(19) if VELOCITIES[which][dimension] == -1]
        velocity.append((sum(forward) - sum(backward)) / density)
    return (density, velocity)


def step_kernel(
    with_moments, strength_ref, inner_ref, low_ref, high_ref, rows_ref, discs_ref, solid_ref, *rest
):
    if with_moments:
        out_ref, velocity_ref, flow_ref, posts_ref, sums_ref = rest
    else:
        out_ref, posts_ref = rest
    fans = discs_ref.shape[0]
    slab_len, band_width, height = out_ref.shape[1:]

    def collide_into(populations, index, rows):
        density, velocity = plane_moments(populations)
        force_field = strength_ref[0] * discs_ref[0, index, rows]
        for fan_number in range(1, fans):
            force_field = force_field + strength_ref[fan_number] * discs_ref[fan_number, index, rows]
        solid_flag = solid_ref[index, rows] != 0.0
        speed_sq = velocity[0] * velocity[0] + velocity[1] * velocity[1] + velocity[2] * velocity[2]
        for which in range(19):
            shift_x, shift_y, shift_z = VELOCITIES[which]
            along = shift_x * velocity[0] + shift_y * velocity[1] + shift_z * velocity[2]
            balance = (
                WEIGHTS[which] * density * (1.0 + 3.0 * along + 4.5 * along * along - 1.5 * speed_sq)
            )
            relaxed = populations[which] - RELAX_RATE * (populations[which] - balance)
            if shift_x != 0:
                relaxed = relaxed + 3.0 * WEIGHTS[which] * shift_x * force_field
            posts_ref[which, index, rows] = jnp.where(
                solid_flag, populations[OPPOSITE[which]], relaxed
            )

    inner = slice(0, band_width)
    rim = slice(band_width, band_width + 2)
    collide_into([low_ref[which, 0] for which in range(19)], 0, inner)
    collide_into([high_ref[which, 0] for which in range(19)], slab_len + 1, inner)

    def collide_plane(index, carry):
        collide_into([inner_ref[which, index - 1] for which in range(19)], index, inner)
        return carry

    lax.fori_loop(1, slab_len + 1, collide_plane, 0)

    def collide_rim(index, carry):
        collide_into([rows_ref[which, index] for which in range(19)], index, rim)
        return carry

    lax.fori_loop(0, slab_len + 2, collide_rim, 0)
    lane = lax.broadcasted_iota(jnp.int32, (slab_len, band_width, height), 2)
    row = lax.broadcasted_iota(jnp.int32, (slab_len, band_width, height), 1)
    for which in range(19):
        shift_x, shift_y, shift_z = VELOCITIES[which]
        planes = slice(1 - shift_x, 1 - shift_x + slab_len)
        piece = posts_ref[which, planes, 0:band_width, :]
        if shift_y == 1:
            rim_row = posts_ref[which, planes, band_width : band_width + 1, :]
            piece = jnp.where(row == 0, rim_row, pltpu.roll(piece, 1, 1))
        elif shift_y == -1:
            rim_row = posts_ref[which, planes, band_width + 1 : band_width + 2, :]
            piece = jnp.where(row == band_width - 1, rim_row, pltpu.roll(piece, band_width - 1, 1))
        if shift_z == 1:
            piece = jnp.where(lane == 0, 0.0, pltpu.roll(piece, 1, 2))
        elif shift_z == -1:
            piece = jnp.where(lane == height - 1, 0.0, pltpu.roll(piece, height - 1, 2))
        out_ref[which] = piece
    if not with_moments:
        return
    moments_into(out_ref, discs_ref, 1, velocity_ref, flow_ref, sums_ref)


def moments_into(populations_ref, discs_ref, rim, velocity_ref, flow_ref, sums_ref):
    fans = discs_ref.shape[0]
    band_width = populations_ref.shape[2]
    sums_ref[...] = jnp.zeros(sums_ref.shape, jnp.float32)

    def moment_plane(index, carry):
        density, velocity = plane_moments([populations_ref[which, index] for which in range(19)])
        for dimension in range(3):
            velocity_ref[dimension, index] = velocity[dimension]
        for fan_number in range(fans):
            sums_ref[fan_number] += (
                discs_ref[fan_number, index + rim, 0:band_width, :] * velocity[0]
            )
        return carry

    lax.fori_loop(0, populations_ref.shape[1], moment_plane, 0)
    for fan_number in range(fans):
        flow_ref[fan_number : fan_number + 1, :] = jnp.broadcast_to(
            jnp.sum(sums_ref[fan_number], axis=(0, 1), keepdims=True), (1, flow_ref.shape[1])
        )


def first_moments(populations, discs):
    fans, slab_len, band_width, height = discs.shape
    vmem = pl.BlockSpec(memory_space=pltpu.VMEM)
    return pl.pallas_call(
        lambda populations_ref, discs_ref, velocity_ref, flow_ref, sums_ref: moments_into(
            populations_ref, discs_ref, 0, velocity_ref, flow_ref, sums_ref
        ),
        out_shape=(
            jax.ShapeDtypeStruct((3, slab_len, band_width, height), jnp.float32),
            jax.ShapeDtypeStruct((fans, height), jnp.float32),
        ),
        in_specs=[vmem, vmem],
        out_specs=(vmem, vmem),
        scratch_shapes=[pltpu.VMEM((fans, band_width, height), jnp.float32)],
        cost_estimate=pl.CostEstimate(
            flops=60 * discs[0].size, transcendentals=0, bytes_accessed=4 * populations.size
        ),
    )(populations, discs)


def lattice_step(strength, inner, low, high, rows, discs, solid_rim, with_moments):
    slab_len = inner.shape[1]
    band_width = inner.shape[2]
    height = inner.shape[3]
    fans = discs.shape[0]
    out_shape = [jax.ShapeDtypeStruct((19, slab_len, band_width, height), jnp.float32)]
    if with_moments:
        out_shape.append(jax.ShapeDtypeStruct((3, slab_len, band_width, height), jnp.float32))
        out_shape.append(jax.ShapeDtypeStruct((fans, height), jnp.float32))
    scratch = [pltpu.VMEM((19, slab_len + 2, band_width + 2, height), jnp.float32)]
    if with_moments:
        scratch.append(pltpu.VMEM((fans, band_width, height), jnp.float32))
    vmem = pl.BlockSpec(memory_space=pltpu.VMEM)
    return pl.pallas_call(
        functools.partial(step_kernel, with_moments),
        out_shape=tuple(out_shape),
        in_specs=[pl.BlockSpec(memory_space=pltpu.SMEM)] + [vmem] * 6,
        out_specs=tuple([vmem] * len(out_shape)),
        scratch_shapes=scratch,
        cost_estimate=pl.CostEstimate(
            flops=300 * solid_rim.size, transcendentals=0, bytes_accessed=12 * inner.size
        ),
    )(strength, inner, low, high, rows, discs, solid_rim)


def disc_count():
    inside = 0
    for offset_a in range(-RAD, RAD + 1):
        for offset_b in range(-RAD, RAD + 1):
            if offset_a * offset_a + offset_b * offset_b <= RAD * RAD:
                inside = inside + 1
    return FAN_LEN * inside


def fan_discs(fan_hubs, coord_x, coord_y, coord_z, length_total):
    discs = []
    for fan_number in range(fan_hubs.shape[0]):
        offset_x = jnp.mod(coord_x - fan_hubs[fan_number, 0], length_total)
        offset_y = coord_y - fan_hubs[fan_number, 1]
        offset_z = coord_z - fan_hubs[fan_number, 2]
        discs.append(
            (offset_x < FAN_LEN) & (offset_y * offset_y + offset_z * offset_z <= RAD * RAD)
        )
    return discs


def partial_flow(discs, velocity, solid_flag):
    return jnp.stack(
        [
            jnp.sum(jnp.where(disc_nodes & jnp.logical_not(solid_flag), velocity[0], 0.0))
            for disc_nodes in discs
        ]
    )


def force_from(discs, totals, fan_gain, jet_speed):
    strength = fan_gain * (jet_speed - totals / float(disc_count()))
    force_field = jnp.zeros(discs[0].shape, jnp.float32)
    for fan_number in range(len(discs)):
        force_field = force_field + jnp.where(discs[fan_number], strength[fan_number], 0.0)
    return force_field


def advance(center, ahead_x, behind_x, ahead_y, behind_y, ahead_z, behind_z, velocity, solid_flag):
    laplace = ahead_x + behind_x + ahead_y + behind_y + ahead_z + behind_z - 6.0 * center
    advect = 0.5 * (
        velocity[0] * (ahead_x - behind_x)
        + velocity[1] * (ahead_y - behind_y)
        + velocity[2] * (ahead_z - behind_z)
    )
    return jnp.where(solid_flag, 0.0, center + DIFFUSIVITY * laplace - advect)


def shift_height(field, shift_z):
    if shift_z == 0:
        return field
    zero_layer = jnp.zeros(field.shape[:-1] + (1,), field.dtype)
    if shift_z == 1:
        return jnp.concatenate([zero_layer, field[..., :-1]], axis=-1)
    return jnp.concatenate([field[..., 1:], zero_layer], axis=-1)


def rim_round(fields, flow, axis, dim, reach):
    count = lax.axis_size(axis)
    fans = flow.shape[0]
    channels = [field.shape[0] for field in fields]

    def piece(start):
        cells = [lax.slice_in_dim(field, start, start + 1, axis=dim) for field in fields]
        carrier = jnp.zeros(cells[0].shape[1:], jnp.float32).at[0, 0, :fans].set(flow)[None]
        return jnp.concatenate(cells + [carrier], axis=0)

    head = piece(0)
    tail = piece(fields[0].shape[dim] - 1)
    forward = [(i, (i + 1) % count) for i in range(count)]
    backward = [((i + 1) % count, i) for i in range(count)]
    both = None
    if count == 2:
        both = lax.ppermute(jnp.concatenate([tail, head], axis=dim), axis, forward)
        from_left = lax.slice_in_dim(both, 0, 1, axis=dim)
        from_right = lax.slice_in_dim(both, 1, 2, axis=dim)
        total = flow + from_left[-1, 0, 0, :fans]
    else:
        from_left = lax.ppermute(tail, axis, forward)
        from_right = lax.ppermute(head, axis, backward)
        total = flow + from_left[-1, 0, 0, :fans] + from_right[-1, 0, 0, :fans]
    for offset in sorted(set(step % count for step in range(-reach, reach + 1)) - {0, 1, count - 1}):
        total = total + lax.ppermute(flow, axis, [(i, (i + offset) % count) for i in range(count)])
    extended = [(from_left, from_right, both)]
    first = channels[0]
    for field, channel in zip(fields[1:], channels[1:]):
        left = from_left[first : first + channel]
        right = from_right[first : first + channel]
        if dim == 1:
            extended.append(jnp.concatenate([left, field, right], axis=dim))
        else:
            extended.append(jnp.concatenate([field, left, right], axis=dim))
        first = first + channel
    return (extended, total)


def window_sum(values, axis, width):
    count = lax.axis_size(axis)
    total = values
    for offset in sorted(set(step % count for step in range(-width, width + 1)) - {0}):
        total = total + lax.ppermute(
            values, axis, [(i, (i + offset) % count) for i in range(count)]
        )
    return total


def source_release(sources, source_rate, offset_len, offset_band, slab_len, band_width, height):
    local_x = sources[:, 0] - offset_len
    local_y = sources[:, 1] - offset_band
    pick_x = (local_x[:, None] == jnp.arange(slab_len, dtype=jnp.int32)[None, :]).astype(
        jnp.float32
    )
    pick_y = (local_y[:, None] == jnp.arange(band_width, dtype=jnp.int32)[None, :]).astype(
        jnp.float32
    )
    pick_z = (sources[:, 2][:, None] == jnp.arange(height, dtype=jnp.int32)[None, :]).astype(
        jnp.float32
    )
    weighted = source_rate[:, None] * pick_x
    cross_table = (pick_y[:, :, None] * pick_z[:, None, :]).reshape(
        sources.shape[0], band_width * height
    )
    released = jnp.dot(
        weighted.T, cross_table, precision=lax.Precision.HIGHEST, preferred_element_type=jnp.float32
    )
    return released.reshape(slab_len, band_width, height)


def body(populations, solid_mask, smoke_field, fan_hubs, fan_gain, jet_speed, sources, source_rate):
    slab_len = populations.shape[1]
    band_width = populations.shape[2]
    height = populations.shape[3]
    offset_len = lax.axis_index("len") * slab_len
    offset_band = lax.axis_index("band") * band_width
    length_total = slab_len * lax.axis_size("len")
    breadth_total = band_width * lax.axis_size("band")
    solid_flag = solid_mask == 1
    coord_x = offset_len - 1 + jnp.arange(slab_len + 2, dtype=jnp.int32)
    coord_y = jnp.mod(
        offset_band
        + jnp.concatenate(
            [jnp.arange(band_width, dtype=jnp.int32), jnp.array([-1, band_width], jnp.int32)]
        ),
        breadth_total,
    )
    coord_z = jnp.arange(height, dtype=jnp.int32)
    along_in = jnp.mod(coord_x[None, :] - fan_hubs[:, 0:1], length_total) < FAN_LEN
    offset_y = coord_y[None, :] - fan_hubs[:, 1:2]
    offset_z = coord_z[None, :] - fan_hubs[:, 2:3]
    across_in = (
        offset_y[:, :, None] * offset_y[:, :, None] + offset_z[:, None, :] * offset_z[:, None, :]
        <= RAD * RAD
    )
    released = source_release(
        sources, source_rate, offset_len, offset_band, slab_len, band_width, height
    )
    len_reach = max(-(-FAN_LEN // slab_len), (slab_len + FAN_LEN - 1) // slab_len)
    band_reach = max(-(-(2 * RAD + 1) // band_width), (band_width + 2 * RAD) // band_width)
    inner_discs = (
        along_in[:, 1:-1, None, None]
        & across_in[:, None, 0:band_width]
        & jnp.logical_not(solid_flag)[None]
    ).astype(jnp.float32)
    velocity, flow = first_moments(populations, inner_discs)
    partials = flow[:, 0]
    for repeat in range(ITERS):
        fields = [populations, smoke_field[None]]
        if repeat == 0:
            fields.append(solid_flag.astype(jnp.float32)[None])
        fields, totals = rim_round(fields, partials, "len", 1, len_reach)
        low, high, _ = fields[0]
        fields[0] = jnp.concatenate([low[:19], populations, high[:19]], axis=1)
        fields, totals = rim_round(fields, totals, "band", 2, band_reach)
        if fields[0][2] is None:
            rows = jnp.concatenate([fields[0][0][:19], fields[0][1][:19]], axis=2)
        else:
            rows = fields[0][2]
        rimmed = fields[1][0]
        if repeat == 0:
            solid_rim = fields[2][0]
            air_rim = solid_rim == 0.0
            discs = (along_in[:, :, None, None] & across_in[:, None] & air_rim[None]).astype(
                jnp.float32
            )
        strength = fan_gain * (jet_speed - totals / float(disc_count()))
        last = repeat == ITERS - 1
        stepped = lattice_step(strength, populations, low, high, rows, discs, solid_rim, not last)
        ahead_x = rimmed[2:, 0:band_width]
        behind_x = rimmed[:-2, 0:band_width]
        ahead_y = jnp.concatenate(
            [rimmed[1:-1, 1:band_width], rimmed[1:-1, band_width + 1 : band_width + 2]], axis=1
        )
        behind_y = jnp.concatenate(
            [rimmed[1:-1, band_width : band_width + 1], rimmed[1:-1, 0 : band_width - 1]], axis=1
        )
        smoke_field = advance(
            smoke_field,
            ahead_x,
            behind_x,
            ahead_y,
            behind_y,
            shift_height(smoke_field, -1),
            shift_height(smoke_field, 1),
            velocity,
            solid_flag,
        )
        smoke_field = smoke_field + released
        populations = stepped[0]
        if not last:
            velocity = stepped[1]
            partials = stepped[2][:, 0]
    return (populations, smoke_field)


def solution(mesh):
    placed = (
        P(None, "len", "band", None),
        P("len", "band", None),
        P("len", "band", None),
        P(),
        P(),
        P(),
        P(),
        P(),
    )
    return jax.shard_map(
        body,
        mesh=mesh,
        in_specs=placed,
        out_specs=(P(None, "len", "band", None), P("len", "band", None)),
        check_vma=False,
    )
```

```python
import functools

import jax
import jax.numpy as jnp
from jax import lax
from jax.experimental import pallas as pl
from jax.experimental.pallas import tpu as pltpu
from jax.sharding import PartitionSpec as P

RAD = 3
FAN_LEN = 16
ITERS = 3


VELOCITIES = (
    (0, 0, 0),
    (1, 0, 0),
    (-1, 0, 0),
    (0, 1, 0),
    (0, -1, 0),
    (0, 0, 1),
    (0, 0, -1),
    (1, 1, 0),
    (-1, -1, 0),
    (1, -1, 0),
    (-1, 1, 0),
    (1, 0, 1),
    (-1, 0, -1),
    (1, 0, -1),
    (-1, 0, 1),
    (0, 1, 1),
    (0, -1, -1),
    (0, 1, -1),
    (0, -1, 1),
)
WEIGHTS = (1.0 / 3.0,) + (1.0 / 18.0,) * 6 + (1.0 / 36.0,) * 12
OPPOSITE = (0, 2, 1, 4, 3, 6, 5, 8, 7, 10, 9, 12, 11, 14, 13, 16, 15, 18, 17)
RELAX_RATE = 1.0 / 0.6
DIFFUSIVITY = 0.12


def extended_2(cells, sides, width):
    for axis, dim in sides:
        count = lax.axis_size(axis)
        head = lax.slice_in_dim(cells, 0, width, axis=dim)
        tail = lax.slice_in_dim(cells, cells.shape[dim] - width, cells.shape[dim], axis=dim)
        cells = jnp.concatenate(
            [
                lax.ppermute(tail, axis, [(i, (i + 1) % count) for i in range(count)]),
                cells,
                lax.ppermute(head, axis, [((i + 1) % count, i) for i in range(count)]),
            ],
            axis=dim,
        )
    return cells


def moments(populations):
    density = jnp.sum(populations, axis=0)
    velocity = []
    for dimension in range(3):
        forward = [populations[which] for which in range(19) if VELOCITIES[which][dimension] == 1]
        backward = [populations[which] for which in range(19) if VELOCITIES[which][dimension] == -1]
        velocity.append((sum(forward) - sum(backward)) / density)
    return (density, velocity)


def plane_moments(populations):
    density = sum(populations[1:], populations[0])
    velocity = []
    for dimension in range(3):
        forward = [populations[which] for which in range(19) if VELOCITIES[which][dimension] == 1]
        backward = [populations[which] for which in range(19) if VELOCITIES[which][dimension] == -1]
        velocity.append((sum(forward) - sum(backward)) / density)
    return (density, velocity)


def step_kernel(
    with_moments, strength_ref, inner_ref, low_ref, high_ref, rows_ref, discs_ref, solid_ref, *rest
):
    if with_moments:
        out_ref, velocity_ref, flow_ref, head_ref, tail_ref, posts_ref, sums_ref = rest
    else:
        out_ref, posts_ref = rest
    fans = discs_ref.shape[0]
    slab_len, band_width, height = out_ref.shape[1:]

    def collide_into(populations, index, rows):
        density, velocity = plane_moments(populations)
        force_field = strength_ref[0] * discs_ref[0, index, rows]
        for fan_number in range(1, fans):
            force_field = force_field + strength_ref[fan_number] * discs_ref[fan_number, index, rows]
        solid_flag = solid_ref[index, rows] != 0.0
        speed_sq = velocity[0] * velocity[0] + velocity[1] * velocity[1] + velocity[2] * velocity[2]
        for which in range(19):
            shift_x, shift_y, shift_z = VELOCITIES[which]
            along = shift_x * velocity[0] + shift_y * velocity[1] + shift_z * velocity[2]
            balance = (
                WEIGHTS[which] * density * (1.0 + 3.0 * along + 4.5 * along * along - 1.5 * speed_sq)
            )
            relaxed = populations[which] - RELAX_RATE * (populations[which] - balance)
            if shift_x != 0:
                relaxed = relaxed + 3.0 * WEIGHTS[which] * shift_x * force_field
            posts_ref[which, index, rows] = jnp.where(
                solid_flag, populations[OPPOSITE[which]], relaxed
            )

    inner = slice(0, band_width)
    rim = slice(band_width, band_width + 2)
    collide_into([low_ref[which, 0] for which in range(19)], 0, inner)
    collide_into([high_ref[which, 0] for which in range(19)], slab_len + 1, inner)

    def collide_plane(index, carry):
        collide_into([inner_ref[which, index - 1] for which in range(19)], index, inner)
        return carry

    lax.fori_loop(1, slab_len + 1, collide_plane, 0)

    def collide_rim(index, carry):
        collide_into([rows_ref[which, index] for which in range(19)], index, rim)
        return carry

    lax.fori_loop(0, slab_len + 2, collide_rim, 0)
    lane = lax.broadcasted_iota(jnp.int32, (slab_len, band_width, height), 2)
    row = lax.broadcasted_iota(jnp.int32, (slab_len, band_width, height), 1)
    for which in range(19):
        shift_x, shift_y, shift_z = VELOCITIES[which]
        planes = slice(1 - shift_x, 1 - shift_x + slab_len)
        piece = posts_ref[which, planes, 0:band_width, :]
        if shift_y == 1:
            rim_row = posts_ref[which, planes, band_width : band_width + 1, :]
            piece = jnp.where(row == 0, rim_row, pltpu.roll(piece, 1, 1))
        elif shift_y == -1:
            rim_row = posts_ref[which, planes, band_width + 1 : band_width + 2, :]
            piece = jnp.where(row == band_width - 1, rim_row, pltpu.roll(piece, band_width - 1, 1))
        if shift_z == 1:
            piece = jnp.where(lane == 0, 0.0, pltpu.roll(piece, 1, 2))
        elif shift_z == -1:
            piece = jnp.where(lane == height - 1, 0.0, pltpu.roll(piece, height - 1, 2))
        out_ref[which] = piece
        if with_moments:
            head_ref[which] = piece[0:1]
            tail_ref[which] = piece[slab_len - 1 : slab_len]
    if not with_moments:
        return
    moments_into(out_ref, discs_ref, 1, velocity_ref, flow_ref, sums_ref)


def moments_into(populations_ref, discs_ref, rim, velocity_ref, flow_ref, sums_ref):
    fans = discs_ref.shape[0]
    band_width = populations_ref.shape[2]
    sums_ref[...] = jnp.zeros(sums_ref.shape, jnp.float32)

    def moment_plane(index, carry):
        density, velocity = plane_moments([populations_ref[which, index] for which in range(19)])
        for dimension in range(3):
            velocity_ref[dimension, index] = velocity[dimension]
        for fan_number in range(fans):
            sums_ref[fan_number] += (
                discs_ref[fan_number, index + rim, 0:band_width, :] * velocity[0]
            )
        return carry

    lax.fori_loop(0, populations_ref.shape[1], moment_plane, 0)
    for fan_number in range(fans):
        flow_ref[fan_number : fan_number + 1, :] = jnp.broadcast_to(
            jnp.sum(sums_ref[fan_number], axis=(0, 1), keepdims=True), (1, flow_ref.shape[1])
        )


def first_moments(populations, discs):
    fans, slab_len, band_width, height = discs.shape
    vmem = pl.BlockSpec(memory_space=pltpu.VMEM)
    return pl.pallas_call(
        lambda populations_ref, discs_ref, velocity_ref, flow_ref, sums_ref: moments_into(
            populations_ref, discs_ref, 0, velocity_ref, flow_ref, sums_ref
        ),
        out_shape=(
            jax.ShapeDtypeStruct((3, slab_len, band_width, height), jnp.float32),
            jax.ShapeDtypeStruct((fans, height), jnp.float32),
        ),
        in_specs=[vmem, vmem],
        out_specs=(vmem, vmem),
        scratch_shapes=[pltpu.VMEM((fans, band_width, height), jnp.float32)],
        cost_estimate=pl.CostEstimate(
            flops=60 * discs[0].size, transcendentals=0, bytes_accessed=4 * populations.size
        ),
    )(populations, discs)


def lattice_step(strength, inner, low, high, rows, discs, solid_rim, with_moments):
    slab_len = inner.shape[1]
    band_width = inner.shape[2]
    height = inner.shape[3]
    fans = discs.shape[0]
    out_shape = [jax.ShapeDtypeStruct((19, slab_len, band_width, height), jnp.float32)]
    if with_moments:
        out_shape.append(jax.ShapeDtypeStruct((3, slab_len, band_width, height), jnp.float32))
        out_shape.append(jax.ShapeDtypeStruct((fans, height), jnp.float32))
        out_shape.append(jax.ShapeDtypeStruct((19, 1, band_width, height), jnp.float32))
        out_shape.append(jax.ShapeDtypeStruct((19, 1, band_width, height), jnp.float32))
    scratch = [pltpu.VMEM((19, slab_len + 2, band_width + 2, height), jnp.float32)]
    if with_moments:
        scratch.append(pltpu.VMEM((fans, band_width, height), jnp.float32))
    vmem = pl.BlockSpec(memory_space=pltpu.VMEM)
    return pl.pallas_call(
        functools.partial(step_kernel, with_moments),
        out_shape=tuple(out_shape),
        in_specs=[pl.BlockSpec(memory_space=pltpu.SMEM)] + [vmem] * 6,
        out_specs=tuple([vmem] * len(out_shape)),
        scratch_shapes=scratch,
        cost_estimate=pl.CostEstimate(
            flops=300 * solid_rim.size, transcendentals=0, bytes_accessed=12 * inner.size
        ),
    )(strength, inner, low, high, rows, discs, solid_rim)


def disc_count():
    inside = 0
    for offset_a in range(-RAD, RAD + 1):
        for offset_b in range(-RAD, RAD + 1):
            if offset_a * offset_a + offset_b * offset_b <= RAD * RAD:
                inside = inside + 1
    return FAN_LEN * inside


def fan_discs(fan_hubs, coord_x, coord_y, coord_z, length_total):
    discs = []
    for fan_number in range(fan_hubs.shape[0]):
        offset_x = jnp.mod(coord_x - fan_hubs[fan_number, 0], length_total)
        offset_y = coord_y - fan_hubs[fan_number, 1]
        offset_z = coord_z - fan_hubs[fan_number, 2]
        discs.append(
            (offset_x < FAN_LEN) & (offset_y * offset_y + offset_z * offset_z <= RAD * RAD)
        )
    return discs


def partial_flow(discs, velocity, solid_flag):
    return jnp.stack(
        [
            jnp.sum(jnp.where(disc_nodes & jnp.logical_not(solid_flag), velocity[0], 0.0))
            for disc_nodes in discs
        ]
    )


def force_from(discs, totals, fan_gain, jet_speed):
    strength = fan_gain * (jet_speed - totals / float(disc_count()))
    force_field = jnp.zeros(discs[0].shape, jnp.float32)
    for fan_number in range(len(discs)):
        force_field = force_field + jnp.where(discs[fan_number], strength[fan_number], 0.0)
    return force_field


def advance(center, ahead_x, behind_x, ahead_y, behind_y, ahead_z, behind_z, velocity, solid_flag):
    laplace = ahead_x + behind_x + ahead_y + behind_y + ahead_z + behind_z - 6.0 * center
    advect = 0.5 * (
        velocity[0] * (ahead_x - behind_x)
        + velocity[1] * (ahead_y - behind_y)
        + velocity[2] * (ahead_z - behind_z)
    )
    return jnp.where(solid_flag, 0.0, center + DIFFUSIVITY * laplace - advect)


def shift_height(field, shift_z):
    if shift_z == 0:
        return field
    zero_layer = jnp.zeros(field.shape[:-1] + (1,), field.dtype)
    if shift_z == 1:
        return jnp.concatenate([zero_layer, field[..., :-1]], axis=-1)
    return jnp.concatenate([field[..., 1:], zero_layer], axis=-1)


def rim_round(fields, flow, axis, dim, reach, edges=None):
    count = lax.axis_size(axis)
    fans = flow.shape[0]
    channels = [field.shape[0] for field in fields]

    def piece(start):
        cells = [lax.slice_in_dim(field, start, start + 1, axis=dim) for field in fields]
        if edges is not None:
            cells[0] = edges[0] if start == 0 else edges[1]
        carrier = jnp.zeros(cells[0].shape[1:], jnp.float32).at[0, 0, :fans].set(flow)[None]
        return jnp.concatenate(cells + [carrier], axis=0)

    head = piece(0)
    tail = piece(fields[0].shape[dim] - 1)
    forward = [(i, (i + 1) % count) for i in range(count)]
    backward = [((i + 1) % count, i) for i in range(count)]
    both = None
    if count == 2:
        both = lax.ppermute(jnp.concatenate([tail, head], axis=dim), axis, forward)
        from_left = lax.slice_in_dim(both, 0, 1, axis=dim)
        from_right = lax.slice_in_dim(both, 1, 2, axis=dim)
        total = flow + from_left[-1, 0, 0, :fans]
    else:
        from_left = lax.ppermute(tail, axis, forward)
        from_right = lax.ppermute(head, axis, backward)
        total = flow + from_left[-1, 0, 0, :fans] + from_right[-1, 0, 0, :fans]
    for offset in sorted(set(step % count for step in range(-reach, reach + 1)) - {0, 1, count - 1}):
        total = total + lax.ppermute(flow, axis, [(i, (i + offset) % count) for i in range(count)])
    extended = [(from_left, from_right, both)]
    first = channels[0]
    for field, channel in zip(fields[1:], channels[1:]):
        left = from_left[first : first + channel]
        right = from_right[first : first + channel]
        if dim == 1:
            extended.append(jnp.concatenate([left, field, right], axis=dim))
        else:
            extended.append(jnp.concatenate([field, left, right], axis=dim))
        first = first + channel
    return (extended, total)


def window_sum(values, axis, width):
    count = lax.axis_size(axis)
    total = values
    for offset in sorted(set(step % count for step in range(-width, width + 1)) - {0}):
        total = total + lax.ppermute(
            values, axis, [(i, (i + offset) % count) for i in range(count)]
        )
    return total


def source_release(sources, source_rate, offset_len, offset_band, slab_len, band_width, height):
    local_x = sources[:, 0] - offset_len
    local_y = sources[:, 1] - offset_band
    pick_x = (local_x[:, None] == jnp.arange(slab_len, dtype=jnp.int32)[None, :]).astype(
        jnp.float32
    )
    pick_y = (local_y[:, None] == jnp.arange(band_width, dtype=jnp.int32)[None, :]).astype(
        jnp.float32
    )
    pick_z = (sources[:, 2][:, None] == jnp.arange(height, dtype=jnp.int32)[None, :]).astype(
        jnp.float32
    )
    weighted = source_rate[:, None] * pick_x
    cross_table = (pick_y[:, :, None] * pick_z[:, None, :]).reshape(
        sources.shape[0], band_width * height
    )
    released = jnp.dot(
        weighted.T, cross_table, precision=lax.Precision.HIGHEST, preferred_element_type=jnp.float32
    )
    return released.reshape(slab_len, band_width, height)


def body(populations, solid_mask, smoke_field, fan_hubs, fan_gain, jet_speed, sources, source_rate):
    slab_len = populations.shape[1]
    band_width = populations.shape[2]
    height = populations.shape[3]
    offset_len = lax.axis_index("len") * slab_len
    offset_band = lax.axis_index("band") * band_width
    length_total = slab_len * lax.axis_size("len")
    breadth_total = band_width * lax.axis_size("band")
    solid_flag = solid_mask == 1
    coord_x = offset_len - 1 + jnp.arange(slab_len + 2, dtype=jnp.int32)
    coord_y = jnp.mod(
        offset_band
        + jnp.concatenate(
            [jnp.arange(band_width, dtype=jnp.int32), jnp.array([-1, band_width], jnp.int32)]
        ),
        breadth_total,
    )
    coord_z = jnp.arange(height, dtype=jnp.int32)
    along_in = jnp.mod(coord_x[None, :] - fan_hubs[:, 0:1], length_total) < FAN_LEN
    offset_y = coord_y[None, :] - fan_hubs[:, 1:2]
    offset_z = coord_z[None, :] - fan_hubs[:, 2:3]
    across_in = (
        offset_y[:, :, None] * offset_y[:, :, None] + offset_z[:, None, :] * offset_z[:, None, :]
        <= RAD * RAD
    )
    released = source_release(
        sources, source_rate, offset_len, offset_band, slab_len, band_width, height
    )
    len_reach = max(-(-FAN_LEN // slab_len), (slab_len + FAN_LEN - 1) // slab_len)
    band_reach = max(-(-(2 * RAD + 1) // band_width), (band_width + 2 * RAD) // band_width)
    inner_discs = (
        along_in[:, 1:-1, None, None]
        & across_in[:, None, 0:band_width]
        & jnp.logical_not(solid_flag)[None]
    ).astype(jnp.float32)
    velocity, flow = first_moments(populations, inner_discs)
    partials = flow[:, 0]
    edges = None
    for repeat in range(ITERS):
        fields = [populations, smoke_field[None]]
        if repeat == 0:
            fields.append(solid_flag.astype(jnp.float32)[None])
        fields, totals = rim_round(fields, partials, "len", 1, len_reach, edges)
        low, high, _ = fields[0]
        fields[0] = jnp.concatenate([low[:19], populations, high[:19]], axis=1)
        fields, totals = rim_round(fields, totals, "band", 2, band_reach)
        if fields[0][2] is None:
            rows = jnp.concatenate([fields[0][0][:19], fields[0][1][:19]], axis=2)
        else:
            rows = fields[0][2]
        rimmed = fields[1][0]
        if repeat == 0:
            solid_rim = fields[2][0]
            air_rim = solid_rim == 0.0
            discs = (along_in[:, :, None, None] & across_in[:, None] & air_rim[None]).astype(
                jnp.float32
            )
        strength = fan_gain * (jet_speed - totals / float(disc_count()))
        last = repeat == ITERS - 1
        stepped = lattice_step(strength, populations, low, high, rows, discs, solid_rim, not last)
        ahead_x = rimmed[2:, 0:band_width]
        behind_x = rimmed[:-2, 0:band_width]
        ahead_y = jnp.concatenate(
            [rimmed[1:-1, 1:band_width], rimmed[1:-1, band_width + 1 : band_width + 2]], axis=1
        )
        behind_y = jnp.concatenate(
            [rimmed[1:-1, band_width : band_width + 1], rimmed[1:-1, 0 : band_width - 1]], axis=1
        )
        smoke_field = advance(
            smoke_field,
            ahead_x,
            behind_x,
            ahead_y,
            behind_y,
            shift_height(smoke_field, -1),
            shift_height(smoke_field, 1),
            velocity,
            solid_flag,
        )
        smoke_field = smoke_field + released
        populations = stepped[0]
        if not last:
            velocity = stepped[1]
            partials = stepped[2][:, 0]
            edges = (stepped[3], stepped[4])
    return (populations, smoke_field)


def solution(mesh):
    placed = (
        P(None, "len", "band", None),
        P("len", "band", None),
        P("len", "band", None),
        P(),
        P(),
        P(),
        P(),
        P(),
    )
    return jax.shard_map(
        body,
        mesh=mesh,
        in_specs=placed,
        out_specs=(P(None, "len", "band", None), P("len", "band", None)),
        check_vma=False,
    )
```

```python
import functools

import jax
import jax.numpy as jnp
from jax import lax
from jax.experimental import pallas as pl
from jax.experimental.pallas import tpu as pltpu
from jax.sharding import PartitionSpec as P

RAD = 3
FAN_LEN = 16
ITERS = 3


VELOCITIES = (
    (0, 0, 0),
    (1, 0, 0),
    (-1, 0, 0),
    (0, 1, 0),
    (0, -1, 0),
    (0, 0, 1),
    (0, 0, -1),
    (1, 1, 0),
    (-1, -1, 0),
    (1, -1, 0),
    (-1, 1, 0),
    (1, 0, 1),
    (-1, 0, -1),
    (1, 0, -1),
    (-1, 0, 1),
    (0, 1, 1),
    (0, -1, -1),
    (0, 1, -1),
    (0, -1, 1),
)
WEIGHTS = (1.0 / 3.0,) + (1.0 / 18.0,) * 6 + (1.0 / 36.0,) * 12
OPPOSITE = (0, 2, 1, 4, 3, 6, 5, 8, 7, 10, 9, 12, 11, 14, 13, 16, 15, 18, 17)
RELAX_RATE = 1.0 / 0.6
DIFFUSIVITY = 0.12


def extended_2(cells, sides, width):
    for axis, dim in sides:
        count = lax.axis_size(axis)
        head = lax.slice_in_dim(cells, 0, width, axis=dim)
        tail = lax.slice_in_dim(cells, cells.shape[dim] - width, cells.shape[dim], axis=dim)
        cells = jnp.concatenate(
            [
                lax.ppermute(tail, axis, [(i, (i + 1) % count) for i in range(count)]),
                cells,
                lax.ppermute(head, axis, [((i + 1) % count, i) for i in range(count)]),
            ],
            axis=dim,
        )
    return cells


def moments(populations):
    density = jnp.sum(populations, axis=0)
    velocity = []
    for dimension in range(3):
        forward = [populations[which] for which in range(19) if VELOCITIES[which][dimension] == 1]
        backward = [populations[which] for which in range(19) if VELOCITIES[which][dimension] == -1]
        velocity.append((sum(forward) - sum(backward)) / density)
    return (density, velocity)


def plane_moments(populations):
    density = sum(populations[1:], populations[0])
    velocity = []
    for dimension in range(3):
        forward = [populations[which] for which in range(19) if VELOCITIES[which][dimension] == 1]
        backward = [populations[which] for which in range(19) if VELOCITIES[which][dimension] == -1]
        velocity.append((sum(forward) - sum(backward)) / density)
    return (density, velocity)


def step_kernel(
    with_moments, strength_ref, inner_ref, low_ref, high_ref, rows_ref, discs_ref, solid_ref, *rest
):
    if with_moments:
        out_ref, velocity_ref, flow_ref, posts_ref, sums_ref = rest
    else:
        out_ref, posts_ref = rest
    fans = discs_ref.shape[0]
    slab_len, band_width, height = out_ref.shape[1:]

    def collide_into(populations, index, rows):
        density, velocity = plane_moments(populations)
        force_field = strength_ref[0] * discs_ref[0, index, rows]
        for fan_number in range(1, fans):
            force_field = force_field + strength_ref[fan_number] * discs_ref[fan_number, index, rows]
        solid_flag = solid_ref[index, rows] != 0.0
        speed_sq = velocity[0] * velocity[0] + velocity[1] * velocity[1] + velocity[2] * velocity[2]
        for which in range(19):
            shift_x, shift_y, shift_z = VELOCITIES[which]
            along = shift_x * velocity[0] + shift_y * velocity[1] + shift_z * velocity[2]
            balance = (
                WEIGHTS[which] * density * (1.0 + 3.0 * along + 4.5 * along * along - 1.5 * speed_sq)
            )
            relaxed = populations[which] - RELAX_RATE * (populations[which] - balance)
            if shift_x != 0:
                relaxed = relaxed + 3.0 * WEIGHTS[which] * shift_x * force_field
            posts_ref[which, index, rows] = jnp.where(
                solid_flag, populations[OPPOSITE[which]], relaxed
            )

    inner = slice(0, band_width)
    rim = slice(band_width, band_width + 2)
    collide_into([low_ref[which, 0] for which in range(19)], 0, inner)
    collide_into([high_ref[which, 0] for which in range(19)], slab_len + 1, inner)

    def collide_plane(index, carry):
        collide_into([inner_ref[which, index - 1] for which in range(19)], index, inner)
        return carry

    lax.fori_loop(1, slab_len + 1, collide_plane, 0)

    def collide_rim(index, carry):
        collide_into([rows_ref[which, index] for which in range(19)], index, rim)
        return carry

    lax.fori_loop(0, slab_len + 2, collide_rim, 0)
    lane = lax.broadcasted_iota(jnp.int32, (slab_len, band_width, height), 2)
    row = lax.broadcasted_iota(jnp.int32, (slab_len, band_width, height), 1)
    for which in range(19):
        shift_x, shift_y, shift_z = VELOCITIES[which]
        planes = slice(1 - shift_x, 1 - shift_x + slab_len)
        piece = posts_ref[which, planes, 0:band_width, :]
        if shift_y == 1:
            rim_row = posts_ref[which, planes, band_width : band_width + 1, :]
            piece = jnp.where(row == 0, rim_row, pltpu.roll(piece, 1, 1))
        elif shift_y == -1:
            rim_row = posts_ref[which, planes, band_width + 1 : band_width + 2, :]
            piece = jnp.where(row == band_width - 1, rim_row, pltpu.roll(piece, band_width - 1, 1))
        if shift_z == 1:
            piece = jnp.where(lane == 0, 0.0, pltpu.roll(piece, 1, 2))
        elif shift_z == -1:
            piece = jnp.where(lane == height - 1, 0.0, pltpu.roll(piece, height - 1, 2))
        out_ref[which] = piece
    if not with_moments:
        return
    moments_into(out_ref, discs_ref, 1, velocity_ref, flow_ref, sums_ref)


def moments_into(populations_ref, discs_ref, rim, velocity_ref, flow_ref, sums_ref):
    fans = discs_ref.shape[0]
    band_width = populations_ref.shape[2]
    sums_ref[...] = jnp.zeros(sums_ref.shape, jnp.float32)

    def moment_plane(index, carry):
        density, velocity = plane_moments([populations_ref[which, index] for which in range(19)])
        for dimension in range(3):
            velocity_ref[dimension, index] = velocity[dimension]
        for fan_number in range(fans):
            sums_ref[fan_number] += (
                discs_ref[fan_number, index + rim, 0:band_width, :] * velocity[0]
            )
        return carry

    lax.fori_loop(0, populations_ref.shape[1], moment_plane, 0)
    lane = lax.broadcasted_iota(jnp.int32, (1, flow_ref.shape[1]), 1)
    head_row = jnp.zeros((1, flow_ref.shape[1]), jnp.float32)
    for fan_number in range(fans):
        head_row = jnp.where(
            lane == fan_number,
            jnp.sum(sums_ref[fan_number], axis=(0, 1), keepdims=True),
            head_row,
        )
    flow_ref[...] = jnp.zeros(flow_ref.shape, jnp.float32)
    flow_ref[0:1, :] = head_row


def first_moments(populations, discs):
    fans, slab_len, band_width, height = discs.shape
    vmem = pl.BlockSpec(memory_space=pltpu.VMEM)
    return pl.pallas_call(
        lambda populations_ref, discs_ref, velocity_ref, flow_ref, sums_ref: moments_into(
            populations_ref, discs_ref, 0, velocity_ref, flow_ref, sums_ref
        ),
        out_shape=(
            jax.ShapeDtypeStruct((3, slab_len, band_width, height), jnp.float32),
            jax.ShapeDtypeStruct((band_width, height), jnp.float32),
        ),
        in_specs=[vmem, vmem],
        out_specs=(vmem, vmem),
        scratch_shapes=[pltpu.VMEM((fans, band_width, height), jnp.float32)],
        cost_estimate=pl.CostEstimate(
            flops=60 * discs[0].size, transcendentals=0, bytes_accessed=4 * populations.size
        ),
    )(populations, discs)


def lattice_step(strength, inner, low, high, rows, discs, solid_rim, with_moments):
    slab_len = inner.shape[1]
    band_width = inner.shape[2]
    height = inner.shape[3]
    fans = discs.shape[0]
    out_shape = [jax.ShapeDtypeStruct((19, slab_len, band_width, height), jnp.float32)]
    if with_moments:
        out_shape.append(jax.ShapeDtypeStruct((3, slab_len, band_width, height), jnp.float32))
        out_shape.append(jax.ShapeDtypeStruct((band_width, height), jnp.float32))
    scratch = [pltpu.VMEM((19, slab_len + 2, band_width + 2, height), jnp.float32)]
    if with_moments:
        scratch.append(pltpu.VMEM((fans, band_width, height), jnp.float32))
    vmem = pl.BlockSpec(memory_space=pltpu.VMEM)
    return pl.pallas_call(
        functools.partial(step_kernel, with_moments),
        out_shape=tuple(out_shape),
        in_specs=[pl.BlockSpec(memory_space=pltpu.SMEM)] + [vmem] * 6,
        out_specs=tuple([vmem] * len(out_shape)),
        scratch_shapes=scratch,
        cost_estimate=pl.CostEstimate(
            flops=300 * solid_rim.size, transcendentals=0, bytes_accessed=12 * inner.size
        ),
    )(strength, inner, low, high, rows, discs, solid_rim)


def disc_count():
    inside = 0
    for offset_a in range(-RAD, RAD + 1):
        for offset_b in range(-RAD, RAD + 1):
            if offset_a * offset_a + offset_b * offset_b <= RAD * RAD:
                inside = inside + 1
    return FAN_LEN * inside


def fan_discs(fan_hubs, coord_x, coord_y, coord_z, length_total):
    discs = []
    for fan_number in range(fan_hubs.shape[0]):
        offset_x = jnp.mod(coord_x - fan_hubs[fan_number, 0], length_total)
        offset_y = coord_y - fan_hubs[fan_number, 1]
        offset_z = coord_z - fan_hubs[fan_number, 2]
        discs.append(
            (offset_x < FAN_LEN) & (offset_y * offset_y + offset_z * offset_z <= RAD * RAD)
        )
    return discs


def partial_flow(discs, velocity, solid_flag):
    return jnp.stack(
        [
            jnp.sum(jnp.where(disc_nodes & jnp.logical_not(solid_flag), velocity[0], 0.0))
            for disc_nodes in discs
        ]
    )


def force_from(discs, totals, fan_gain, jet_speed):
    strength = fan_gain * (jet_speed - totals / float(disc_count()))
    force_field = jnp.zeros(discs[0].shape, jnp.float32)
    for fan_number in range(len(discs)):
        force_field = force_field + jnp.where(discs[fan_number], strength[fan_number], 0.0)
    return force_field


def advance(center, ahead_x, behind_x, ahead_y, behind_y, ahead_z, behind_z, velocity, solid_flag):
    laplace = ahead_x + behind_x + ahead_y + behind_y + ahead_z + behind_z - 6.0 * center
    advect = 0.5 * (
        velocity[0] * (ahead_x - behind_x)
        + velocity[1] * (ahead_y - behind_y)
        + velocity[2] * (ahead_z - behind_z)
    )
    return jnp.where(solid_flag, 0.0, center + DIFFUSIVITY * laplace - advect)


def shift_height(field, shift_z):
    if shift_z == 0:
        return field
    zero_layer = jnp.zeros(field.shape[:-1] + (1,), field.dtype)
    if shift_z == 1:
        return jnp.concatenate([zero_layer, field[..., :-1]], axis=-1)
    return jnp.concatenate([field[..., 1:], zero_layer], axis=-1)


def rim_round(fields, flow, axis, dim, reach):
    count = lax.axis_size(axis)
    fans = flow.shape[0]
    channels = [field.shape[0] for field in fields]

    def piece(start):
        cells = [lax.slice_in_dim(field, start, start + 1, axis=dim) for field in fields]
        if flow.ndim == 2:
            carrier = flow[None, None]
        else:
            carrier = jnp.zeros(cells[0].shape[1:], jnp.float32).at[0, 0, :fans].set(flow)[None]
        return jnp.concatenate(cells + [carrier], axis=0)

    def pick(received):
        if flow.ndim == 2:
            return received[-1, 0]
        return received[-1, 0, 0, :fans]

    head = piece(0)
    tail = piece(fields[0].shape[dim] - 1)
    forward = [(i, (i + 1) % count) for i in range(count)]
    backward = [((i + 1) % count, i) for i in range(count)]
    both = None
    if count == 2:
        both = lax.ppermute(jnp.concatenate([tail, head], axis=dim), axis, forward)
        from_left = lax.slice_in_dim(both, 0, 1, axis=dim)
        from_right = lax.slice_in_dim(both, 1, 2, axis=dim)
        total = flow + pick(from_left)
    else:
        from_left = lax.ppermute(tail, axis, forward)
        from_right = lax.ppermute(head, axis, backward)
        total = flow + pick(from_left) + pick(from_right)
    for offset in sorted(set(step % count for step in range(-reach, reach + 1)) - {0, 1, count - 1}):
        total = total + lax.ppermute(flow, axis, [(i, (i + offset) % count) for i in range(count)])
    extended = [(from_left, from_right, both)]
    first = channels[0]
    for field, channel in zip(fields[1:], channels[1:]):
        left = from_left[first : first + channel]
        right = from_right[first : first + channel]
        if dim == 1:
            extended.append(jnp.concatenate([left, field, right], axis=dim))
        else:
            extended.append(jnp.concatenate([field, left, right], axis=dim))
        first = first + channel
    return (extended, total)


def window_sum(values, axis, width):
    count = lax.axis_size(axis)
    total = values
    for offset in sorted(set(step % count for step in range(-width, width + 1)) - {0}):
        total = total + lax.ppermute(
            values, axis, [(i, (i + offset) % count) for i in range(count)]
        )
    return total


def source_release(sources, source_rate, offset_len, offset_band, slab_len, band_width, height):
    local_x = sources[:, 0] - offset_len
    local_y = sources[:, 1] - offset_band
    pick_x = (local_x[:, None] == jnp.arange(slab_len, dtype=jnp.int32)[None, :]).astype(
        jnp.float32
    )
    pick_y = (local_y[:, None] == jnp.arange(band_width, dtype=jnp.int32)[None, :]).astype(
        jnp.float32
    )
    pick_z = (sources[:, 2][:, None] == jnp.arange(height, dtype=jnp.int32)[None, :]).astype(
        jnp.float32
    )
    weighted = source_rate[:, None] * pick_x
    cross_table = (pick_y[:, :, None] * pick_z[:, None, :]).reshape(
        sources.shape[0], band_width * height
    )
    released = jnp.dot(
        weighted.T, cross_table, precision=lax.Precision.HIGHEST, preferred_element_type=jnp.float32
    )
    return released.reshape(slab_len, band_width, height)


def body(populations, solid_mask, smoke_field, fan_hubs, fan_gain, jet_speed, sources, source_rate):
    slab_len = populations.shape[1]
    band_width = populations.shape[2]
    height = populations.shape[3]
    offset_len = lax.axis_index("len") * slab_len
    offset_band = lax.axis_index("band") * band_width
    length_total = slab_len * lax.axis_size("len")
    breadth_total = band_width * lax.axis_size("band")
    solid_flag = solid_mask == 1
    coord_x = offset_len - 1 + jnp.arange(slab_len + 2, dtype=jnp.int32)
    coord_y = jnp.mod(
        offset_band
        + jnp.concatenate(
            [jnp.arange(band_width, dtype=jnp.int32), jnp.array([-1, band_width], jnp.int32)]
        ),
        breadth_total,
    )
    coord_z = jnp.arange(height, dtype=jnp.int32)
    along_in = jnp.mod(coord_x[None, :] - fan_hubs[:, 0:1], length_total) < FAN_LEN
    offset_y = coord_y[None, :] - fan_hubs[:, 1:2]
    offset_z = coord_z[None, :] - fan_hubs[:, 2:3]
    across_in = (
        offset_y[:, :, None] * offset_y[:, :, None] + offset_z[:, None, :] * offset_z[:, None, :]
        <= RAD * RAD
    )
    released = source_release(
        sources, source_rate, offset_len, offset_band, slab_len, band_width, height
    )
    len_reach = max(-(-FAN_LEN // slab_len), (slab_len + FAN_LEN - 1) // slab_len)
    band_reach = max(-(-(2 * RAD + 1) // band_width), (band_width + 2 * RAD) // band_width)
    inner_discs = (
        along_in[:, 1:-1, None, None]
        & across_in[:, None, 0:band_width]
        & jnp.logical_not(solid_flag)[None]
    ).astype(jnp.float32)
    velocity, flow = first_moments(populations, inner_discs)
    partials = flow
    for repeat in range(ITERS):
        fields = [populations, smoke_field[None]]
        if repeat == 0:
            fields.append(solid_flag.astype(jnp.float32)[None])
        fields, totals = rim_round(fields, partials, "len", 1, len_reach)
        totals = totals[0, : fan_hubs.shape[0]]
        low, high, _ = fields[0]
        fields[0] = jnp.concatenate([low[:19], populations, high[:19]], axis=1)
        fields, totals = rim_round(fields, totals, "band", 2, band_reach)
        if fields[0][2] is None:
            rows = jnp.concatenate([fields[0][0][:19], fields[0][1][:19]], axis=2)
        else:
            rows = fields[0][2]
        rimmed = fields[1][0]
        if repeat == 0:
            solid_rim = fields[2][0]
            air_rim = solid_rim == 0.0
            discs = (along_in[:, :, None, None] & across_in[:, None] & air_rim[None]).astype(
                jnp.float32
            )
        strength = fan_gain * (jet_speed - totals / float(disc_count()))
        last = repeat == ITERS - 1
        stepped = lattice_step(strength, populations, low, high, rows, discs, solid_rim, not last)
        ahead_x = rimmed[2:, 0:band_width]
        behind_x = rimmed[:-2, 0:band_width]
        ahead_y = jnp.concatenate(
            [rimmed[1:-1, 1:band_width], rimmed[1:-1, band_width + 1 : band_width + 2]], axis=1
        )
        behind_y = jnp.concatenate(
            [rimmed[1:-1, band_width : band_width + 1], rimmed[1:-1, 0 : band_width - 1]], axis=1
        )
        smoke_field = advance(
            smoke_field,
            ahead_x,
            behind_x,
            ahead_y,
            behind_y,
            shift_height(smoke_field, -1),
            shift_height(smoke_field, 1),
            velocity,
            solid_flag,
        )
        smoke_field = smoke_field + released
        populations = stepped[0]
        if not last:
            velocity = stepped[1]
            partials = stepped[2]
    return (populations, smoke_field)


def solution(mesh):
    placed = (
        P(None, "len", "band", None),
        P("len", "band", None),
        P("len", "band", None),
        P(),
        P(),
        P(),
        P(),
        P(),
    )
    return jax.shard_map(
        body,
        mesh=mesh,
        in_specs=placed,
        out_specs=(P(None, "len", "band", None), P("len", "band", None)),
        check_vma=False,
    )
```

```python
import functools

import jax
import jax.numpy as jnp
from jax import lax
from jax.experimental import pallas as pl
from jax.experimental.pallas import tpu as pltpu
from jax.sharding import PartitionSpec as P

RAD = 3
FAN_LEN = 16
ITERS = 3


VELOCITIES = (
    (0, 0, 0),
    (1, 0, 0),
    (-1, 0, 0),
    (0, 1, 0),
    (0, -1, 0),
    (0, 0, 1),
    (0, 0, -1),
    (1, 1, 0),
    (-1, -1, 0),
    (1, -1, 0),
    (-1, 1, 0),
    (1, 0, 1),
    (-1, 0, -1),
    (1, 0, -1),
    (-1, 0, 1),
    (0, 1, 1),
    (0, -1, -1),
    (0, 1, -1),
    (0, -1, 1),
)
WEIGHTS = (1.0 / 3.0,) + (1.0 / 18.0,) * 6 + (1.0 / 36.0,) * 12
OPPOSITE = (0, 2, 1, 4, 3, 6, 5, 8, 7, 10, 9, 12, 11, 14, 13, 16, 15, 18, 17)
RELAX_RATE = 1.0 / 0.6
DIFFUSIVITY = 0.12


def extended_2(cells, sides, width):
    for axis, dim in sides:
        count = lax.axis_size(axis)
        head = lax.slice_in_dim(cells, 0, width, axis=dim)
        tail = lax.slice_in_dim(cells, cells.shape[dim] - width, cells.shape[dim], axis=dim)
        cells = jnp.concatenate(
            [
                lax.ppermute(tail, axis, [(i, (i + 1) % count) for i in range(count)]),
                cells,
                lax.ppermute(head, axis, [((i + 1) % count, i) for i in range(count)]),
            ],
            axis=dim,
        )
    return cells


def moments(populations):
    density = jnp.sum(populations, axis=0)
    velocity = []
    for dimension in range(3):
        forward = [populations[which] for which in range(19) if VELOCITIES[which][dimension] == 1]
        backward = [populations[which] for which in range(19) if VELOCITIES[which][dimension] == -1]
        velocity.append((sum(forward) - sum(backward)) / density)
    return (density, velocity)


def plane_moments(populations):
    density = sum(populations[1:], populations[0])
    velocity = []
    for dimension in range(3):
        forward = [populations[which] for which in range(19) if VELOCITIES[which][dimension] == 1]
        backward = [populations[which] for which in range(19) if VELOCITIES[which][dimension] == -1]
        velocity.append((sum(forward) - sum(backward)) / density)
    return (density, velocity)


def step_kernel(
    with_moments, strength_ref, inner_ref, low_ref, high_ref, rows_ref, discs_ref, solid_ref, *rest
):
    if with_moments:
        out_ref, velocity_ref, flow_ref, posts_ref, sums_ref = rest
    else:
        out_ref, posts_ref = rest
    fans = discs_ref.shape[0]
    slab_len, band_width, height = out_ref.shape[1:]

    def collide_into(populations, index, rows):
        density, velocity = plane_moments(populations)
        force_field = strength_ref[0] * discs_ref[0, index, rows]
        for fan_number in range(1, fans):
            force_field = force_field + strength_ref[fan_number] * discs_ref[fan_number, index, rows]
        solid_flag = solid_ref[index, rows] != 0.0
        speed_sq = velocity[0] * velocity[0] + velocity[1] * velocity[1] + velocity[2] * velocity[2]
        for which in range(19):
            shift_x, shift_y, shift_z = VELOCITIES[which]
            along = shift_x * velocity[0] + shift_y * velocity[1] + shift_z * velocity[2]
            balance = (
                WEIGHTS[which] * density * (1.0 + 3.0 * along + 4.5 * along * along - 1.5 * speed_sq)
            )
            relaxed = populations[which] - RELAX_RATE * (populations[which] - balance)
            if shift_x != 0:
                relaxed = relaxed + 3.0 * WEIGHTS[which] * shift_x * force_field
            posts_ref[which, index, rows] = jnp.where(
                solid_flag, populations[OPPOSITE[which]], relaxed
            )

    inner = slice(0, band_width)
    rim = slice(band_width, band_width + 2)
    collide_into([low_ref[which, 0] for which in range(19)], 0, inner)
    collide_into([high_ref[which, 0] for which in range(19)], slab_len + 1, inner)

    def collide_plane(index, carry):
        collide_into([inner_ref[which, index - 1] for which in range(19)], index, inner)
        return carry

    lax.fori_loop(1, slab_len + 1, collide_plane, 0)

    def collide_rim(index, carry):
        collide_into([rows_ref[which, index] for which in range(19)], index, rim)
        return carry

    lax.fori_loop(0, slab_len + 2, collide_rim, 0)
    lane = lax.broadcasted_iota(jnp.int32, (slab_len, band_width, height), 2)
    row = lax.broadcasted_iota(jnp.int32, (slab_len, band_width, height), 1)
    for which in range(19):
        shift_x, shift_y, shift_z = VELOCITIES[which]
        planes = slice(1 - shift_x, 1 - shift_x + slab_len)
        piece = posts_ref[which, planes, 0:band_width, :]
        if shift_y == 1:
            rim_row = posts_ref[which, planes, band_width : band_width + 1, :]
            piece = jnp.where(row == 0, rim_row, pltpu.roll(piece, 1, 1))
        elif shift_y == -1:
            rim_row = posts_ref[which, planes, band_width + 1 : band_width + 2, :]
            piece = jnp.where(row == band_width - 1, rim_row, pltpu.roll(piece, band_width - 1, 1))
        if shift_z == 1:
            piece = jnp.where(lane == 0, 0.0, pltpu.roll(piece, 1, 2))
        elif shift_z == -1:
            piece = jnp.where(lane == height - 1, 0.0, pltpu.roll(piece, height - 1, 2))
        out_ref[which] = piece
    if not with_moments:
        return
    moments_into(out_ref, discs_ref, solid_ref, 1, velocity_ref, flow_ref, sums_ref)


def moments_into(populations_ref, discs_ref, solid_ref, rim, velocity_ref, flow_ref, sums_ref):
    fans = discs_ref.shape[0]
    band_width = populations_ref.shape[2]
    sums_ref[...] = jnp.zeros(sums_ref.shape, jnp.float32)

    def moment_plane(index, carry):
        density, velocity = plane_moments([populations_ref[which, index] for which in range(19)])
        for dimension in range(3):
            velocity_ref[dimension, index] = velocity[dimension]
        solid_flag = solid_ref[index + rim, 0:band_width, :] != 0.0
        for fan_number in range(fans):
            sums_ref[fan_number] += jnp.where(
                solid_flag, 0.0, discs_ref[fan_number, index + rim, 0:band_width, :] * velocity[0]
            )
        return carry

    lax.fori_loop(0, populations_ref.shape[1], moment_plane, 0)
    for fan_number in range(fans):
        flow_ref[fan_number : fan_number + 1, :] = jnp.broadcast_to(
            jnp.sum(sums_ref[fan_number], axis=(0, 1), keepdims=True), (1, flow_ref.shape[1])
        )


def first_moments(populations, discs, solid):
    fans, slab_len, band_width, height = discs.shape
    vmem = pl.BlockSpec(memory_space=pltpu.VMEM)
    return pl.pallas_call(
        lambda populations_ref, discs_ref, solid_ref, velocity_ref, flow_ref, sums_ref: moments_into(
            populations_ref, discs_ref, solid_ref, 0, velocity_ref, flow_ref, sums_ref
        ),
        out_shape=(
            jax.ShapeDtypeStruct((3, slab_len, band_width, height), jnp.float32),
            jax.ShapeDtypeStruct((fans, height), jnp.float32),
        ),
        in_specs=[vmem, vmem, vmem],
        out_specs=(vmem, vmem),
        scratch_shapes=[pltpu.VMEM((fans, band_width, height), jnp.float32)],
        cost_estimate=pl.CostEstimate(
            flops=60 * discs[0].size, transcendentals=0, bytes_accessed=4 * populations.size
        ),
    )(populations, discs, solid)


def lattice_step(strength, inner, low, high, rows, discs, solid_rim, with_moments):
    slab_len = inner.shape[1]
    band_width = inner.shape[2]
    height = inner.shape[3]
    fans = discs.shape[0]
    out_shape = [jax.ShapeDtypeStruct((19, slab_len, band_width, height), jnp.float32)]
    if with_moments:
        out_shape.append(jax.ShapeDtypeStruct((3, slab_len, band_width, height), jnp.float32))
        out_shape.append(jax.ShapeDtypeStruct((fans, height), jnp.float32))
    scratch = [pltpu.VMEM((19, slab_len + 2, band_width + 2, height), jnp.float32)]
    if with_moments:
        scratch.append(pltpu.VMEM((fans, band_width, height), jnp.float32))
    vmem = pl.BlockSpec(memory_space=pltpu.VMEM)
    return pl.pallas_call(
        functools.partial(step_kernel, with_moments),
        out_shape=tuple(out_shape),
        in_specs=[pl.BlockSpec(memory_space=pltpu.SMEM)] + [vmem] * 6,
        out_specs=tuple([vmem] * len(out_shape)),
        scratch_shapes=scratch,
        cost_estimate=pl.CostEstimate(
            flops=300 * solid_rim.size, transcendentals=0, bytes_accessed=12 * inner.size
        ),
    )(strength, inner, low, high, rows, discs, solid_rim)


def disc_count():
    inside = 0
    for offset_a in range(-RAD, RAD + 1):
        for offset_b in range(-RAD, RAD + 1):
            if offset_a * offset_a + offset_b * offset_b <= RAD * RAD:
                inside = inside + 1
    return FAN_LEN * inside


def fan_discs(fan_hubs, coord_x, coord_y, coord_z, length_total):
    discs = []
    for fan_number in range(fan_hubs.shape[0]):
        offset_x = jnp.mod(coord_x - fan_hubs[fan_number, 0], length_total)
        offset_y = coord_y - fan_hubs[fan_number, 1]
        offset_z = coord_z - fan_hubs[fan_number, 2]
        discs.append(
            (offset_x < FAN_LEN) & (offset_y * offset_y + offset_z * offset_z <= RAD * RAD)
        )
    return discs


def partial_flow(discs, velocity, solid_flag):
    return jnp.stack(
        [
            jnp.sum(jnp.where(disc_nodes & jnp.logical_not(solid_flag), velocity[0], 0.0))
            for disc_nodes in discs
        ]
    )


def force_from(discs, totals, fan_gain, jet_speed):
    strength = fan_gain * (jet_speed - totals / float(disc_count()))
    force_field = jnp.zeros(discs[0].shape, jnp.float32)
    for fan_number in range(len(discs)):
        force_field = force_field + jnp.where(discs[fan_number], strength[fan_number], 0.0)
    return force_field


def advance(center, ahead_x, behind_x, ahead_y, behind_y, ahead_z, behind_z, velocity, solid_flag):
    laplace = ahead_x + behind_x + ahead_y + behind_y + ahead_z + behind_z - 6.0 * center
    advect = 0.5 * (
        velocity[0] * (ahead_x - behind_x)
        + velocity[1] * (ahead_y - behind_y)
        + velocity[2] * (ahead_z - behind_z)
    )
    return jnp.where(solid_flag, 0.0, center + DIFFUSIVITY * laplace - advect)


def shift_height(field, shift_z):
    if shift_z == 0:
        return field
    zero_layer = jnp.zeros(field.shape[:-1] + (1,), field.dtype)
    if shift_z == 1:
        return jnp.concatenate([zero_layer, field[..., :-1]], axis=-1)
    return jnp.concatenate([field[..., 1:], zero_layer], axis=-1)


def rim_round(fields, flow, axis, dim, reach):
    count = lax.axis_size(axis)
    fans = flow.shape[0]
    channels = [field.shape[0] for field in fields]

    def piece(start):
        cells = [lax.slice_in_dim(field, start, start + 1, axis=dim) for field in fields]
        carrier = jnp.zeros(cells[0].shape[1:], jnp.float32).at[0, 0, :fans].set(flow)[None]
        return jnp.concatenate(cells + [carrier], axis=0)

    head = piece(0)
    tail = piece(fields[0].shape[dim] - 1)
    forward = [(i, (i + 1) % count) for i in range(count)]
    backward = [((i + 1) % count, i) for i in range(count)]
    both = None
    if count == 2:
        both = lax.ppermute(jnp.concatenate([tail, head], axis=dim), axis, forward)
        from_left = lax.slice_in_dim(both, 0, 1, axis=dim)
        from_right = lax.slice_in_dim(both, 1, 2, axis=dim)
        total = flow + from_left[-1, 0, 0, :fans]
    else:
        from_left = lax.ppermute(tail, axis, forward)
        from_right = lax.ppermute(head, axis, backward)
        total = flow + from_left[-1, 0, 0, :fans] + from_right[-1, 0, 0, :fans]
    for offset in sorted(set(step % count for step in range(-reach, reach + 1)) - {0, 1, count - 1}):
        total = total + lax.ppermute(flow, axis, [(i, (i + offset) % count) for i in range(count)])
    extended = [(from_left, from_right, both)]
    first = channels[0]
    for field, channel in zip(fields[1:], channels[1:]):
        left = from_left[first : first + channel]
        right = from_right[first : first + channel]
        if dim == 1:
            extended.append(jnp.concatenate([left, field, right], axis=dim))
        else:
            extended.append(jnp.concatenate([field, left, right], axis=dim))
        first = first + channel
    return (extended, total)


def window_sum(values, axis, width):
    count = lax.axis_size(axis)
    total = values
    for offset in sorted(set(step % count for step in range(-width, width + 1)) - {0}):
        total = total + lax.ppermute(
            values, axis, [(i, (i + offset) % count) for i in range(count)]
        )
    return total


def source_release(sources, source_rate, offset_len, offset_band, slab_len, band_width, height):
    local_x = sources[:, 0] - offset_len
    local_y = sources[:, 1] - offset_band
    pick_x = (local_x[:, None] == jnp.arange(slab_len, dtype=jnp.int32)[None, :]).astype(
        jnp.float32
    )
    pick_y = (local_y[:, None] == jnp.arange(band_width, dtype=jnp.int32)[None, :]).astype(
        jnp.float32
    )
    pick_z = (sources[:, 2][:, None] == jnp.arange(height, dtype=jnp.int32)[None, :]).astype(
        jnp.float32
    )
    weighted = source_rate[:, None] * pick_x
    cross_table = (pick_y[:, :, None] * pick_z[:, None, :]).reshape(
        sources.shape[0], band_width * height
    )
    released = jnp.dot(
        weighted.T, cross_table, precision=lax.Precision.HIGHEST, preferred_element_type=jnp.float32
    )
    return released.reshape(slab_len, band_width, height)


def body(populations, solid_mask, smoke_field, fan_hubs, fan_gain, jet_speed, sources, source_rate):
    slab_len = populations.shape[1]
    band_width = populations.shape[2]
    height = populations.shape[3]
    offset_len = lax.axis_index("len") * slab_len
    offset_band = lax.axis_index("band") * band_width
    length_total = slab_len * lax.axis_size("len")
    breadth_total = band_width * lax.axis_size("band")
    solid_flag = solid_mask == 1
    coord_x = offset_len - 1 + jnp.arange(slab_len + 2, dtype=jnp.int32)
    coord_y = jnp.mod(
        offset_band
        + jnp.concatenate(
            [jnp.arange(band_width, dtype=jnp.int32), jnp.array([-1, band_width], jnp.int32)]
        ),
        breadth_total,
    )
    coord_z = jnp.arange(height, dtype=jnp.int32)
    along_in = jnp.mod(coord_x[None, :] - fan_hubs[:, 0:1], length_total) < FAN_LEN
    offset_y = coord_y[None, :] - fan_hubs[:, 1:2]
    offset_z = coord_z[None, :] - fan_hubs[:, 2:3]
    across_in = (
        offset_y[:, :, None] * offset_y[:, :, None] + offset_z[:, None, :] * offset_z[:, None, :]
        <= RAD * RAD
    )
    released = source_release(
        sources, source_rate, offset_len, offset_band, slab_len, band_width, height
    )
    len_reach = max(-(-FAN_LEN // slab_len), (slab_len + FAN_LEN - 1) // slab_len)
    band_reach = max(-(-(2 * RAD + 1) // band_width), (band_width + 2 * RAD) // band_width)
    discs = (along_in[:, :, None, None] & across_in[:, None]).astype(jnp.float32)
    solid_planes = solid_flag.astype(jnp.float32)
    velocity, flow = first_moments(populations, discs[:, 1:-1, 0:band_width], solid_planes)
    partials = flow[:, 0]
    for repeat in range(ITERS):
        fields = [populations, smoke_field[None]]
        if repeat == 0:
            fields.append(solid_planes[None])
        fields, totals = rim_round(fields, partials, "len", 1, len_reach)
        low, high, _ = fields[0]
        fields[0] = jnp.concatenate([low[:19], populations, high[:19]], axis=1)
        fields, totals = rim_round(fields, totals, "band", 2, band_reach)
        if fields[0][2] is None:
            rows = jnp.concatenate([fields[0][0][:19], fields[0][1][:19]], axis=2)
        else:
            rows = fields[0][2]
        rimmed = fields[1][0]
        if repeat == 0:
            solid_rim = fields[2][0]
        strength = fan_gain * (jet_speed - totals / float(disc_count()))
        last = repeat == ITERS - 1
        stepped = lattice_step(strength, populations, low, high, rows, discs, solid_rim, not last)
        ahead_x = rimmed[2:, 0:band_width]
        behind_x = rimmed[:-2, 0:band_width]
        ahead_y = jnp.concatenate(
            [rimmed[1:-1, 1:band_width], rimmed[1:-1, band_width + 1 : band_width + 2]], axis=1
        )
        behind_y = jnp.concatenate(
            [rimmed[1:-1, band_width : band_width + 1], rimmed[1:-1, 0 : band_width - 1]], axis=1
        )
        smoke_field = advance(
            smoke_field,
            ahead_x,
            behind_x,
            ahead_y,
            behind_y,
            shift_height(smoke_field, -1),
            shift_height(smoke_field, 1),
            velocity,
            solid_flag,
        )
        smoke_field = smoke_field + released
        populations = stepped[0]
        if not last:
            velocity = stepped[1]
            partials = stepped[2][:, 0]
    return (populations, smoke_field)


def solution(mesh):
    placed = (
        P(None, "len", "band", None),
        P("len", "band", None),
        P("len", "band", None),
        P(),
        P(),
        P(),
        P(),
        P(),
    )
    return jax.shard_map(
        body,
        mesh=mesh,
        in_specs=placed,
        out_specs=(P(None, "len", "band", None), P("len", "band", None)),
        check_vma=False,
    )
```

```python
import functools

import jax
import jax.numpy as jnp
from jax import lax
from jax.experimental import pallas as pl
from jax.experimental.pallas import tpu as pltpu
from jax.sharding import PartitionSpec as P

RAD = 3
FAN_LEN = 16
ITERS = 3


VELOCITIES = (
    (0, 0, 0),
    (1, 0, 0),
    (-1, 0, 0),
    (0, 1, 0),
    (0, -1, 0),
    (0, 0, 1),
    (0, 0, -1),
    (1, 1, 0),
    (-1, -1, 0),
    (1, -1, 0),
    (-1, 1, 0),
    (1, 0, 1),
    (-1, 0, -1),
    (1, 0, -1),
    (-1, 0, 1),
    (0, 1, 1),
    (0, -1, -1),
    (0, 1, -1),
    (0, -1, 1),
)
WEIGHTS = (1.0 / 3.0,) + (1.0 / 18.0,) * 6 + (1.0 / 36.0,) * 12
OPPOSITE = (0, 2, 1, 4, 3, 6, 5, 8, 7, 10, 9, 12, 11, 14, 13, 16, 15, 18, 17)
RELAX_RATE = 1.0 / 0.6
DIFFUSIVITY = 0.12


def extended_2(cells, sides, width):
    for axis, dim in sides:
        count = lax.axis_size(axis)
        head = lax.slice_in_dim(cells, 0, width, axis=dim)
        tail = lax.slice_in_dim(cells, cells.shape[dim] - width, cells.shape[dim], axis=dim)
        cells = jnp.concatenate(
            [
                lax.ppermute(tail, axis, [(i, (i + 1) % count) for i in range(count)]),
                cells,
                lax.ppermute(head, axis, [((i + 1) % count, i) for i in range(count)]),
            ],
            axis=dim,
        )
    return cells


def moments(populations):
    density = jnp.sum(populations, axis=0)
    velocity = []
    for dimension in range(3):
        forward = [populations[which] for which in range(19) if VELOCITIES[which][dimension] == 1]
        backward = [populations[which] for which in range(19) if VELOCITIES[which][dimension] == -1]
        velocity.append((sum(forward) - sum(backward)) / density)
    return (density, velocity)


def plane_moments(populations):
    density = sum(populations[1:], populations[0])
    velocity = []
    for dimension in range(3):
        forward = [populations[which] for which in range(19) if VELOCITIES[which][dimension] == 1]
        backward = [populations[which] for which in range(19) if VELOCITIES[which][dimension] == -1]
        velocity.append((sum(forward) - sum(backward)) / density)
    return (density, velocity)


def step_kernel(
    with_moments, strength_ref, inner_ref, low_ref, high_ref, rows_ref, discs_ref, solid_ref, *rest
):
    if with_moments:
        out_ref, velocity_ref, flow_ref, posts_ref, sums_ref = rest
    else:
        out_ref, posts_ref = rest
    fans = discs_ref.shape[0]
    slab_len, band_width, height = out_ref.shape[1:]

    def collide_into(populations, index, rows):
        density, velocity = plane_moments(populations)
        force_field = strength_ref[0] * discs_ref[0, index, rows]
        for fan_number in range(1, fans):
            force_field = force_field + strength_ref[fan_number] * discs_ref[fan_number, index, rows]
        solid_flag = solid_ref[index, rows] != 0.0
        speed_sq = velocity[0] * velocity[0] + velocity[1] * velocity[1] + velocity[2] * velocity[2]
        for which in range(19):
            shift_x, shift_y, shift_z = VELOCITIES[which]
            along = shift_x * velocity[0] + shift_y * velocity[1] + shift_z * velocity[2]
            balance = (
                WEIGHTS[which] * density * (1.0 + 3.0 * along + 4.5 * along * along - 1.5 * speed_sq)
            )
            relaxed = populations[which] - RELAX_RATE * (populations[which] - balance)
            if shift_x != 0:
                relaxed = relaxed + 3.0 * WEIGHTS[which] * shift_x * force_field
            posts_ref[which, index, rows] = jnp.where(
                solid_flag, populations[OPPOSITE[which]], relaxed
            )

    inner = slice(0, band_width)
    rim = slice(band_width, band_width + 2)
    collide_into([low_ref[which, 0] for which in range(19)], 0, inner)
    collide_into([high_ref[which, 0] for which in range(19)], slab_len + 1, inner)

    def collide_plane(index, carry):
        collide_into([inner_ref[which, index - 1] for which in range(19)], index, inner)
        return carry

    lax.fori_loop(1, slab_len + 1, collide_plane, 0)

    def collide_rim(index, carry):
        collide_into([rows_ref[which, index] for which in range(19)], index, rim)
        return carry

    lax.fori_loop(0, slab_len + 2, collide_rim, 0)
    lane = lax.broadcasted_iota(jnp.int32, (slab_len, band_width, height), 2)
    row = lax.broadcasted_iota(jnp.int32, (slab_len, band_width, height), 1)
    for which in range(19):
        shift_x, shift_y, shift_z = VELOCITIES[which]
        planes = slice(1 - shift_x, 1 - shift_x + slab_len)
        piece = posts_ref[which, planes, 0:band_width, :]
        if shift_y == 1:
            rim_row = posts_ref[which, planes, band_width : band_width + 1, :]
            piece = jnp.where(row == 0, rim_row, pltpu.roll(piece, 1, 1))
        elif shift_y == -1:
            rim_row = posts_ref[which, planes, band_width + 1 : band_width + 2, :]
            piece = jnp.where(row == band_width - 1, rim_row, pltpu.roll(piece, band_width - 1, 1))
        if shift_z == 1:
            piece = jnp.where(lane == 0, 0.0, pltpu.roll(piece, 1, 2))
        elif shift_z == -1:
            piece = jnp.where(lane == height - 1, 0.0, pltpu.roll(piece, height - 1, 2))
        out_ref[which] = piece
    if not with_moments:
        return
    moments_into(out_ref, discs_ref, solid_ref, 1, velocity_ref, flow_ref, sums_ref)


def moments_into(populations_ref, discs_ref, solid_ref, rim, velocity_ref, flow_ref, sums_ref):
    fans = discs_ref.shape[0]
    band_width = populations_ref.shape[2]
    sums_ref[...] = jnp.zeros(sums_ref.shape, jnp.float32)

    def moment_plane(index, carry):
        density, velocity = plane_moments([populations_ref[which, index] for which in range(19)])
        for dimension in range(3):
            velocity_ref[dimension, index] = velocity[dimension]
        solid_flag = solid_ref[index + rim, 0:band_width, :] != 0.0
        for fan_number in range(fans):
            sums_ref[fan_number] += jnp.where(
                solid_flag, 0.0, discs_ref[fan_number, index + 1, 0:band_width, :] * velocity[0]
            )
        return carry

    lax.fori_loop(0, populations_ref.shape[1], moment_plane, 0)
    for fan_number in range(fans):
        flow_ref[fan_number : fan_number + 1, :] = jnp.broadcast_to(
            jnp.sum(sums_ref[fan_number], axis=(0, 1), keepdims=True), (1, flow_ref.shape[1])
        )


def first_moments(populations, discs, solid):
    fans = discs.shape[0]
    slab_len, band_width, height = populations.shape[1:]
    vmem = pl.BlockSpec(memory_space=pltpu.VMEM)
    return pl.pallas_call(
        lambda populations_ref, discs_ref, solid_ref, velocity_ref, flow_ref, sums_ref: moments_into(
            populations_ref, discs_ref, solid_ref, 0, velocity_ref, flow_ref, sums_ref
        ),
        out_shape=(
            jax.ShapeDtypeStruct((3, slab_len, band_width, height), jnp.float32),
            jax.ShapeDtypeStruct((fans, height), jnp.float32),
        ),
        in_specs=[vmem, vmem, vmem],
        out_specs=(vmem, vmem),
        scratch_shapes=[pltpu.VMEM((fans, band_width, height), jnp.float32)],
        cost_estimate=pl.CostEstimate(
            flops=60 * discs[0].size, transcendentals=0, bytes_accessed=4 * populations.size
        ),
    )(populations, discs, solid)


def lattice_step(strength, inner, low, high, rows, discs, solid_rim, with_moments):
    slab_len = inner.shape[1]
    band_width = inner.shape[2]
    height = inner.shape[3]
    fans = discs.shape[0]
    out_shape = [jax.ShapeDtypeStruct((19, slab_len, band_width, height), jnp.float32)]
    if with_moments:
        out_shape.append(jax.ShapeDtypeStruct((3, slab_len, band_width, height), jnp.float32))
        out_shape.append(jax.ShapeDtypeStruct((fans, height), jnp.float32))
    scratch = [pltpu.VMEM((19, slab_len + 2, band_width + 2, height), jnp.float32)]
    if with_moments:
        scratch.append(pltpu.VMEM((fans, band_width, height), jnp.float32))
    vmem = pl.BlockSpec(memory_space=pltpu.VMEM)
    return pl.pallas_call(
        functools.partial(step_kernel, with_moments),
        out_shape=tuple(out_shape),
        in_specs=[pl.BlockSpec(memory_space=pltpu.SMEM)] + [vmem] * 6,
        out_specs=tuple([vmem] * len(out_shape)),
        scratch_shapes=scratch,
        cost_estimate=pl.CostEstimate(
            flops=300 * solid_rim.size, transcendentals=0, bytes_accessed=12 * inner.size
        ),
    )(strength, inner, low, high, rows, discs, solid_rim)


def disc_count():
    inside = 0
    for offset_a in range(-RAD, RAD + 1):
        for offset_b in range(-RAD, RAD + 1):
            if offset_a * offset_a + offset_b * offset_b <= RAD * RAD:
                inside = inside + 1
    return FAN_LEN * inside


def fan_discs(fan_hubs, coord_x, coord_y, coord_z, length_total):
    discs = []
    for fan_number in range(fan_hubs.shape[0]):
        offset_x = jnp.mod(coord_x - fan_hubs[fan_number, 0], length_total)
        offset_y = coord_y - fan_hubs[fan_number, 1]
        offset_z = coord_z - fan_hubs[fan_number, 2]
        discs.append(
            (offset_x < FAN_LEN) & (offset_y * offset_y + offset_z * offset_z <= RAD * RAD)
        )
    return discs


def partial_flow(discs, velocity, solid_flag):
    return jnp.stack(
        [
            jnp.sum(jnp.where(disc_nodes & jnp.logical_not(solid_flag), velocity[0], 0.0))
            for disc_nodes in discs
        ]
    )


def force_from(discs, totals, fan_gain, jet_speed):
    strength = fan_gain * (jet_speed - totals / float(disc_count()))
    force_field = jnp.zeros(discs[0].shape, jnp.float32)
    for fan_number in range(len(discs)):
        force_field = force_field + jnp.where(discs[fan_number], strength[fan_number], 0.0)
    return force_field


def advance(center, ahead_x, behind_x, ahead_y, behind_y, ahead_z, behind_z, velocity, solid_flag):
    laplace = ahead_x + behind_x + ahead_y + behind_y + ahead_z + behind_z - 6.0 * center
    advect = 0.5 * (
        velocity[0] * (ahead_x - behind_x)
        + velocity[1] * (ahead_y - behind_y)
        + velocity[2] * (ahead_z - behind_z)
    )
    return jnp.where(solid_flag, 0.0, center + DIFFUSIVITY * laplace - advect)


def shift_height(field, shift_z):
    if shift_z == 0:
        return field
    zero_layer = jnp.zeros(field.shape[:-1] + (1,), field.dtype)
    if shift_z == 1:
        return jnp.concatenate([zero_layer, field[..., :-1]], axis=-1)
    return jnp.concatenate([field[..., 1:], zero_layer], axis=-1)


def rim_round(fields, flow, axis, dim, reach):
    count = lax.axis_size(axis)
    fans = flow.shape[0]
    channels = [field.shape[0] for field in fields]

    def piece(start):
        cells = [lax.slice_in_dim(field, start, start + 1, axis=dim) for field in fields]
        carrier = jnp.zeros(cells[0].shape[1:], jnp.float32).at[0, 0, :fans].set(flow)[None]
        return jnp.concatenate(cells + [carrier], axis=0)

    head = piece(0)
    tail = piece(fields[0].shape[dim] - 1)
    forward = [(i, (i + 1) % count) for i in range(count)]
    backward = [((i + 1) % count, i) for i in range(count)]
    both = None
    if count == 2:
        both = lax.ppermute(jnp.concatenate([tail, head], axis=dim), axis, forward)
        from_left = lax.slice_in_dim(both, 0, 1, axis=dim)
        from_right = lax.slice_in_dim(both, 1, 2, axis=dim)
        total = flow + from_left[-1, 0, 0, :fans]
    else:
        from_left = lax.ppermute(tail, axis, forward)
        from_right = lax.ppermute(head, axis, backward)
        total = flow + from_left[-1, 0, 0, :fans] + from_right[-1, 0, 0, :fans]
    for offset in sorted(set(step % count for step in range(-reach, reach + 1)) - {0, 1, count - 1}):
        total = total + lax.ppermute(flow, axis, [(i, (i + offset) % count) for i in range(count)])
    extended = [(from_left, from_right, both)]
    first = channels[0]
    for field, channel in zip(fields[1:], channels[1:]):
        left = from_left[first : first + channel]
        right = from_right[first : first + channel]
        if dim == 1:
            extended.append(jnp.concatenate([left, field, right], axis=dim))
        else:
            extended.append(jnp.concatenate([field, left, right], axis=dim))
        first = first + channel
    return (extended, total)


def window_sum(values, axis, width):
    count = lax.axis_size(axis)
    total = values
    for offset in sorted(set(step % count for step in range(-width, width + 1)) - {0}):
        total = total + lax.ppermute(
            values, axis, [(i, (i + offset) % count) for i in range(count)]
        )
    return total


def source_release(sources, source_rate, offset_len, offset_band, slab_len, band_width, height):
    local_x = sources[:, 0] - offset_len
    local_y = sources[:, 1] - offset_band
    pick_x = (local_x[:, None] == jnp.arange(slab_len, dtype=jnp.int32)[None, :]).astype(
        jnp.float32
    )
    pick_y = (local_y[:, None] == jnp.arange(band_width, dtype=jnp.int32)[None, :]).astype(
        jnp.float32
    )
    pick_z = (sources[:, 2][:, None] == jnp.arange(height, dtype=jnp.int32)[None, :]).astype(
        jnp.float32
    )
    weighted = source_rate[:, None] * pick_x
    cross_table = (pick_y[:, :, None] * pick_z[:, None, :]).reshape(
        sources.shape[0], band_width * height
    )
    released = jnp.dot(
        weighted.T, cross_table, precision=lax.Precision.HIGHEST, preferred_element_type=jnp.float32
    )
    return released.reshape(slab_len, band_width, height)


def body(populations, solid_mask, smoke_field, fan_hubs, fan_gain, jet_speed, sources, source_rate):
    slab_len = populations.shape[1]
    band_width = populations.shape[2]
    height = populations.shape[3]
    offset_len = lax.axis_index("len") * slab_len
    offset_band = lax.axis_index("band") * band_width
    length_total = slab_len * lax.axis_size("len")
    breadth_total = band_width * lax.axis_size("band")
    solid_flag = solid_mask == 1
    coord_x = offset_len - 1 + jnp.arange(slab_len + 2, dtype=jnp.int32)
    coord_y = jnp.mod(
        offset_band
        + jnp.concatenate(
            [jnp.arange(band_width, dtype=jnp.int32), jnp.array([-1, band_width], jnp.int32)]
        ),
        breadth_total,
    )
    coord_z = jnp.arange(height, dtype=jnp.int32)
    along_in = jnp.mod(coord_x[None, :] - fan_hubs[:, 0:1], length_total) < FAN_LEN
    offset_y = coord_y[None, :] - fan_hubs[:, 1:2]
    offset_z = coord_z[None, :] - fan_hubs[:, 2:3]
    across_in = (
        offset_y[:, :, None] * offset_y[:, :, None] + offset_z[:, None, :] * offset_z[:, None, :]
        <= RAD * RAD
    )
    released = source_release(
        sources, source_rate, offset_len, offset_band, slab_len, band_width, height
    )
    len_reach = max(-(-FAN_LEN // slab_len), (slab_len + FAN_LEN - 1) // slab_len)
    band_reach = max(-(-(2 * RAD + 1) // band_width), (band_width + 2 * RAD) // band_width)
    discs = (along_in[:, :, None, None] & across_in[:, None]).astype(jnp.float32)
    solid_planes = solid_flag.astype(jnp.float32)
    velocity, flow = first_moments(populations, discs, solid_planes)
    partials = flow[:, 0]
    for repeat in range(ITERS):
        fields = [populations, smoke_field[None]]
        if repeat == 0:
            fields.append(solid_planes[None])
        fields, totals = rim_round(fields, partials, "len", 1, len_reach)
        low, high, _ = fields[0]
        fields[0] = jnp.concatenate([low[:19], populations, high[:19]], axis=1)
        fields, totals = rim_round(fields, totals, "band", 2, band_reach)
        if fields[0][2] is None:
            rows = jnp.concatenate([fields[0][0][:19], fields[0][1][:19]], axis=2)
        else:
            rows = fields[0][2]
        rimmed = fields[1][0]
        if repeat == 0:
            solid_rim = fields[2][0]
        strength = fan_gain * (jet_speed - totals / float(disc_count()))
        last = repeat == ITERS - 1
        stepped = lattice_step(strength, populations, low, high, rows, discs, solid_rim, not last)
        ahead_x = rimmed[2:, 0:band_width]
        behind_x = rimmed[:-2, 0:band_width]
        ahead_y = jnp.concatenate(
            [rimmed[1:-1, 1:band_width], rimmed[1:-1, band_width + 1 : band_width + 2]], axis=1
        )
        behind_y = jnp.concatenate(
            [rimmed[1:-1, band_width : band_width + 1], rimmed[1:-1, 0 : band_width - 1]], axis=1
        )
        smoke_field = advance(
            smoke_field,
            ahead_x,
            behind_x,
            ahead_y,
            behind_y,
            shift_height(smoke_field, -1),
            shift_height(smoke_field, 1),
            velocity,
            solid_flag,
        )
        smoke_field = smoke_field + released
        populations = stepped[0]
        if not last:
            velocity = stepped[1]
            partials = stepped[2][:, 0]
    return (populations, smoke_field)


def solution(mesh):
    placed = (
        P(None, "len", "band", None),
        P("len", "band", None),
        P("len", "band", None),
        P(),
        P(),
        P(),
        P(),
        P(),
    )
    return jax.shard_map(
        body,
        mesh=mesh,
        in_specs=placed,
        out_specs=(P(None, "len", "band", None), P("len", "band", None)),
        check_vma=False,
    )
```

```python
import functools

import jax
import jax.numpy as jnp
from jax import lax
from jax.experimental import pallas as pl
from jax.experimental.pallas import tpu as pltpu
from jax.sharding import PartitionSpec as P

RAD = 3
FAN_LEN = 16
ITERS = 3


VELOCITIES = (
    (0, 0, 0),
    (1, 0, 0),
    (-1, 0, 0),
    (0, 1, 0),
    (0, -1, 0),
    (0, 0, 1),
    (0, 0, -1),
    (1, 1, 0),
    (-1, -1, 0),
    (1, -1, 0),
    (-1, 1, 0),
    (1, 0, 1),
    (-1, 0, -1),
    (1, 0, -1),
    (-1, 0, 1),
    (0, 1, 1),
    (0, -1, -1),
    (0, 1, -1),
    (0, -1, 1),
)
WEIGHTS = (1.0 / 3.0,) + (1.0 / 18.0,) * 6 + (1.0 / 36.0,) * 12
OPPOSITE = (0, 2, 1, 4, 3, 6, 5, 8, 7, 10, 9, 12, 11, 14, 13, 16, 15, 18, 17)
RELAX_RATE = 1.0 / 0.6
DIFFUSIVITY = 0.12


def extended_2(cells, sides, width):
    for axis, dim in sides:
        count = lax.axis_size(axis)
        head = lax.slice_in_dim(cells, 0, width, axis=dim)
        tail = lax.slice_in_dim(cells, cells.shape[dim] - width, cells.shape[dim], axis=dim)
        cells = jnp.concatenate(
            [
                lax.ppermute(tail, axis, [(i, (i + 1) % count) for i in range(count)]),
                cells,
                lax.ppermute(head, axis, [((i + 1) % count, i) for i in range(count)]),
            ],
            axis=dim,
        )
    return cells


def moments(populations):
    density = jnp.sum(populations, axis=0)
    velocity = []
    for dimension in range(3):
        forward = [populations[which] for which in range(19) if VELOCITIES[which][dimension] == 1]
        backward = [populations[which] for which in range(19) if VELOCITIES[which][dimension] == -1]
        velocity.append((sum(forward) - sum(backward)) / density)
    return (density, velocity)


def plane_moments(populations):
    density = sum(populations[1:], populations[0])
    velocity = []
    for dimension in range(3):
        forward = [populations[which] for which in range(19) if VELOCITIES[which][dimension] == 1]
        backward = [populations[which] for which in range(19) if VELOCITIES[which][dimension] == -1]
        velocity.append((sum(forward) - sum(backward)) / density)
    return (density, velocity)


def step_kernel(
    with_moments, strength_ref, inner_ref, low_ref, high_ref, rows_ref, discs_ref, solid_ref, *rest
):
    if with_moments:
        out_ref, velocity_ref, flow_ref, posts_ref, sums_ref = rest
    else:
        out_ref, posts_ref = rest
    fans = discs_ref.shape[0]
    slab_len, band_width, height = out_ref.shape[1:]

    def collide_into(populations, index, rows):
        density, velocity = plane_moments(populations)
        force_field = strength_ref[0] * discs_ref[0, index, rows]
        for fan_number in range(1, fans):
            force_field = force_field + strength_ref[fan_number] * discs_ref[fan_number, index, rows]
        solid_flag = solid_ref[index, rows] != 0.0
        speed_sq = velocity[0] * velocity[0] + velocity[1] * velocity[1] + velocity[2] * velocity[2]
        for which in range(19):
            shift_x, shift_y, shift_z = VELOCITIES[which]
            along = shift_x * velocity[0] + shift_y * velocity[1] + shift_z * velocity[2]
            balance = (
                WEIGHTS[which] * density * (1.0 + 3.0 * along + 4.5 * along * along - 1.5 * speed_sq)
            )
            relaxed = populations[which] - RELAX_RATE * (populations[which] - balance)
            if shift_x != 0:
                relaxed = relaxed + 3.0 * WEIGHTS[which] * shift_x * force_field
            posts_ref[which, index, rows] = jnp.where(
                solid_flag, populations[OPPOSITE[which]], relaxed
            )

    inner = slice(0, band_width)
    rim = slice(band_width, band_width + 2)
    collide_into([low_ref[which, 0] for which in range(19)], 0, inner)
    collide_into([high_ref[which, 0] for which in range(19)], slab_len + 1, inner)

    def collide_plane(index, carry):
        collide_into([inner_ref[which, index - 1] for which in range(19)], index, inner)
        return carry

    lax.fori_loop(1, slab_len + 1, collide_plane, 0)

    def collide_rim(index, carry):
        collide_into([rows_ref[which, index] for which in range(19)], index, rim)
        return carry

    lax.fori_loop(0, slab_len + 2, collide_rim, 0)
    lane = lax.broadcasted_iota(jnp.int32, (slab_len, band_width, height), 2)
    row = lax.broadcasted_iota(jnp.int32, (slab_len, band_width, height), 1)
    for which in range(19):
        shift_x, shift_y, shift_z = VELOCITIES[which]
        planes = slice(1 - shift_x, 1 - shift_x + slab_len)
        piece = posts_ref[which, planes, 0:band_width, :]
        if shift_y == 1:
            rim_row = posts_ref[which, planes, band_width : band_width + 1, :]
            piece = jnp.where(row == 0, rim_row, pltpu.roll(piece, 1, 1))
        elif shift_y == -1:
            rim_row = posts_ref[which, planes, band_width + 1 : band_width + 2, :]
            piece = jnp.where(row == band_width - 1, rim_row, pltpu.roll(piece, band_width - 1, 1))
        if shift_z == 1:
            piece = jnp.where(lane == 0, 0.0, pltpu.roll(piece, 1, 2))
        elif shift_z == -1:
            piece = jnp.where(lane == height - 1, 0.0, pltpu.roll(piece, height - 1, 2))
        out_ref[which] = piece
    if not with_moments:
        return
    moments_into(out_ref, discs_ref, solid_ref, 1, velocity_ref, flow_ref, sums_ref)


def moments_into(populations_ref, discs_ref, solid_ref, rim, velocity_ref, flow_ref, sums_ref):
    fans = discs_ref.shape[0]
    band_width = populations_ref.shape[2]
    sums_ref[...] = jnp.zeros(sums_ref.shape, jnp.float32)

    def moment_plane(index, carry):
        density, velocity = plane_moments([populations_ref[which, index] for which in range(19)])
        for dimension in range(3):
            velocity_ref[dimension, index] = velocity[dimension]
        solid_flag = solid_ref[index + rim, 0:band_width, :] != 0.0
        for fan_number in range(fans):
            sums_ref[fan_number] += jnp.where(
                solid_flag, 0.0, discs_ref[fan_number, index + rim, 0:band_width, :] * velocity[0]
            )
        return carry

    lax.fori_loop(0, populations_ref.shape[1], moment_plane, 0)
    for fan_number in range(fans):
        flow_ref[fan_number] = jnp.sum(sums_ref[fan_number])


def first_moments(populations, discs, solid):
    fans, slab_len, band_width, height = discs.shape
    vmem = pl.BlockSpec(memory_space=pltpu.VMEM)
    return pl.pallas_call(
        lambda populations_ref, discs_ref, solid_ref, velocity_ref, flow_ref, sums_ref: moments_into(
            populations_ref, discs_ref, solid_ref, 0, velocity_ref, flow_ref, sums_ref
        ),
        out_shape=(
            jax.ShapeDtypeStruct((3, slab_len, band_width, height), jnp.float32),
            jax.ShapeDtypeStruct((fans,), jnp.float32),
        ),
        in_specs=[vmem, vmem, vmem],
        out_specs=(vmem, pl.BlockSpec(memory_space=pltpu.SMEM)),
        scratch_shapes=[pltpu.VMEM((fans, band_width, height), jnp.float32)],
        cost_estimate=pl.CostEstimate(
            flops=60 * discs[0].size, transcendentals=0, bytes_accessed=4 * populations.size
        ),
    )(populations, discs, solid)


def lattice_step(strength, inner, low, high, rows, discs, solid_rim, with_moments):
    slab_len = inner.shape[1]
    band_width = inner.shape[2]
    height = inner.shape[3]
    fans = discs.shape[0]
    out_shape = [jax.ShapeDtypeStruct((19, slab_len, band_width, height), jnp.float32)]
    if with_moments:
        out_shape.append(jax.ShapeDtypeStruct((3, slab_len, band_width, height), jnp.float32))
        out_shape.append(jax.ShapeDtypeStruct((fans,), jnp.float32))
    scratch = [pltpu.VMEM((19, slab_len + 2, band_width + 2, height), jnp.float32)]
    if with_moments:
        scratch.append(pltpu.VMEM((fans, band_width, height), jnp.float32))
    vmem = pl.BlockSpec(memory_space=pltpu.VMEM)
    return pl.pallas_call(
        functools.partial(step_kernel, with_moments),
        out_shape=tuple(out_shape),
        in_specs=[pl.BlockSpec(memory_space=pltpu.SMEM)] + [vmem] * 6,
        out_specs=tuple(
            [vmem] * (len(out_shape) - 1)
            + [pl.BlockSpec(memory_space=pltpu.SMEM) if with_moments else vmem]
        ),
        scratch_shapes=scratch,
        cost_estimate=pl.CostEstimate(
            flops=300 * solid_rim.size, transcendentals=0, bytes_accessed=12 * inner.size
        ),
    )(strength, inner, low, high, rows, discs, solid_rim)


def disc_count():
    inside = 0
    for offset_a in range(-RAD, RAD + 1):
        for offset_b in range(-RAD, RAD + 1):
            if offset_a * offset_a + offset_b * offset_b <= RAD * RAD:
                inside = inside + 1
    return FAN_LEN * inside


def fan_discs(fan_hubs, coord_x, coord_y, coord_z, length_total):
    discs = []
    for fan_number in range(fan_hubs.shape[0]):
        offset_x = jnp.mod(coord_x - fan_hubs[fan_number, 0], length_total)
        offset_y = coord_y - fan_hubs[fan_number, 1]
        offset_z = coord_z - fan_hubs[fan_number, 2]
        discs.append(
            (offset_x < FAN_LEN) & (offset_y * offset_y + offset_z * offset_z <= RAD * RAD)
        )
    return discs


def partial_flow(discs, velocity, solid_flag):
    return jnp.stack(
        [
            jnp.sum(jnp.where(disc_nodes & jnp.logical_not(solid_flag), velocity[0], 0.0))
            for disc_nodes in discs
        ]
    )


def force_from(discs, totals, fan_gain, jet_speed):
    strength = fan_gain * (jet_speed - totals / float(disc_count()))
    force_field = jnp.zeros(discs[0].shape, jnp.float32)
    for fan_number in range(len(discs)):
        force_field = force_field + jnp.where(discs[fan_number], strength[fan_number], 0.0)
    return force_field


def advance(center, ahead_x, behind_x, ahead_y, behind_y, ahead_z, behind_z, velocity, solid_flag):
    laplace = ahead_x + behind_x + ahead_y + behind_y + ahead_z + behind_z - 6.0 * center
    advect = 0.5 * (
        velocity[0] * (ahead_x - behind_x)
        + velocity[1] * (ahead_y - behind_y)
        + velocity[2] * (ahead_z - behind_z)
    )
    return jnp.where(solid_flag, 0.0, center + DIFFUSIVITY * laplace - advect)


def shift_height(field, shift_z):
    if shift_z == 0:
        return field
    zero_layer = jnp.zeros(field.shape[:-1] + (1,), field.dtype)
    if shift_z == 1:
        return jnp.concatenate([zero_layer, field[..., :-1]], axis=-1)
    return jnp.concatenate([field[..., 1:], zero_layer], axis=-1)


def rim_round(fields, flow, axis, dim, reach):
    count = lax.axis_size(axis)
    fans = flow.shape[0]
    channels = [field.shape[0] for field in fields]

    def piece(start):
        cells = [lax.slice_in_dim(field, start, start + 1, axis=dim) for field in fields]
        carrier = jnp.zeros(cells[0].shape[1:], jnp.float32).at[0, 0, :fans].set(flow)[None]
        return jnp.concatenate(cells + [carrier], axis=0)

    head = piece(0)
    tail = piece(fields[0].shape[dim] - 1)
    forward = [(i, (i + 1) % count) for i in range(count)]
    backward = [((i + 1) % count, i) for i in range(count)]
    both = None
    if count == 2:
        both = lax.ppermute(jnp.concatenate([tail, head], axis=dim), axis, forward)
        from_left = lax.slice_in_dim(both, 0, 1, axis=dim)
        from_right = lax.slice_in_dim(both, 1, 2, axis=dim)
        total = flow + from_left[-1, 0, 0, :fans]
    else:
        from_left = lax.ppermute(tail, axis, forward)
        from_right = lax.ppermute(head, axis, backward)
        total = flow + from_left[-1, 0, 0, :fans] + from_right[-1, 0, 0, :fans]
    for offset in sorted(set(step % count for step in range(-reach, reach + 1)) - {0, 1, count - 1}):
        total = total + lax.ppermute(flow, axis, [(i, (i + offset) % count) for i in range(count)])
    extended = [(from_left, from_right, both)]
    first = channels[0]
    for field, channel in zip(fields[1:], channels[1:]):
        left = from_left[first : first + channel]
        right = from_right[first : first + channel]
        if dim == 1:
            extended.append(jnp.concatenate([left, field, right], axis=dim))
        else:
            extended.append(jnp.concatenate([field, left, right], axis=dim))
        first = first + channel
    return (extended, total)


def window_sum(values, axis, width):
    count = lax.axis_size(axis)
    total = values
    for offset in sorted(set(step % count for step in range(-width, width + 1)) - {0}):
        total = total + lax.ppermute(
            values, axis, [(i, (i + offset) % count) for i in range(count)]
        )
    return total


def source_release(sources, source_rate, offset_len, offset_band, slab_len, band_width, height):
    local_x = sources[:, 0] - offset_len
    local_y = sources[:, 1] - offset_band
    pick_x = (local_x[:, None] == jnp.arange(slab_len, dtype=jnp.int32)[None, :]).astype(
        jnp.float32
    )
    pick_y = (local_y[:, None] == jnp.arange(band_width, dtype=jnp.int32)[None, :]).astype(
        jnp.float32
    )
    pick_z = (sources[:, 2][:, None] == jnp.arange(height, dtype=jnp.int32)[None, :]).astype(
        jnp.float32
    )
    weighted = source_rate[:, None] * pick_x
    cross_table = (pick_y[:, :, None] * pick_z[:, None, :]).reshape(
        sources.shape[0], band_width * height
    )
    released = jnp.dot(
        weighted.T, cross_table, precision=lax.Precision.HIGHEST, preferred_element_type=jnp.float32
    )
    return released.reshape(slab_len, band_width, height)


def body(populations, solid_mask, smoke_field, fan_hubs, fan_gain, jet_speed, sources, source_rate):
    slab_len = populations.shape[1]
    band_width = populations.shape[2]
    height = populations.shape[3]
    offset_len = lax.axis_index("len") * slab_len
    offset_band = lax.axis_index("band") * band_width
    length_total = slab_len * lax.axis_size("len")
    breadth_total = band_width * lax.axis_size("band")
    solid_flag = solid_mask == 1
    coord_x = offset_len - 1 + jnp.arange(slab_len + 2, dtype=jnp.int32)
    coord_y = jnp.mod(
        offset_band
        + jnp.concatenate(
            [jnp.arange(band_width, dtype=jnp.int32), jnp.array([-1, band_width], jnp.int32)]
        ),
        breadth_total,
    )
    coord_z = jnp.arange(height, dtype=jnp.int32)
    along_in = jnp.mod(coord_x[None, :] - fan_hubs[:, 0:1], length_total) < FAN_LEN
    offset_y = coord_y[None, :] - fan_hubs[:, 1:2]
    offset_z = coord_z[None, :] - fan_hubs[:, 2:3]
    across_in = (
        offset_y[:, :, None] * offset_y[:, :, None] + offset_z[:, None, :] * offset_z[:, None, :]
        <= RAD * RAD
    )
    released = source_release(
        sources, source_rate, offset_len, offset_band, slab_len, band_width, height
    )
    len_reach = max(-(-FAN_LEN // slab_len), (slab_len + FAN_LEN - 1) // slab_len)
    band_reach = max(-(-(2 * RAD + 1) // band_width), (band_width + 2 * RAD) // band_width)
    discs = (along_in[:, :, None, None] & across_in[:, None]).astype(jnp.float32)
    solid_planes = solid_flag.astype(jnp.float32)
    velocity, flow = first_moments(populations, discs[:, 1:-1, 0:band_width], solid_planes)
    partials = flow
    for repeat in range(ITERS):
        fields = [populations, smoke_field[None]]
        if repeat == 0:
            fields.append(solid_planes[None])
        fields, totals = rim_round(fields, partials, "len", 1, len_reach)
        low, high, _ = fields[0]
        fields[0] = jnp.concatenate([low[:19], populations, high[:19]], axis=1)
        fields, totals = rim_round(fields, totals, "band", 2, band_reach)
        if fields[0][2] is None:
            rows = jnp.concatenate([fields[0][0][:19], fields[0][1][:19]], axis=2)
        else:
            rows = fields[0][2]
        rimmed = fields[1][0]
        if repeat == 0:
            solid_rim = fields[2][0]
        strength = fan_gain * (jet_speed - totals / float(disc_count()))
        last = repeat == ITERS - 1
        stepped = lattice_step(strength, populations, low, high, rows, discs, solid_rim, not last)
        ahead_x = rimmed[2:, 0:band_width]
        behind_x = rimmed[:-2, 0:band_width]
        ahead_y = jnp.concatenate(
            [rimmed[1:-1, 1:band_width], rimmed[1:-1, band_width + 1 : band_width + 2]], axis=1
        )
        behind_y = jnp.concatenate(
            [rimmed[1:-1, band_width : band_width + 1], rimmed[1:-1, 0 : band_width - 1]], axis=1
        )
        smoke_field = advance(
            smoke_field,
            ahead_x,
            behind_x,
            ahead_y,
            behind_y,
            shift_height(smoke_field, -1),
            shift_height(smoke_field, 1),
            velocity,
            solid_flag,
        )
        smoke_field = smoke_field + released
        populations = stepped[0]
        if not last:
            velocity = stepped[1]
            partials = stepped[2]
    return (populations, smoke_field)


def solution(mesh):
    placed = (
        P(None, "len", "band", None),
        P("len", "band", None),
        P("len", "band", None),
        P(),
        P(),
        P(),
        P(),
        P(),
    )
    return jax.shard_map(
        body,
        mesh=mesh,
        in_specs=placed,
        out_specs=(P(None, "len", "band", None), P("len", "band", None)),
        check_vma=False,
    )
```

```python
import functools

import jax
import jax.numpy as jnp
from jax import lax
from jax.experimental import pallas as pl
from jax.experimental.pallas import tpu as pltpu
from jax.sharding import PartitionSpec as P

RAD = 3
FAN_LEN = 16
ITERS = 3


VELOCITIES = (
    (0, 0, 0),
    (1, 0, 0),
    (-1, 0, 0),
    (0, 1, 0),
    (0, -1, 0),
    (0, 0, 1),
    (0, 0, -1),
    (1, 1, 0),
    (-1, -1, 0),
    (1, -1, 0),
    (-1, 1, 0),
    (1, 0, 1),
    (-1, 0, -1),
    (1, 0, -1),
    (-1, 0, 1),
    (0, 1, 1),
    (0, -1, -1),
    (0, 1, -1),
    (0, -1, 1),
)
WEIGHTS = (1.0 / 3.0,) + (1.0 / 18.0,) * 6 + (1.0 / 36.0,) * 12
OPPOSITE = (0, 2, 1, 4, 3, 6, 5, 8, 7, 10, 9, 12, 11, 14, 13, 16, 15, 18, 17)
RELAX_RATE = 1.0 / 0.6
DIFFUSIVITY = 0.12


def extended_2(cells, sides, width):
    for axis, dim in sides:
        count = lax.axis_size(axis)
        head = lax.slice_in_dim(cells, 0, width, axis=dim)
        tail = lax.slice_in_dim(cells, cells.shape[dim] - width, cells.shape[dim], axis=dim)
        cells = jnp.concatenate(
            [
                lax.ppermute(tail, axis, [(i, (i + 1) % count) for i in range(count)]),
                cells,
                lax.ppermute(head, axis, [((i + 1) % count, i) for i in range(count)]),
            ],
            axis=dim,
        )
    return cells


def moments(populations):
    density = jnp.sum(populations, axis=0)
    velocity = []
    for dimension in range(3):
        forward = [populations[which] for which in range(19) if VELOCITIES[which][dimension] == 1]
        backward = [populations[which] for which in range(19) if VELOCITIES[which][dimension] == -1]
        velocity.append((sum(forward) - sum(backward)) / density)
    return (density, velocity)


def plane_moments(populations):
    density = sum(populations[1:], populations[0])
    velocity = []
    for dimension in range(3):
        forward = [populations[which] for which in range(19) if VELOCITIES[which][dimension] == 1]
        backward = [populations[which] for which in range(19) if VELOCITIES[which][dimension] == -1]
        velocity.append((sum(forward) - sum(backward)) / density)
    return (density, velocity)


def step_kernel(
    with_moments, strength_ref, inner_ref, low_ref, high_ref, rows_ref, discs_ref, solid_ref, *rest
):
    if with_moments:
        out_ref, velocity_ref, flow_ref, posts_ref, sums_ref = rest
    else:
        out_ref, posts_ref = rest
    fans = discs_ref.shape[0]
    slab_len, band_width, height = out_ref.shape[1:]

    def collide_into(populations, index, rows):
        density, velocity = plane_moments(populations)
        force_field = strength_ref[0] * discs_ref[0, index, rows]
        for fan_number in range(1, fans):
            force_field = force_field + strength_ref[fan_number] * discs_ref[fan_number, index, rows]
        solid_flag = solid_ref[index, rows] != 0.0
        speed_sq = velocity[0] * velocity[0] + velocity[1] * velocity[1] + velocity[2] * velocity[2]
        for which in range(19):
            shift_x, shift_y, shift_z = VELOCITIES[which]
            along = shift_x * velocity[0] + shift_y * velocity[1] + shift_z * velocity[2]
            balance = (
                WEIGHTS[which] * density * (1.0 + 3.0 * along + 4.5 * along * along - 1.5 * speed_sq)
            )
            relaxed = populations[which] - RELAX_RATE * (populations[which] - balance)
            if shift_x != 0:
                relaxed = relaxed + 3.0 * WEIGHTS[which] * shift_x * force_field
            posts_ref[which, index, rows] = jnp.where(
                solid_flag, populations[OPPOSITE[which]], relaxed
            )

    inner = slice(0, band_width)
    rim = slice(band_width, band_width + 2)
    collide_into([low_ref[which, 0] for which in range(19)], 0, inner)
    collide_into([high_ref[which, 0] for which in range(19)], slab_len + 1, inner)

    def collide_plane(index, carry):
        collide_into([inner_ref[which, index - 1] for which in range(19)], index, inner)
        return carry

    lax.fori_loop(1, slab_len + 1, collide_plane, 0)

    def collide_rim(index, carry):
        collide_into([rows_ref[which, index] for which in range(19)], index, rim)
        return carry

    lax.fori_loop(0, slab_len + 2, collide_rim, 0)
    lane = lax.broadcasted_iota(jnp.int32, (slab_len, band_width, height), 2)
    row = lax.broadcasted_iota(jnp.int32, (slab_len, band_width, height), 1)
    for which in range(19):
        shift_x, shift_y, shift_z = VELOCITIES[which]
        planes = slice(1 - shift_x, 1 - shift_x + slab_len)
        piece = posts_ref[which, planes, 0:band_width, :]
        if shift_y == 1:
            rim_row = posts_ref[which, planes, band_width : band_width + 1, :]
            piece = jnp.where(row == 0, rim_row, pltpu.roll(piece, 1, 1))
        elif shift_y == -1:
            rim_row = posts_ref[which, planes, band_width + 1 : band_width + 2, :]
            piece = jnp.where(row == band_width - 1, rim_row, pltpu.roll(piece, band_width - 1, 1))
        if shift_z == 1:
            piece = jnp.where(lane == 0, 0.0, pltpu.roll(piece, 1, 2))
        elif shift_z == -1:
            piece = jnp.where(lane == height - 1, 0.0, pltpu.roll(piece, height - 1, 2))
        out_ref[which] = piece
    if not with_moments:
        return
    moments_into(out_ref, discs_ref, solid_ref, 1, velocity_ref, flow_ref, sums_ref)


def moments_into(populations_ref, discs_ref, solid_ref, rim, velocity_ref, flow_ref, sums_ref):
    fans = discs_ref.shape[0]
    band_width = populations_ref.shape[2]
    sums_ref[...] = jnp.zeros(sums_ref.shape, jnp.float32)

    def moment_plane(index, carry):
        density, velocity = plane_moments([populations_ref[which, index] for which in range(19)])
        for dimension in range(3):
            velocity_ref[dimension, index] = velocity[dimension]
        solid_flag = solid_ref[index + rim, 0:band_width, :] != 0
        for fan_number in range(fans):
            sums_ref[fan_number] += jnp.where(
                solid_flag, 0.0, discs_ref[fan_number, index + rim, 0:band_width, :] * velocity[0]
            )
        return carry

    lax.fori_loop(0, populations_ref.shape[1], moment_plane, 0)
    for fan_number in range(fans):
        flow_ref[fan_number] = jnp.sum(sums_ref[fan_number])


def first_moments(populations, discs, solid):
    fans, slab_len, band_width, height = discs.shape
    vmem = pl.BlockSpec(memory_space=pltpu.VMEM)
    return pl.pallas_call(
        lambda populations_ref, discs_ref, solid_ref, velocity_ref, flow_ref, sums_ref: moments_into(
            populations_ref, discs_ref, solid_ref, 0, velocity_ref, flow_ref, sums_ref
        ),
        out_shape=(
            jax.ShapeDtypeStruct((3, slab_len, band_width, height), jnp.float32),
            jax.ShapeDtypeStruct((fans,), jnp.float32),
        ),
        in_specs=[vmem, vmem, vmem],
        out_specs=(vmem, pl.BlockSpec(memory_space=pltpu.SMEM)),
        scratch_shapes=[pltpu.VMEM((fans, band_width, height), jnp.float32)],
        cost_estimate=pl.CostEstimate(
            flops=60 * discs[0].size, transcendentals=0, bytes_accessed=4 * populations.size
        ),
    )(populations, discs, solid)


def lattice_step(strength, inner, low, high, rows, discs, solid_rim, with_moments):
    slab_len = inner.shape[1]
    band_width = inner.shape[2]
    height = inner.shape[3]
    fans = discs.shape[0]
    out_shape = [jax.ShapeDtypeStruct((19, slab_len, band_width, height), jnp.float32)]
    if with_moments:
        out_shape.append(jax.ShapeDtypeStruct((3, slab_len, band_width, height), jnp.float32))
        out_shape.append(jax.ShapeDtypeStruct((fans,), jnp.float32))
    scratch = [pltpu.VMEM((19, slab_len + 2, band_width + 2, height), jnp.float32)]
    if with_moments:
        scratch.append(pltpu.VMEM((fans, band_width, height), jnp.float32))
    vmem = pl.BlockSpec(memory_space=pltpu.VMEM)
    return pl.pallas_call(
        functools.partial(step_kernel, with_moments),
        out_shape=tuple(out_shape),
        in_specs=[pl.BlockSpec(memory_space=pltpu.SMEM)] + [vmem] * 6,
        out_specs=tuple(
            [vmem] * (len(out_shape) - 1)
            + [pl.BlockSpec(memory_space=pltpu.SMEM) if with_moments else vmem]
        ),
        scratch_shapes=scratch,
        cost_estimate=pl.CostEstimate(
            flops=300 * solid_rim.size, transcendentals=0, bytes_accessed=12 * inner.size
        ),
    )(strength, inner, low, high, rows, discs, solid_rim)


def disc_count():
    inside = 0
    for offset_a in range(-RAD, RAD + 1):
        for offset_b in range(-RAD, RAD + 1):
            if offset_a * offset_a + offset_b * offset_b <= RAD * RAD:
                inside = inside + 1
    return FAN_LEN * inside


def fan_discs(fan_hubs, coord_x, coord_y, coord_z, length_total):
    discs = []
    for fan_number in range(fan_hubs.shape[0]):
        offset_x = jnp.mod(coord_x - fan_hubs[fan_number, 0], length_total)
        offset_y = coord_y - fan_hubs[fan_number, 1]
        offset_z = coord_z - fan_hubs[fan_number, 2]
        discs.append(
            (offset_x < FAN_LEN) & (offset_y * offset_y + offset_z * offset_z <= RAD * RAD)
        )
    return discs


def partial_flow(discs, velocity, solid_flag):
    return jnp.stack(
        [
            jnp.sum(jnp.where(disc_nodes & jnp.logical_not(solid_flag), velocity[0], 0.0))
            for disc_nodes in discs
        ]
    )


def force_from(discs, totals, fan_gain, jet_speed):
    strength = fan_gain * (jet_speed - totals / float(disc_count()))
    force_field = jnp.zeros(discs[0].shape, jnp.float32)
    for fan_number in range(len(discs)):
        force_field = force_field + jnp.where(discs[fan_number], strength[fan_number], 0.0)
    return force_field


def advance(center, ahead_x, behind_x, ahead_y, behind_y, ahead_z, behind_z, velocity, solid_flag):
    laplace = ahead_x + behind_x + ahead_y + behind_y + ahead_z + behind_z - 6.0 * center
    advect = 0.5 * (
        velocity[0] * (ahead_x - behind_x)
        + velocity[1] * (ahead_y - behind_y)
        + velocity[2] * (ahead_z - behind_z)
    )
    return jnp.where(solid_flag, 0.0, center + DIFFUSIVITY * laplace - advect)


def shift_height(field, shift_z):
    if shift_z == 0:
        return field
    zero_layer = jnp.zeros(field.shape[:-1] + (1,), field.dtype)
    if shift_z == 1:
        return jnp.concatenate([zero_layer, field[..., :-1]], axis=-1)
    return jnp.concatenate([field[..., 1:], zero_layer], axis=-1)


def rim_round(fields, flow, axis, dim, reach):
    count = lax.axis_size(axis)
    fans = flow.shape[0]
    channels = [field.shape[0] for field in fields]

    def piece(start):
        cells = [lax.slice_in_dim(field, start, start + 1, axis=dim) for field in fields]
        carrier = jnp.zeros(cells[0].shape[1:], jnp.float32).at[0, 0, :fans].set(flow)[None]
        return jnp.concatenate(cells + [carrier], axis=0)

    head = piece(0)
    tail = piece(fields[0].shape[dim] - 1)
    forward = [(i, (i + 1) % count) for i in range(count)]
    backward = [((i + 1) % count, i) for i in range(count)]
    both = None
    if count == 2:
        both = lax.ppermute(jnp.concatenate([tail, head], axis=dim), axis, forward)
        from_left = lax.slice_in_dim(both, 0, 1, axis=dim)
        from_right = lax.slice_in_dim(both, 1, 2, axis=dim)
        total = flow + from_left[-1, 0, 0, :fans]
    else:
        from_left = lax.ppermute(tail, axis, forward)
        from_right = lax.ppermute(head, axis, backward)
        total = flow + from_left[-1, 0, 0, :fans] + from_right[-1, 0, 0, :fans]
    for offset in sorted(set(step % count for step in range(-reach, reach + 1)) - {0, 1, count - 1}):
        total = total + lax.ppermute(flow, axis, [(i, (i + offset) % count) for i in range(count)])
    extended = [(from_left, from_right, both)]
    first = channels[0]
    for field, channel in zip(fields[1:], channels[1:]):
        left = from_left[first : first + channel]
        right = from_right[first : first + channel]
        if dim == 1:
            extended.append(jnp.concatenate([left, field, right], axis=dim))
        else:
            extended.append(jnp.concatenate([field, left, right], axis=dim))
        first = first + channel
    return (extended, total)


def window_sum(values, axis, width):
    count = lax.axis_size(axis)
    total = values
    for offset in sorted(set(step % count for step in range(-width, width + 1)) - {0}):
        total = total + lax.ppermute(
            values, axis, [(i, (i + offset) % count) for i in range(count)]
        )
    return total


def source_release(sources, source_rate, offset_len, offset_band, slab_len, band_width, height):
    local_x = sources[:, 0] - offset_len
    local_y = sources[:, 1] - offset_band
    pick_x = (local_x[:, None] == jnp.arange(slab_len, dtype=jnp.int32)[None, :]).astype(
        jnp.float32
    )
    pick_y = (local_y[:, None] == jnp.arange(band_width, dtype=jnp.int32)[None, :]).astype(
        jnp.float32
    )
    pick_z = (sources[:, 2][:, None] == jnp.arange(height, dtype=jnp.int32)[None, :]).astype(
        jnp.float32
    )
    weighted = source_rate[:, None] * pick_x
    cross_table = (pick_y[:, :, None] * pick_z[:, None, :]).reshape(
        sources.shape[0], band_width * height
    )
    released = jnp.dot(
        weighted.T, cross_table, precision=lax.Precision.HIGHEST, preferred_element_type=jnp.float32
    )
    return released.reshape(slab_len, band_width, height)


def body(populations, solid_mask, smoke_field, fan_hubs, fan_gain, jet_speed, sources, source_rate):
    slab_len = populations.shape[1]
    band_width = populations.shape[2]
    height = populations.shape[3]
    offset_len = lax.axis_index("len") * slab_len
    offset_band = lax.axis_index("band") * band_width
    length_total = slab_len * lax.axis_size("len")
    breadth_total = band_width * lax.axis_size("band")
    solid_flag = solid_mask == 1
    coord_x = offset_len - 1 + jnp.arange(slab_len + 2, dtype=jnp.int32)
    coord_y = jnp.mod(
        offset_band
        + jnp.concatenate(
            [jnp.arange(band_width, dtype=jnp.int32), jnp.array([-1, band_width], jnp.int32)]
        ),
        breadth_total,
    )
    coord_z = jnp.arange(height, dtype=jnp.int32)
    along_in = jnp.mod(coord_x[None, :] - fan_hubs[:, 0:1], length_total) < FAN_LEN
    offset_y = coord_y[None, :] - fan_hubs[:, 1:2]
    offset_z = coord_z[None, :] - fan_hubs[:, 2:3]
    across_in = (
        offset_y[:, :, None] * offset_y[:, :, None] + offset_z[:, None, :] * offset_z[:, None, :]
        <= RAD * RAD
    )
    released = source_release(
        sources, source_rate, offset_len, offset_band, slab_len, band_width, height
    )
    len_reach = max(-(-FAN_LEN // slab_len), (slab_len + FAN_LEN - 1) // slab_len)
    band_reach = max(-(-(2 * RAD + 1) // band_width), (band_width + 2 * RAD) // band_width)
    discs = (along_in[:, :, None, None] & across_in[:, None]).astype(jnp.float32)
    solid_planes = solid_flag.astype(jnp.float32)
    velocity, flow = first_moments(populations, discs[:, 1:-1, 0:band_width], solid_mask)
    partials = flow
    for repeat in range(ITERS):
        fields = [populations, smoke_field[None]]
        if repeat == 0:
            fields.append(solid_planes[None])
        fields, totals = rim_round(fields, partials, "len", 1, len_reach)
        low, high, _ = fields[0]
        fields[0] = jnp.concatenate([low[:19], populations, high[:19]], axis=1)
        fields, totals = rim_round(fields, totals, "band", 2, band_reach)
        if fields[0][2] is None:
            rows = jnp.concatenate([fields[0][0][:19], fields[0][1][:19]], axis=2)
        else:
            rows = fields[0][2]
        rimmed = fields[1][0]
        if repeat == 0:
            solid_rim = fields[2][0]
        strength = fan_gain * (jet_speed - totals / float(disc_count()))
        last = repeat == ITERS - 1
        stepped = lattice_step(strength, populations, low, high, rows, discs, solid_rim, not last)
        ahead_x = rimmed[2:, 0:band_width]
        behind_x = rimmed[:-2, 0:band_width]
        ahead_y = jnp.concatenate(
            [rimmed[1:-1, 1:band_width], rimmed[1:-1, band_width + 1 : band_width + 2]], axis=1
        )
        behind_y = jnp.concatenate(
            [rimmed[1:-1, band_width : band_width + 1], rimmed[1:-1, 0 : band_width - 1]], axis=1
        )
        smoke_field = advance(
            smoke_field,
            ahead_x,
            behind_x,
            ahead_y,
            behind_y,
            shift_height(smoke_field, -1),
            shift_height(smoke_field, 1),
            velocity,
            solid_flag,
        )
        smoke_field = smoke_field + released
        populations = stepped[0]
        if not last:
            velocity = stepped[1]
            partials = stepped[2]
    return (populations, smoke_field)


def solution(mesh):
    placed = (
        P(None, "len", "band", None),
        P("len", "band", None),
        P("len", "band", None),
        P(),
        P(),
        P(),
        P(),
        P(),
    )
    return jax.shard_map(
        body,
        mesh=mesh,
        in_specs=placed,
        out_specs=(P(None, "len", "band", None), P("len", "band", None)),
        check_vma=False,
    )
```

```python
import functools

import jax
import jax.numpy as jnp
from jax import lax
from jax.experimental import pallas as pl
from jax.experimental.pallas import tpu as pltpu
from jax.sharding import PartitionSpec as P

RAD = 3
FAN_LEN = 16
ITERS = 3


VELOCITIES = (
    (0, 0, 0),
    (1, 0, 0),
    (-1, 0, 0),
    (0, 1, 0),
    (0, -1, 0),
    (0, 0, 1),
    (0, 0, -1),
    (1, 1, 0),
    (-1, -1, 0),
    (1, -1, 0),
    (-1, 1, 0),
    (1, 0, 1),
    (-1, 0, -1),
    (1, 0, -1),
    (-1, 0, 1),
    (0, 1, 1),
    (0, -1, -1),
    (0, 1, -1),
    (0, -1, 1),
)
WEIGHTS = (1.0 / 3.0,) + (1.0 / 18.0,) * 6 + (1.0 / 36.0,) * 12
OPPOSITE = (0, 2, 1, 4, 3, 6, 5, 8, 7, 10, 9, 12, 11, 14, 13, 16, 15, 18, 17)
RELAX_RATE = 1.0 / 0.6
DIFFUSIVITY = 0.12


def extended_2(cells, sides, width):
    for axis, dim in sides:
        count = lax.axis_size(axis)
        head = lax.slice_in_dim(cells, 0, width, axis=dim)
        tail = lax.slice_in_dim(cells, cells.shape[dim] - width, cells.shape[dim], axis=dim)
        cells = jnp.concatenate(
            [
                lax.ppermute(tail, axis, [(i, (i + 1) % count) for i in range(count)]),
                cells,
                lax.ppermute(head, axis, [((i + 1) % count, i) for i in range(count)]),
            ],
            axis=dim,
        )
    return cells


def moments(populations):
    density = jnp.sum(populations, axis=0)
    velocity = []
    for dimension in range(3):
        forward = [populations[which] for which in range(19) if VELOCITIES[which][dimension] == 1]
        backward = [populations[which] for which in range(19) if VELOCITIES[which][dimension] == -1]
        velocity.append((sum(forward) - sum(backward)) / density)
    return (density, velocity)


def plane_moments(populations):
    density = sum(populations[1:], populations[0])
    velocity = []
    for dimension in range(3):
        forward = [populations[which] for which in range(19) if VELOCITIES[which][dimension] == 1]
        backward = [populations[which] for which in range(19) if VELOCITIES[which][dimension] == -1]
        velocity.append((sum(forward) - sum(backward)) / density)
    return (density, velocity)


def step_kernel(
    with_moments, strength_ref, inner_ref, low_ref, high_ref, rows_ref, discs_ref, solid_ref, *rest
):
    if with_moments:
        out_ref, velocity_ref, flow_ref, posts_ref, sums_ref = rest
    else:
        out_ref, posts_ref = rest
    fans = discs_ref.shape[0]
    slab_len, band_width, height = out_ref.shape[1:]

    def collide_into(populations, index, rows):
        density, velocity = plane_moments(populations)
        force_field = strength_ref[0] * discs_ref[0, index, rows]
        for fan_number in range(1, fans):
            force_field = force_field + strength_ref[fan_number] * discs_ref[fan_number, index, rows]
        solid_flag = solid_ref[index, rows] != 0.0
        speed_sq = velocity[0] * velocity[0] + velocity[1] * velocity[1] + velocity[2] * velocity[2]
        for which in range(19):
            shift_x, shift_y, shift_z = VELOCITIES[which]
            along = shift_x * velocity[0] + shift_y * velocity[1] + shift_z * velocity[2]
            balance = (
                WEIGHTS[which] * density * (1.0 + 3.0 * along + 4.5 * along * along - 1.5 * speed_sq)
            )
            relaxed = populations[which] - RELAX_RATE * (populations[which] - balance)
            if shift_x != 0:
                relaxed = relaxed + 3.0 * WEIGHTS[which] * shift_x * force_field
            posts_ref[which, index, rows] = jnp.where(
                solid_flag, populations[OPPOSITE[which]], relaxed
            )

    inner = slice(0, band_width)
    rim = slice(band_width, band_width + 2)
    collide_into([low_ref[which, 0] for which in range(19)], 0, inner)
    collide_into([high_ref[which, 0] for which in range(19)], slab_len + 1, inner)

    def collide_plane(index, carry):
        collide_into([inner_ref[which, index - 1] for which in range(19)], index, inner)
        return carry

    lax.fori_loop(1, slab_len + 1, collide_plane, 0)

    def collide_rim(index, carry):
        collide_into([rows_ref[which, index] for which in range(19)], index, rim)
        return carry

    lax.fori_loop(0, slab_len + 2, collide_rim, 0)
    lane = lax.broadcasted_iota(jnp.int32, (slab_len, band_width, height), 2)
    row = lax.broadcasted_iota(jnp.int32, (slab_len, band_width, height), 1)
    for which in range(19):
        shift_x, shift_y, shift_z = VELOCITIES[which]
        planes = slice(1 - shift_x, 1 - shift_x + slab_len)
        piece = posts_ref[which, planes, 0:band_width, :]
        if shift_y == 1:
            rim_row = posts_ref[which, planes, band_width : band_width + 1, :]
            piece = jnp.where(row == 0, rim_row, pltpu.roll(piece, 1, 1))
        elif shift_y == -1:
            rim_row = posts_ref[which, planes, band_width + 1 : band_width + 2, :]
            piece = jnp.where(row == band_width - 1, rim_row, pltpu.roll(piece, band_width - 1, 1))
        if shift_z == 1:
            piece = jnp.where(lane == 0, 0.0, pltpu.roll(piece, 1, 2))
        elif shift_z == -1:
            piece = jnp.where(lane == height - 1, 0.0, pltpu.roll(piece, height - 1, 2))
        out_ref[which] = piece
    if not with_moments:
        return
    moments_into(out_ref, discs_ref, solid_ref, 1, velocity_ref, flow_ref, sums_ref)


def moments_into(populations_ref, discs_ref, solid_ref, rim, velocity_ref, flow_ref, sums_ref):
    fans = discs_ref.shape[0]
    band_width = populations_ref.shape[2]
    sums_ref[...] = jnp.zeros(sums_ref.shape, jnp.float32)

    def moment_plane(index, carry):
        density, velocity = plane_moments([populations_ref[which, index] for which in range(19)])
        for dimension in range(3):
            velocity_ref[dimension, index] = velocity[dimension]
        solid_flag = solid_ref[index + rim, 0:band_width, :] != 0
        for fan_number in range(fans):
            sums_ref[fan_number] += jnp.where(
                solid_flag, 0.0, discs_ref[fan_number, index + rim, 0:band_width, :] * velocity[0]
            )
        return carry

    lax.fori_loop(0, populations_ref.shape[1], moment_plane, 0)
    for fan_number in range(fans):
        flow_ref[fan_number] = jnp.sum(sums_ref[fan_number])


def first_moments(populations, discs, solid):
    fans, slab_len, band_width, height = discs.shape
    vmem = pl.BlockSpec(memory_space=pltpu.VMEM)
    return pl.pallas_call(
        lambda populations_ref, discs_ref, solid_ref, velocity_ref, flow_ref, sums_ref: moments_into(
            populations_ref, discs_ref, solid_ref, 0, velocity_ref, flow_ref, sums_ref
        ),
        out_shape=(
            jax.ShapeDtypeStruct((3, slab_len, band_width, height), jnp.float32),
            jax.ShapeDtypeStruct((fans,), jnp.float32),
        ),
        in_specs=[vmem, vmem, vmem],
        out_specs=(vmem, pl.BlockSpec(memory_space=pltpu.SMEM)),
        scratch_shapes=[pltpu.VMEM((fans, band_width, height), jnp.float32)],
        cost_estimate=pl.CostEstimate(
            flops=60 * discs[0].size, transcendentals=0, bytes_accessed=4 * populations.size
        ),
    )(populations, discs, solid)


def lattice_step(strength, inner, low, high, rows, discs, solid_rim, with_moments):
    slab_len = inner.shape[1]
    band_width = inner.shape[2]
    height = inner.shape[3]
    fans = discs.shape[0]
    out_shape = [jax.ShapeDtypeStruct((19, slab_len, band_width, height), jnp.float32)]
    if with_moments:
        out_shape.append(jax.ShapeDtypeStruct((3, slab_len, band_width, height), jnp.float32))
        out_shape.append(jax.ShapeDtypeStruct((fans,), jnp.float32))
    scratch = [pltpu.VMEM((19, slab_len + 2, band_width + 2, height), jnp.float32)]
    if with_moments:
        scratch.append(pltpu.VMEM((fans, band_width, height), jnp.float32))
    vmem = pl.BlockSpec(memory_space=pltpu.VMEM)
    return pl.pallas_call(
        functools.partial(step_kernel, with_moments),
        out_shape=tuple(out_shape),
        in_specs=[pl.BlockSpec(memory_space=pltpu.SMEM)] + [vmem] * 6,
        out_specs=tuple(
            [vmem] * (len(out_shape) - 1)
            + [pl.BlockSpec(memory_space=pltpu.SMEM) if with_moments else vmem]
        ),
        scratch_shapes=scratch,
        cost_estimate=pl.CostEstimate(
            flops=300 * solid_rim.size, transcendentals=0, bytes_accessed=12 * inner.size
        ),
    )(strength, inner, low, high, rows, discs, solid_rim)


def disc_count():
    inside = 0
    for offset_a in range(-RAD, RAD + 1):
        for offset_b in range(-RAD, RAD + 1):
            if offset_a * offset_a + offset_b * offset_b <= RAD * RAD:
                inside = inside + 1
    return FAN_LEN * inside


def fan_discs(fan_hubs, coord_x, coord_y, coord_z, length_total):
    discs = []
    for fan_number in range(fan_hubs.shape[0]):
        offset_x = jnp.mod(coord_x - fan_hubs[fan_number, 0], length_total)
        offset_y = coord_y - fan_hubs[fan_number, 1]
        offset_z = coord_z - fan_hubs[fan_number, 2]
        discs.append(
            (offset_x < FAN_LEN) & (offset_y * offset_y + offset_z * offset_z <= RAD * RAD)
        )
    return discs


def partial_flow(discs, velocity, solid_flag):
    return jnp.stack(
        [
            jnp.sum(jnp.where(disc_nodes & jnp.logical_not(solid_flag), velocity[0], 0.0))
            for disc_nodes in discs
        ]
    )


def force_from(discs, totals, fan_gain, jet_speed):
    strength = fan_gain * (jet_speed - totals / float(disc_count()))
    force_field = jnp.zeros(discs[0].shape, jnp.float32)
    for fan_number in range(len(discs)):
        force_field = force_field + jnp.where(discs[fan_number], strength[fan_number], 0.0)
    return force_field


def advance(center, ahead_x, behind_x, ahead_y, behind_y, ahead_z, behind_z, velocity, solid_flag):
    laplace = ahead_x + behind_x + ahead_y + behind_y + ahead_z + behind_z - 6.0 * center
    advect = 0.5 * (
        velocity[0] * (ahead_x - behind_x)
        + velocity[1] * (ahead_y - behind_y)
        + velocity[2] * (ahead_z - behind_z)
    )
    return jnp.where(solid_flag, 0.0, center + DIFFUSIVITY * laplace - advect)


def shift_height(field, shift_z):
    if shift_z == 0:
        return field
    zero_layer = jnp.zeros(field.shape[:-1] + (1,), field.dtype)
    if shift_z == 1:
        return jnp.concatenate([zero_layer, field[..., :-1]], axis=-1)
    return jnp.concatenate([field[..., 1:], zero_layer], axis=-1)


def rim_round(fields, flow, axis, dim, reach):
    count = lax.axis_size(axis)
    fans = flow.shape[0]
    channels = [field.shape[0] for field in fields]

    def piece(start):
        cells = [lax.slice_in_dim(field, start, start + 1, axis=dim) for field in fields]
        carrier = jnp.zeros(cells[0].shape[1:], jnp.float32).at[0, 0, :fans].set(flow)[None]
        return jnp.concatenate(cells + [carrier], axis=0)

    head = piece(0)
    tail = piece(fields[0].shape[dim] - 1)
    forward = [(i, (i + 1) % count) for i in range(count)]
    backward = [((i + 1) % count, i) for i in range(count)]
    both = None
    if count == 2:
        both = lax.ppermute(jnp.concatenate([tail, head], axis=dim), axis, forward)
        from_left = lax.slice_in_dim(both, 0, 1, axis=dim)
        from_right = lax.slice_in_dim(both, 1, 2, axis=dim)
        total = flow + from_left[-1, 0, 0, :fans]
    else:
        from_left = lax.ppermute(tail, axis, forward)
        from_right = lax.ppermute(head, axis, backward)
        total = flow + from_left[-1, 0, 0, :fans] + from_right[-1, 0, 0, :fans]
    for offset in sorted(set(step % count for step in range(-reach, reach + 1)) - {0, 1, count - 1}):
        total = total + lax.ppermute(flow, axis, [(i, (i + offset) % count) for i in range(count)])
    extended = [(from_left, from_right, both)]
    first = channels[0]
    for field, channel in zip(fields[1:], channels[1:]):
        left = from_left[first : first + channel]
        right = from_right[first : first + channel]
        if dim == 1:
            extended.append(jnp.concatenate([left, field, right], axis=dim))
        else:
            extended.append(jnp.concatenate([field, left, right], axis=dim))
        first = first + channel
    return (extended, total)


def window_sum(values, axis, width):
    count = lax.axis_size(axis)
    total = values
    for offset in sorted(set(step % count for step in range(-width, width + 1)) - {0}):
        total = total + lax.ppermute(
            values, axis, [(i, (i + offset) % count) for i in range(count)]
        )
    return total


def source_release(sources, source_rate, offset_len, offset_band, slab_len, band_width, height):
    local_x = sources[:, 0] - offset_len
    local_y = sources[:, 1] - offset_band
    pick_x = (local_x[:, None] == jnp.arange(slab_len, dtype=jnp.int32)[None, :]).astype(
        jnp.float32
    )
    pick_y = (local_y[:, None] == jnp.arange(band_width, dtype=jnp.int32)[None, :]).astype(
        jnp.float32
    )
    pick_z = (sources[:, 2][:, None] == jnp.arange(height, dtype=jnp.int32)[None, :]).astype(
        jnp.float32
    )
    weighted = source_rate[:, None] * pick_x
    cross_table = (pick_y[:, :, None] * pick_z[:, None, :]).reshape(
        sources.shape[0], band_width * height
    )
    released = jnp.dot(
        weighted.T, cross_table, precision=lax.Precision.HIGHEST, preferred_element_type=jnp.float32
    )
    return released.reshape(slab_len, band_width, height)


def body(populations, solid_mask, smoke_field, fan_hubs, fan_gain, jet_speed, sources, source_rate):
    slab_len = populations.shape[1]
    band_width = populations.shape[2]
    height = populations.shape[3]
    offset_len = lax.axis_index("len") * slab_len
    offset_band = lax.axis_index("band") * band_width
    length_total = slab_len * lax.axis_size("len")
    breadth_total = band_width * lax.axis_size("band")
    solid_flag = solid_mask == 1
    coord_x = offset_len - 1 + jnp.arange(slab_len + 2, dtype=jnp.int32)
    coord_y = jnp.mod(
        offset_band
        + jnp.concatenate(
            [jnp.arange(band_width, dtype=jnp.int32), jnp.array([-1, band_width], jnp.int32)]
        ),
        breadth_total,
    )
    coord_z = jnp.arange(height, dtype=jnp.int32)
    along_in = jnp.mod(coord_x[None, :] - fan_hubs[:, 0:1], length_total) < FAN_LEN
    offset_y = coord_y[None, :] - fan_hubs[:, 1:2]
    offset_z = coord_z[None, :] - fan_hubs[:, 2:3]
    across_in = (
        offset_y[:, :, None] * offset_y[:, :, None] + offset_z[:, None, :] * offset_z[:, None, :]
        <= RAD * RAD
    )
    released = source_release(
        sources, source_rate, offset_len, offset_band, slab_len, band_width, height
    )
    len_reach = max(-(-FAN_LEN // slab_len), (slab_len + FAN_LEN - 1) // slab_len)
    band_reach = max(-(-(2 * RAD + 1) // band_width), (band_width + 2 * RAD) // band_width)
    discs = (along_in[:, :, None, None] & across_in[:, None]).astype(jnp.float32)
    solid_planes = solid_flag.astype(jnp.float32)
    inner_discs = (along_in[:, 1:-1, None, None] & across_in[:, None, 0:band_width]).astype(
        jnp.float32
    )
    velocity, flow = first_moments(populations, inner_discs, solid_mask)
    partials = flow
    for repeat in range(ITERS):
        fields = [populations, smoke_field[None]]
        if repeat == 0:
            fields.append(solid_planes[None])
        fields, totals = rim_round(fields, partials, "len", 1, len_reach)
        low, high, _ = fields[0]
        fields[0] = jnp.concatenate([low[:19], populations, high[:19]], axis=1)
        fields, totals = rim_round(fields, totals, "band", 2, band_reach)
        if fields[0][2] is None:
            rows = jnp.concatenate([fields[0][0][:19], fields[0][1][:19]], axis=2)
        else:
            rows = fields[0][2]
        rimmed = fields[1][0]
        if repeat == 0:
            solid_rim = fields[2][0]
        strength = fan_gain * (jet_speed - totals / float(disc_count()))
        last = repeat == ITERS - 1
        stepped = lattice_step(strength, populations, low, high, rows, discs, solid_rim, not last)
        ahead_x = rimmed[2:, 0:band_width]
        behind_x = rimmed[:-2, 0:band_width]
        ahead_y = jnp.concatenate(
            [rimmed[1:-1, 1:band_width], rimmed[1:-1, band_width + 1 : band_width + 2]], axis=1
        )
        behind_y = jnp.concatenate(
            [rimmed[1:-1, band_width : band_width + 1], rimmed[1:-1, 0 : band_width - 1]], axis=1
        )
        smoke_field = advance(
            smoke_field,
            ahead_x,
            behind_x,
            ahead_y,
            behind_y,
            shift_height(smoke_field, -1),
            shift_height(smoke_field, 1),
            velocity,
            solid_flag,
        )
        smoke_field = smoke_field + released
        populations = stepped[0]
        if not last:
            velocity = stepped[1]
            partials = stepped[2]
    return (populations, smoke_field)


def solution(mesh):
    placed = (
        P(None, "len", "band", None),
        P("len", "band", None),
        P("len", "band", None),
        P(),
        P(),
        P(),
        P(),
        P(),
    )
    return jax.shard_map(
        body,
        mesh=mesh,
        in_specs=placed,
        out_specs=(P(None, "len", "band", None), P("len", "band", None)),
        check_vma=False,
    )
```
